128 devices in a mesh: row: 8 (over x, z_lo), col: 16 (over y, z_hi, core).
Axes of the slice: x: 4, y: 4, z: 4 (z_hi: 2, z_lo: 2; z = z_hi * 2 + z_lo), core: 2. Of those that a mesh axis runs over, the one named last changes fastest.
Arguments:
- points: float32 [65536, 64], P(('row', 'col')), may hold values from -6 to 6
- feature_scales: float32 [64], replicated, may hold values from 0.06 to 0.25
- amplitude: float32 [1], replicated, may hold values from 1 to 3
- ridge: float32 [1], replicated, may hold values from 0.5 to 2
Outputs:
- factored: float32 [6, 16, 16, 8, 8192], P(None, 'col', None, 'row')
The draws below stay inside these ranges and needn't reach their ends.
All inputs are finite; a program needn't handle non-finite values.
Results may differ from the reference program's by a relative error of at most 0.0009.
The reference program's roundings to bfloat16 on the way (of `center_first`, `center_panels`, `first_panel` and `second_panel`) count: a program that leaves them out, or rounds other values in their place, can miss the bound.
Values may be sent and summed in bfloat16 or wider, within the bound.
No kernel may reach another device: no remote copies, remote signals or barrier semaphores. Data moves between devices by JAX's collectives and lax.ppermute only.
A program may use at most 128 MiB of HBM per device.

```python
import math
import jax
import jax.numpy as jnp
from jax import lax

FEAT = 64
SLAB = 1536
PANEL = 256
BLK = 16
NB = 64
NPTS = 65536
TB = 6
SB = 128
N_ROW = 8
N_COL = 16


def shard_levels(key, extent, pieces, smallest, high):
    gain = 1.0
    for axis_at, blocks in pieces:
        heights = jax.random.uniform(jax.random.fold_in(jax.random.fold_in(key, 6), axis_at), (blocks,), jnp.float32, smallest / len(pieces), high / len(pieces))
        gain = gain * jnp.repeat(jnp.exp(heights), extent[axis_at] // blocks).reshape((-1,) + (1,) * (len(extent) - 1 - axis_at))
    return gain


def noise(own_key, shape, deviation, limit, split=(), kind=jnp.bfloat16):
    entries = deviation * jax.random.normal(own_key, shape, jnp.float32)
    if split:
        entries = entries * shard_levels(own_key, shape, split, -0.22, 0.18)
    return jnp.clip(entries, -limit, limit).astype(kind)


def setup_inputs(seed: int = 0) -> dict:
    seeds = jax.random.split(jax.random.key(seed), 5)
    points = noise(seeds[0], (NPTS, FEAT), 1.0, 6.0, ((0, 128),), jnp.float32)
    feature_scales = jnp.clip(jnp.exp(jax.random.uniform(seeds[1], (FEAT,), jnp.float32, math.log(0.06), math.log(0.25))), 0.06, 0.25)
    amplitude = jnp.clip(jnp.exp(jax.random.uniform(seeds[2], (1,), jnp.float32, math.log(1.0), math.log(3.0))), 1.0, 3.0)
    ridge = jnp.clip(jnp.exp(jax.random.uniform(seeds[3], (1,), jnp.float32, math.log(0.5), math.log(2.0))), 0.5, 2.0)
    return dict(points=points, feature_scales=feature_scales, amplitude=amplitude, ridge=ridge)


def kernel_rows(left, right, scales, signal):
    left_scaled = left * scales
    right_scaled = right * scales
    left_norms = jnp.sum(left_scaled * left_scaled, axis=1)
    right_norms = jnp.sum(right_scaled * right_scaled, axis=1)
    cross = jnp.dot(left_scaled.astype(jnp.float32), right_scaled.T.astype(jnp.float32), precision=lax.Precision.HIGHEST, preferred_element_type=jnp.float32)
    return signal * jnp.exp(-0.5 * (left_norms[:, None] + right_norms[None, :] - 2.0 * cross))

def lower_inverse(block):
    factor = jnp.linalg.cholesky(block)
    identity = jnp.eye(block.shape[0], dtype=jnp.float32)
    return lax.linalg.triangular_solve(factor, identity, left_side=True, lower=True)

def factor_centers(centers, scales, signal, jitter):
    center_kernel = kernel_rows(centers, centers, scales, signal) + jitter * jnp.eye(centers.shape[0], dtype=jnp.float32)
    first_inverse = lower_inverse(center_kernel[:PANEL, :PANEL])
    center_first = jnp.dot(center_kernel[:, :PANEL].astype(jnp.float32), first_inverse.T.astype(jnp.float32), precision=lax.Precision.HIGHEST, preferred_element_type=jnp.float32).astype(jnp.bfloat16)
    center_second = center_kernel[:, PANEL:2 * PANEL] - jnp.dot(center_first.astype(jnp.float32), center_first[PANEL:2 * PANEL].T.astype(jnp.float32), preferred_element_type=jnp.float32)
    second_inverse = lower_inverse(center_second[PANEL:2 * PANEL])
    second_part = jnp.dot(center_second.astype(jnp.float32), second_inverse.T.astype(jnp.float32), precision=lax.Precision.HIGHEST, preferred_element_type=jnp.float32).astype(jnp.bfloat16)
    return (first_inverse, second_inverse, jnp.concatenate([center_first, second_part], axis=1))

def reference(points, feature_scales, amplitude, ridge):
    signal = amplitude[0]
    jitter = ridge[0]
    centers = points[:SLAB]
    first_inverse, second_inverse, center_panels = factor_centers(centers, feature_scales, signal, jitter)
    slab = kernel_rows(centers, points, feature_scales, signal)
    slab = slab.at[:, :SLAB].add(jitter * jnp.eye(SLAB, dtype=jnp.float32))
    first_panel = jnp.dot(first_inverse.astype(jnp.float32), slab[:PANEL].astype(jnp.float32), precision=lax.Precision.HIGHEST, preferred_element_type=jnp.float32).astype(jnp.bfloat16)
    reduced = slab[PANEL:2 * PANEL] - jnp.dot(center_panels[PANEL:2 * PANEL, :PANEL].astype(jnp.float32), first_panel.astype(jnp.float32), preferred_element_type=jnp.float32)
    second_panel = jnp.dot(second_inverse.astype(jnp.float32), reduced.astype(jnp.float32), precision=lax.Precision.HIGHEST, preferred_element_type=jnp.float32).astype(jnp.bfloat16)
    both_panels = jnp.concatenate([first_panel, second_panel], axis=0)
    trailing = slab[2 * PANEL:] - jnp.dot(center_panels[2 * PANEL:].astype(jnp.float32), both_panels.astype(jnp.float32), preferred_element_type=jnp.float32)
    factored = jnp.concatenate([both_panels.astype(jnp.float32), trailing], axis=0)
    factored = factored.reshape(TB, N_COL, BLK, SB, N_ROW, NB).transpose(0, 1, 2, 4, 3, 5)
    return factored.reshape(TB, N_COL, BLK, N_ROW, SB * NB)
```

```python
import jax
import jax.numpy as jnp
from jax import lax
from jax.sharding import PartitionSpec as P

FEAT = 64
SLAB = 1536
PANEL = 256
BLK = 16

HIGHEST = lax.Precision.HIGHEST


def kernel_block(left, left_norms, right, right_norms, signal):
    cross = jnp.dot(left, right.T, precision=HIGHEST, preferred_element_type=jnp.float32)
    return signal * jnp.exp(-0.5 * (left_norms[:, None] + right_norms[None, :] - 2.0 * cross))


def lower_inverse(block):
    factor = jnp.linalg.cholesky(block)
    identity = jnp.eye(block.shape[0], dtype=jnp.float32)
    return lax.linalg.triangular_solve(factor, identity, left_side=True, lower=True)


def ridge_where(row_ids, col_ids, jitter):
    return jnp.where(row_ids[:, None] == col_ids[None, :], jitter, jnp.float32(0.0))


def on_device(points, feature_scales, amplitude, ridge):
    row_count = lax.axis_size("row")
    col_count = lax.axis_size("col")
    row = lax.axis_index("row")
    column = lax.axis_index("col")
    rows_one = points.shape[0]
    block_rows = rows_one // row_count
    col_blocks = SLAB // (BLK * col_count)
    panel_blocks = PANEL // (BLK * col_count)
    center_sources = SLAB // rows_one
    signal = amplitude[0]
    jitter = ridge[0]

    blocks = points.reshape(row_count, block_rows, FEAT)
    moved = lax.all_to_all(blocks, "row", 0, 0, tiled=True)

    first_slot = lax.all_gather(moved[0], "col", axis=0, tiled=False)[:center_sources]
    center_grid = lax.all_gather(first_slot, "row", axis=0, tiled=False)
    centers = center_grid.transpose(1, 0, 2, 3).reshape(SLAB, FEAT)

    gathered = lax.all_gather(moved, "col", axis=0, tiled=False)
    row_points = gathered.transpose(1, 0, 2, 3).reshape(-1, FEAT)
    grid_rows = row_points.shape[0]

    center_scaled = centers * feature_scales
    center_norms = jnp.sum(center_scaled * center_scaled, axis=1)
    point_scaled = row_points * feature_scales
    point_norms = jnp.sum(point_scaled * point_scaled, axis=1)

    point_ids = (
        lax.broadcasted_iota(jnp.int32, (grid_rows // block_rows, block_rows), 0) * row_count
        + row
    ) * block_rows + lax.broadcasted_iota(jnp.int32, (grid_rows // block_rows, block_rows), 1)
    point_ids = point_ids.reshape(grid_rows)

    own_ids = (
        (
            lax.broadcasted_iota(jnp.int32, (col_blocks, BLK), 0) * col_count + column
        )
        * BLK
        + lax.broadcasted_iota(jnp.int32, (col_blocks, BLK), 1)
    )[2 * panel_blocks :].reshape(-1)
    own_scaled = jnp.take(center_scaled, own_ids, axis=0)
    own_norms = jnp.take(center_norms, own_ids, axis=0)

    lead_ids = jnp.arange(PANEL, dtype=jnp.int32)
    k11 = kernel_block(
        center_scaled[:PANEL], center_norms[:PANEL], center_scaled[:PANEL], center_norms[:PANEL], signal
    ) + ridge_where(lead_ids, lead_ids, jitter)
    first_inverse = lower_inverse(k11)
    used_ids = jnp.concatenate([jnp.arange(PANEL, 2 * PANEL, dtype=jnp.int32), own_ids])
    used_scaled = jnp.concatenate([center_scaled[PANEL : 2 * PANEL], own_scaled])
    used_norms = jnp.concatenate([center_norms[PANEL : 2 * PANEL], own_norms])
    used_kernel = kernel_block(
        used_scaled, used_norms, center_scaled[: 2 * PANEL], center_norms[: 2 * PANEL], signal
    ) + ridge_where(used_ids, jnp.arange(2 * PANEL, dtype=jnp.int32), jitter)
    center_first = jnp.dot(
        used_kernel[:, :PANEL], first_inverse.T, precision=HIGHEST, preferred_element_type=jnp.float32
    ).astype(jnp.bfloat16)
    first_mid = center_first[:PANEL]
    center_second = used_kernel[:, PANEL:] - jnp.dot(
        center_first, first_mid.T, preferred_element_type=jnp.float32
    )
    second_inverse = lower_inverse(center_second[:PANEL])
    second_own = jnp.dot(
        center_second[PANEL:], second_inverse.T, precision=HIGHEST, preferred_element_type=jnp.float32
    ).astype(jnp.bfloat16)
    own_panels = jnp.concatenate([center_first[PANEL:], second_own], axis=1)

    panel_kernel = kernel_block(
        center_scaled[: 2 * PANEL], center_norms[: 2 * PANEL], point_scaled, point_norms, signal
    ) + ridge_where(jnp.arange(2 * PANEL, dtype=jnp.int32), point_ids, jitter)
    first_panel = jnp.dot(
        first_inverse, panel_kernel[:PANEL], precision=HIGHEST, preferred_element_type=jnp.float32
    ).astype(jnp.bfloat16)
    reduced = panel_kernel[PANEL:] - jnp.dot(first_mid, first_panel, preferred_element_type=jnp.float32)
    second_panel = jnp.dot(
        second_inverse, reduced, precision=HIGHEST, preferred_element_type=jnp.float32
    ).astype(jnp.bfloat16)
    panels = jnp.concatenate([first_panel, second_panel], axis=0)

    own_kernel = kernel_block(own_scaled, own_norms, point_scaled, point_norms, signal) + ridge_where(
        own_ids, point_ids, jitter
    )
    trailing = own_kernel - jnp.dot(own_panels, panels, preferred_element_type=jnp.float32)

    own_first = lax.dynamic_slice_in_dim(first_panel, column * BLK, BLK, 0)
    own_second = lax.dynamic_slice_in_dim(second_panel, column * BLK, BLK, 0)
    finished = jnp.concatenate(
        [own_first.astype(jnp.float32), own_second.astype(jnp.float32), trailing], axis=0
    )
    return finished.reshape(col_blocks, 1, BLK, 1, grid_rows)


def solution(mesh):
    placed = (P(("row", "col"), None), P(), P(), P())
    return jax.shard_map(
        on_device,
        mesh=mesh,
        in_specs=placed,
        out_specs=P(None, "col", None, "row", None),
        check_vma=False,
    )
```

```python
import jax
import jax.numpy as jnp
from jax import lax
from jax.sharding import PartitionSpec as P

FEAT = 64
SLAB = 1536
PANEL = 256
BLK = 16

HIGHEST = lax.Precision.HIGHEST


def kernel_block(left, left_norms, right, right_norms, signal):
    cross = jnp.dot(left, right.T, precision=HIGHEST, preferred_element_type=jnp.float32)
    return signal * jnp.exp(-0.5 * (left_norms[:, None] + right_norms[None, :] - 2.0 * cross))


def lower_inverse(block):
    factor = jnp.linalg.cholesky(block)
    identity = jnp.eye(block.shape[0], dtype=jnp.float32)
    return lax.linalg.triangular_solve(factor, identity, left_side=True, lower=True)


def ridge_where(row_ids, col_ids, jitter):
    return jnp.where(row_ids[:, None] == col_ids[None, :], jitter, jnp.float32(0.0))


def on_device(points, feature_scales, amplitude, ridge):
    row_count = lax.axis_size("row")
    col_count = lax.axis_size("col")
    row = lax.axis_index("row")
    column = lax.axis_index("col")
    rows_one = points.shape[0]
    block_rows = rows_one // row_count
    col_blocks = SLAB // (BLK * col_count)
    panel_blocks = PANEL // (BLK * col_count)
    center_sources = SLAB // rows_one
    signal = amplitude[0]
    jitter = ridge[0]

    blocks = points.reshape(row_count, block_rows, FEAT)
    moved = lax.all_to_all(blocks, "row", 0, 0, tiled=True)

    first_slot = lax.all_gather(moved[0], "col", axis=0, tiled=False)[:center_sources]
    center_grid = lax.all_gather(first_slot, "row", axis=0, tiled=False)
    centers = center_grid.transpose(1, 0, 2, 3).reshape(SLAB, FEAT)

    moved, centers = lax.optimization_barrier((moved, centers))
    gathered = lax.all_gather(moved, "col", axis=0, tiled=False)
    row_points = gathered.transpose(1, 0, 2, 3).reshape(-1, FEAT)
    grid_rows = row_points.shape[0]

    center_scaled = centers * feature_scales
    center_norms = jnp.sum(center_scaled * center_scaled, axis=1)
    point_scaled = row_points * feature_scales
    point_norms = jnp.sum(point_scaled * point_scaled, axis=1)

    point_ids = (
        lax.broadcasted_iota(jnp.int32, (grid_rows // block_rows, block_rows), 0) * row_count
        + row
    ) * block_rows + lax.broadcasted_iota(jnp.int32, (grid_rows // block_rows, block_rows), 1)
    point_ids = point_ids.reshape(grid_rows)

    own_ids = (
        (
            lax.broadcasted_iota(jnp.int32, (col_blocks, BLK), 0) * col_count + column
        )
        * BLK
        + lax.broadcasted_iota(jnp.int32, (col_blocks, BLK), 1)
    )[2 * panel_blocks :].reshape(-1)
    own_scaled = jnp.take(center_scaled, own_ids, axis=0)
    own_norms = jnp.take(center_norms, own_ids, axis=0)

    lead_ids = jnp.arange(PANEL, dtype=jnp.int32)
    k11 = kernel_block(
        center_scaled[:PANEL], center_norms[:PANEL], center_scaled[:PANEL], center_norms[:PANEL], signal
    ) + ridge_where(lead_ids, lead_ids, jitter)
    first_inverse = lower_inverse(k11)
    used_ids = jnp.concatenate([jnp.arange(PANEL, 2 * PANEL, dtype=jnp.int32), own_ids])
    used_scaled = jnp.concatenate([center_scaled[PANEL : 2 * PANEL], own_scaled])
    used_norms = jnp.concatenate([center_norms[PANEL : 2 * PANEL], own_norms])
    used_kernel = kernel_block(
        used_scaled, used_norms, center_scaled[: 2 * PANEL], center_norms[: 2 * PANEL], signal
    ) + ridge_where(used_ids, jnp.arange(2 * PANEL, dtype=jnp.int32), jitter)
    center_first = jnp.dot(
        used_kernel[:, :PANEL], first_inverse.T, precision=HIGHEST, preferred_element_type=jnp.float32
    ).astype(jnp.bfloat16)
    first_mid = center_first[:PANEL]
    center_second = used_kernel[:, PANEL:] - jnp.dot(
        center_first, first_mid.T, preferred_element_type=jnp.float32
    )
    second_inverse = lower_inverse(center_second[:PANEL])
    second_own = jnp.dot(
        center_second[PANEL:], second_inverse.T, precision=HIGHEST, preferred_element_type=jnp.float32
    ).astype(jnp.bfloat16)
    own_panels = jnp.concatenate([center_first[PANEL:], second_own], axis=1)

    panel_kernel = kernel_block(
        center_scaled[: 2 * PANEL], center_norms[: 2 * PANEL], point_scaled, point_norms, signal
    ) + ridge_where(jnp.arange(2 * PANEL, dtype=jnp.int32), point_ids, jitter)
    first_panel = jnp.dot(
        first_inverse, panel_kernel[:PANEL], precision=HIGHEST, preferred_element_type=jnp.float32
    ).astype(jnp.bfloat16)
    reduced = panel_kernel[PANEL:] - jnp.dot(first_mid, first_panel, preferred_element_type=jnp.float32)
    second_panel = jnp.dot(
        second_inverse, reduced, precision=HIGHEST, preferred_element_type=jnp.float32
    ).astype(jnp.bfloat16)
    panels = jnp.concatenate([first_panel, second_panel], axis=0)

    own_kernel = kernel_block(own_scaled, own_norms, point_scaled, point_norms, signal) + ridge_where(
        own_ids, point_ids, jitter
    )
    trailing = own_kernel - jnp.dot(own_panels, panels, preferred_element_type=jnp.float32)

    own_first = lax.dynamic_slice_in_dim(first_panel, column * BLK, BLK, 0)
    own_second = lax.dynamic_slice_in_dim(second_panel, column * BLK, BLK, 0)
    finished = jnp.concatenate(
        [own_first.astype(jnp.float32), own_second.astype(jnp.float32), trailing], axis=0
    )
    return finished.reshape(col_blocks, 1, BLK, 1, grid_rows)


def solution(mesh):
    placed = (P(("row", "col"), None), P(), P(), P())
    return jax.shard_map(
        on_device,
        mesh=mesh,
        in_specs=placed,
        out_specs=P(None, "col", None, "row", None),
        check_vma=False,
    )
```

```python
import jax
import jax.numpy as jnp
from jax import lax
from jax.sharding import PartitionSpec as P

FEAT = 64
SLAB = 1536
PANEL = 256
BLK = 16

HIGHEST = lax.Precision.HIGHEST


def kernel_block(left, left_norms, right, right_norms, signal):
    cross = jnp.dot(left, right.T, precision=HIGHEST, preferred_element_type=jnp.float32)
    return signal * jnp.exp(-0.5 * (left_norms[:, None] + right_norms[None, :] - 2.0 * cross))


def lower_inverse(block):
    factor = jnp.linalg.cholesky(block)
    identity = jnp.eye(block.shape[0], dtype=jnp.float32)
    return lax.linalg.triangular_solve(factor, identity, left_side=True, lower=True)


def ridge_where(row_ids, col_ids, jitter):
    return jnp.where(row_ids[:, None] == col_ids[None, :], jitter, jnp.float32(0.0))


def gather_by_all_to_all(piece, axis_name):
    count = lax.axis_size(axis_name)
    copies = jnp.broadcast_to(piece[None], (count,) + piece.shape)
    return lax.all_to_all(copies, axis_name, 0, 0, tiled=True)


def on_device(points, feature_scales, amplitude, ridge):
    row_count = lax.axis_size("row")
    col_count = lax.axis_size("col")
    row = lax.axis_index("row")
    column = lax.axis_index("col")
    rows_one = points.shape[0]
    block_rows = rows_one // row_count
    col_blocks = SLAB // (BLK * col_count)
    panel_blocks = PANEL // (BLK * col_count)
    center_sources = SLAB // rows_one
    signal = amplitude[0]
    jitter = ridge[0]

    blocks = points.reshape(row_count, block_rows, FEAT)
    moved = lax.all_to_all(blocks, "row", 0, 0, tiled=True)

    first_slot = gather_by_all_to_all(moved[0], "col")[:center_sources]
    center_grid = gather_by_all_to_all(first_slot, "row")
    centers = center_grid.transpose(1, 0, 2, 3).reshape(SLAB, FEAT)

    moved, centers = lax.optimization_barrier((moved, centers))
    gathered = lax.all_gather(moved, "col", axis=0, tiled=False)
    row_points = gathered.transpose(1, 0, 2, 3).reshape(-1, FEAT)
    grid_rows = row_points.shape[0]

    center_scaled = centers * feature_scales
    center_norms = jnp.sum(center_scaled * center_scaled, axis=1)
    point_scaled = row_points * feature_scales
    point_norms = jnp.sum(point_scaled * point_scaled, axis=1)

    point_ids = (
        lax.broadcasted_iota(jnp.int32, (grid_rows // block_rows, block_rows), 0) * row_count
        + row
    ) * block_rows + lax.broadcasted_iota(jnp.int32, (grid_rows // block_rows, block_rows), 1)
    point_ids = point_ids.reshape(grid_rows)

    own_ids = (
        (
            lax.broadcasted_iota(jnp.int32, (col_blocks, BLK), 0) * col_count + column
        )
        * BLK
        + lax.broadcasted_iota(jnp.int32, (col_blocks, BLK), 1)
    )[2 * panel_blocks :].reshape(-1)
    own_scaled = jnp.take(center_scaled, own_ids, axis=0)
    own_norms = jnp.take(center_norms, own_ids, axis=0)

    lead_ids = jnp.arange(PANEL, dtype=jnp.int32)
    k11 = kernel_block(
        center_scaled[:PANEL], center_norms[:PANEL], center_scaled[:PANEL], center_norms[:PANEL], signal
    ) + ridge_where(lead_ids, lead_ids, jitter)
    first_inverse = lower_inverse(k11)
    used_ids = jnp.concatenate([jnp.arange(PANEL, 2 * PANEL, dtype=jnp.int32), own_ids])
    used_scaled = jnp.concatenate([center_scaled[PANEL : 2 * PANEL], own_scaled])
    used_norms = jnp.concatenate([center_norms[PANEL : 2 * PANEL], own_norms])
    used_kernel = kernel_block(
        used_scaled, used_norms, center_scaled[: 2 * PANEL], center_norms[: 2 * PANEL], signal
    ) + ridge_where(used_ids, jnp.arange(2 * PANEL, dtype=jnp.int32), jitter)
    center_first = jnp.dot(
        used_kernel[:, :PANEL], first_inverse.T, precision=HIGHEST, preferred_element_type=jnp.float32
    ).astype(jnp.bfloat16)
    first_mid = center_first[:PANEL]
    center_second = used_kernel[:, PANEL:] - jnp.dot(
        center_first, first_mid.T, preferred_element_type=jnp.float32
    )
    second_inverse = lower_inverse(center_second[:PANEL])
    second_own = jnp.dot(
        center_second[PANEL:], second_inverse.T, precision=HIGHEST, preferred_element_type=jnp.float32
    ).astype(jnp.bfloat16)
    own_panels = jnp.concatenate([center_first[PANEL:], second_own], axis=1)

    panel_kernel = kernel_block(
        center_scaled[: 2 * PANEL], center_norms[: 2 * PANEL], point_scaled, point_norms, signal
    ) + ridge_where(jnp.arange(2 * PANEL, dtype=jnp.int32), point_ids, jitter)
    first_panel = jnp.dot(
        first_inverse, panel_kernel[:PANEL], precision=HIGHEST, preferred_element_type=jnp.float32
    ).astype(jnp.bfloat16)
    reduced = panel_kernel[PANEL:] - jnp.dot(first_mid, first_panel, preferred_element_type=jnp.float32)
    second_panel = jnp.dot(
        second_inverse, reduced, precision=HIGHEST, preferred_element_type=jnp.float32
    ).astype(jnp.bfloat16)
    panels = jnp.concatenate([first_panel, second_panel], axis=0)

    own_kernel = kernel_block(own_scaled, own_norms, point_scaled, point_norms, signal) + ridge_where(
        own_ids, point_ids, jitter
    )
    trailing = own_kernel - jnp.dot(own_panels, panels, preferred_element_type=jnp.float32)

    own_first = lax.dynamic_slice_in_dim(first_panel, column * BLK, BLK, 0)
    own_second = lax.dynamic_slice_in_dim(second_panel, column * BLK, BLK, 0)
    finished = jnp.concatenate(
        [own_first.astype(jnp.float32), own_second.astype(jnp.float32), trailing], axis=0
    )
    return finished.reshape(col_blocks, 1, BLK, 1, grid_rows)


def solution(mesh):
    placed = (P(("row", "col"), None), P(), P(), P())
    return jax.shard_map(
        on_device,
        mesh=mesh,
        in_specs=placed,
        out_specs=P(None, "col", None, "row", None),
        check_vma=False,
    )
```

```python
import jax
import jax.numpy as jnp
from jax import lax
from jax.sharding import PartitionSpec as P
from jax.experimental import pallas as pl
from jax.experimental.pallas import tpu as pltpu

FEAT = 64
SLAB = 1536
PANEL = 256
BLK = 16

HIGHEST = lax.Precision.HIGHEST


def kernel_block(left, left_norms, right, right_norms, signal):
    cross = jnp.dot(left, right.T, precision=HIGHEST, preferred_element_type=jnp.float32)
    return signal * jnp.exp(-0.5 * (left_norms[:, None] + right_norms[None, :] - 2.0 * cross))


def _nt(left, right):
    return lax.dot_general(
        left, right, (((1,), (1,)), ((), ())), precision=HIGHEST, preferred_element_type=jnp.float32
    )


def lower_inverse_kernel(a_ref, o_ref, s_ref, x_ref):
    half = a_ref.shape[0] // 2
    lanes = lax.broadcasted_iota(jnp.int32, (half, half), 1)
    rows = lax.broadcasted_iota(jnp.int32, (half, 1), 0)
    lane_row = lax.broadcasted_iota(jnp.int32, (1, half), 1)
    eye = jnp.where(lax.broadcasted_iota(jnp.int32, (half, half), 0) == lanes, 1.0, 0.0)

    def step(k, carry):
        s = s_ref[...]
        x = x_ref[...]
        row = s_ref[pl.ds(k, 1), :]
        col = jnp.sum(jnp.where(lanes == k, s, 0.0), axis=1, keepdims=True)
        root = jnp.sqrt(jnp.sum(jnp.where(lane_row == k, row, 0.0), axis=1, keepdims=True))
        col = jnp.where(rows >= k, col / root, 0.0)
        row = jnp.where(lane_row >= k, row / root, 0.0)
        s_ref[...] = s - col * row
        xk = x_ref[pl.ds(k, 1), :] / root
        x_ref[...] = jnp.where(rows == k, xk, x - jnp.where(rows > k, col, 0.0) * xk)
        return carry

    def base(block):
        s_ref[...] = block
        x_ref[...] = eye.astype(jnp.float32)
        lax.fori_loop(0, half, step, 0)
        return x_ref[...]

    first = base(a_ref[:half, :half])
    lower = _nt(a_ref[half:, :half], first)
    schur = a_ref[half:, half:] - _nt(lower, lower)
    second = base((schur + schur.T) * 0.5)
    below = -jnp.dot(
        second,
        jnp.dot(lower, first, precision=HIGHEST, preferred_element_type=jnp.float32),
        precision=HIGHEST,
        preferred_element_type=jnp.float32,
    )
    o_ref[:half, :half] = first
    o_ref[:half, half:] = jnp.zeros((half, half), jnp.float32)
    o_ref[half:, :half] = below
    o_ref[half:, half:] = second


def lower_inverse(block):
    size = block.shape[0]
    half = size // 2
    block = (block + block.T) * 0.5
    return pl.pallas_call(
        lower_inverse_kernel,
        out_shape=jax.ShapeDtypeStruct((size, size), jnp.float32),
        scratch_shapes=[pltpu.VMEM((half, half), jnp.float32), pltpu.VMEM((half, half), jnp.float32)],
    )(block)


def panel_kernel(
    consts_ref, pts_ref, pnorm_ref, pid_ref, scales_ref, cs_ref, cn_ref, own_cs_ref, own_cn_ref,
    own_ids_ref, finv_ref, sinv_ref, mid_ref, own_panels_ref, sel_ref, out_ref,
):
    signal = consts_ref[0]
    jitter = consts_ref[1]
    tile = pts_ref.shape[0] * pts_ref.shape[2]
    scaled = pts_ref[...].reshape(tile, FEAT) * scales_ref[...]
    pnorm = pnorm_ref[...]
    pid = pid_ref[...]
    cross = _nt(cs_ref[...], scaled)
    values = signal * jnp.exp(-0.5 * (cn_ref[...] + pnorm - 2.0 * cross))
    lead = lax.broadcasted_iota(jnp.int32, values.shape, 0)
    values = values + jnp.where(lead == pid, jitter, jnp.float32(0.0))
    first = jnp.dot(
        finv_ref[...], values[:PANEL], precision=HIGHEST, preferred_element_type=jnp.float32
    ).astype(jnp.bfloat16)
    reduced = values[PANEL:] - jnp.dot(mid_ref[...], first, preferred_element_type=jnp.float32)
    second = jnp.dot(
        sinv_ref[...], reduced, precision=HIGHEST, preferred_element_type=jnp.float32
    ).astype(jnp.bfloat16)
    own_cross = _nt(own_cs_ref[...], scaled)
    own = signal * jnp.exp(-0.5 * (own_cn_ref[...] + pnorm - 2.0 * own_cross))
    own = own + jnp.where(own_ids_ref[...] == pid, jitter, jnp.float32(0.0))
    both = jnp.concatenate([first, second], axis=0)
    trailing = own - jnp.dot(own_panels_ref[...], both, preferred_element_type=jnp.float32)
    sel = sel_ref[...]
    out_ref[:BLK] = jnp.dot(sel, first, preferred_element_type=jnp.float32)
    out_ref[BLK : 2 * BLK] = jnp.dot(sel, second, preferred_element_type=jnp.float32)
    out_ref[2 * BLK :] = trailing


def panel_stage(consts, gathered, pnorm, pid, scales, cs, cn, own_cs, own_cn, own_ids, finv, sinv, mid, own_panels, sel):
    col_count, row_count, block_rows, _ = gathered.shape
    tile = col_count * block_rows
    grid_rows = tile * row_count
    out_rows = 2 * BLK + own_cs.shape[0]

    def whole(array):
        return pl.BlockSpec(array.shape, lambda i: (0,) * array.ndim)

    return pl.pallas_call(
        panel_kernel,
        grid=(row_count,),
        in_specs=[
            pl.BlockSpec(memory_space=pltpu.SMEM),
            pl.BlockSpec((col_count, 1, block_rows, FEAT), lambda i: (0, i, 0, 0)),
            pl.BlockSpec((1, tile), lambda i: (0, i)),
            pl.BlockSpec((1, tile), lambda i: (0, i)),
        ]
        + [whole(a) for a in (scales, cs, cn, own_cs, own_cn, own_ids, finv, sinv, mid, own_panels, sel)],
        out_specs=pl.BlockSpec((out_rows, tile), lambda i: (0, i)),
        out_shape=jax.ShapeDtypeStruct((out_rows, grid_rows), jnp.float32),
    )(consts, gathered, pnorm, pid, scales, cs, cn, own_cs, own_cn, own_ids, finv, sinv, mid, own_panels, sel)


def ridge_where(row_ids, col_ids, jitter):
    return jnp.where(row_ids[:, None] == col_ids[None, :], jitter, jnp.float32(0.0))


def gather_by_all_to_all(piece, axis_name):
    count = lax.axis_size(axis_name)
    copies = jnp.broadcast_to(piece[None], (count,) + piece.shape)
    return lax.all_to_all(copies, axis_name, 0, 0, tiled=True)


def on_device(points, feature_scales, amplitude, ridge):
    row_count = lax.axis_size("row")
    col_count = lax.axis_size("col")
    row = lax.axis_index("row")
    column = lax.axis_index("col")
    rows_one = points.shape[0]
    block_rows = rows_one // row_count
    col_blocks = SLAB // (BLK * col_count)
    panel_blocks = PANEL // (BLK * col_count)
    center_sources = SLAB // rows_one
    signal = amplitude[0]
    jitter = ridge[0]

    blocks = points.reshape(row_count, block_rows, FEAT)
    moved = lax.all_to_all(blocks, "row", 0, 0, tiled=True)

    first_slot = gather_by_all_to_all(moved[0], "col")[:center_sources]
    center_grid = gather_by_all_to_all(first_slot, "row")
    centers = center_grid.transpose(1, 0, 2, 3).reshape(SLAB, FEAT)

    moved, centers = lax.optimization_barrier((moved, centers))
    gathered = lax.all_gather(moved, "col", axis=0, tiled=False)
    grid_rows = gathered.shape[0] * gathered.shape[1] * block_rows

    center_scaled = centers * feature_scales
    center_norms = jnp.sum(center_scaled * center_scaled, axis=1)
    gathered_scaled = gathered * feature_scales
    point_norms = jnp.sum(gathered_scaled * gathered_scaled, axis=3).transpose(1, 0, 2).reshape(1, grid_rows)

    point_ids = (
        lax.broadcasted_iota(jnp.int32, (grid_rows // block_rows, block_rows), 0) * row_count
        + row
    ) * block_rows + lax.broadcasted_iota(jnp.int32, (grid_rows // block_rows, block_rows), 1)
    point_ids = point_ids.reshape(1, grid_rows)

    own_ids = (
        (
            lax.broadcasted_iota(jnp.int32, (col_blocks, BLK), 0) * col_count + column
        )
        * BLK
        + lax.broadcasted_iota(jnp.int32, (col_blocks, BLK), 1)
    )[2 * panel_blocks :].reshape(-1)
    own_scaled = jnp.take(center_scaled, own_ids, axis=0)
    own_norms = jnp.take(center_norms, own_ids, axis=0)

    lead_ids = jnp.arange(PANEL, dtype=jnp.int32)
    k11 = kernel_block(
        center_scaled[:PANEL], center_norms[:PANEL], center_scaled[:PANEL], center_norms[:PANEL], signal
    ) + ridge_where(lead_ids, lead_ids, jitter)
    first_inverse = lower_inverse(k11)
    used_ids = jnp.concatenate([jnp.arange(PANEL, 2 * PANEL, dtype=jnp.int32), own_ids])
    used_scaled = jnp.concatenate([center_scaled[PANEL : 2 * PANEL], own_scaled])
    used_norms = jnp.concatenate([center_norms[PANEL : 2 * PANEL], own_norms])
    used_kernel = kernel_block(
        used_scaled, used_norms, center_scaled[: 2 * PANEL], center_norms[: 2 * PANEL], signal
    ) + ridge_where(used_ids, jnp.arange(2 * PANEL, dtype=jnp.int32), jitter)
    center_first = jnp.dot(
        used_kernel[:, :PANEL], first_inverse.T, precision=HIGHEST, preferred_element_type=jnp.float32
    ).astype(jnp.bfloat16)
    first_mid = center_first[:PANEL]
    center_second = used_kernel[:, PANEL:] - jnp.dot(
        center_first, first_mid.T, preferred_element_type=jnp.float32
    )
    second_inverse = lower_inverse(center_second[:PANEL])
    second_own = jnp.dot(
        center_second[PANEL:], second_inverse.T, precision=HIGHEST, preferred_element_type=jnp.float32
    ).astype(jnp.bfloat16)
    own_panels = jnp.concatenate([center_first[PANEL:], second_own], axis=1)

    select = jnp.where(
        lax.broadcasted_iota(jnp.int32, (BLK, PANEL), 1)
        == column * BLK + lax.broadcasted_iota(jnp.int32, (BLK, PANEL), 0),
        1.0,
        0.0,
    ).astype(jnp.bfloat16)
    consts = jnp.stack([signal, jitter])
    finished = panel_stage(
        consts,
        gathered,
        point_norms,
        point_ids,
        feature_scales.reshape(1, FEAT),
        center_scaled[: 2 * PANEL],
        center_norms[: 2 * PANEL].reshape(-1, 1),
        own_scaled,
        own_norms.reshape(-1, 1),
        own_ids.reshape(-1, 1),
        first_inverse,
        second_inverse,
        first_mid,
        own_panels,
        select,
    )
    return finished.reshape(col_blocks, 1, BLK, 1, grid_rows)


def solution(mesh):
    placed = (P(("row", "col"), None), P(), P(), P())
    return jax.shard_map(
        on_device,
        mesh=mesh,
        in_specs=placed,
        out_specs=P(None, "col", None, "row", None),
        check_vma=False,
    )
```

```python
import jax
import jax.numpy as jnp
from jax import lax
from jax.sharding import PartitionSpec as P
from jax.experimental import pallas as pl
from jax.experimental.pallas import tpu as pltpu

FEAT = 64
SLAB = 1536
PANEL = 256
BLK = 16

HIGHEST = lax.Precision.HIGHEST


def kernel_block(left, left_norms, right, right_norms, signal):
    cross = jnp.dot(left, right.T, precision=HIGHEST, preferred_element_type=jnp.float32)
    return signal * jnp.exp(-0.5 * (left_norms[:, None] + right_norms[None, :] - 2.0 * cross))


def _nt(left, right):
    return lax.dot_general(
        left, right, (((1,), (1,)), ((), ())), precision=HIGHEST, preferred_element_type=jnp.float32
    )


def lower_inverse_kernel(a_ref, o_ref, s_ref, x_ref):
    half = a_ref.shape[0] // 2
    lanes = lax.broadcasted_iota(jnp.int32, (half, half), 1)
    rows = lax.broadcasted_iota(jnp.int32, (half, 1), 0)
    lane_row = lax.broadcasted_iota(jnp.int32, (1, half), 1)
    eye = jnp.where(lax.broadcasted_iota(jnp.int32, (half, half), 0) == lanes, 1.0, 0.0)

    def step(k, carry):
        s = s_ref[...]
        x = x_ref[...]
        row = s_ref[pl.ds(k, 1), :]
        col = jnp.sum(jnp.where(lanes == k, s, 0.0), axis=1, keepdims=True)
        root = jnp.sqrt(jnp.sum(jnp.where(lane_row == k, row, 0.0), axis=1, keepdims=True))
        col = jnp.where(rows >= k, col / root, 0.0)
        row = jnp.where(lane_row >= k, row / root, 0.0)
        s_ref[...] = s - col * row
        xk = x_ref[pl.ds(k, 1), :] / root
        x_ref[...] = jnp.where(rows == k, xk, x - jnp.where(rows > k, col, 0.0) * xk)
        return carry

    def base(block):
        s_ref[...] = block
        x_ref[...] = eye.astype(jnp.float32)
        lax.fori_loop(0, half, step, 0, unroll=2)
        return x_ref[...]

    first = base(a_ref[:half, :half])
    lower = _nt(a_ref[half:, :half], first)
    schur = a_ref[half:, half:] - _nt(lower, lower)
    second = base((schur + schur.T) * 0.5)
    below = -jnp.dot(
        second,
        jnp.dot(lower, first, precision=HIGHEST, preferred_element_type=jnp.float32),
        precision=HIGHEST,
        preferred_element_type=jnp.float32,
    )
    o_ref[:half, :half] = first
    o_ref[:half, half:] = jnp.zeros((half, half), jnp.float32)
    o_ref[half:, :half] = below
    o_ref[half:, half:] = second


def lower_inverse(block):
    size = block.shape[0]
    half = size // 2
    block = (block + block.T) * 0.5
    return pl.pallas_call(
        lower_inverse_kernel,
        out_shape=jax.ShapeDtypeStruct((size, size), jnp.float32),
        scratch_shapes=[pltpu.VMEM((half, half), jnp.float32), pltpu.VMEM((half, half), jnp.float32)],
    )(block)


def lower_times(lower_ref, right):
    half = lower_ref.shape[0] // 2
    top = jnp.dot(
        lower_ref[:half, :half], right[:half], precision=HIGHEST, preferred_element_type=jnp.float32
    )
    bottom = jnp.dot(
        lower_ref[half:, :half], right[:half], precision=HIGHEST, preferred_element_type=jnp.float32
    ) + jnp.dot(
        lower_ref[half:, half:], right[half:], precision=HIGHEST, preferred_element_type=jnp.float32
    )
    return jnp.concatenate([top, bottom], axis=0)


def panel_kernel(
    consts_ref, pts_ref, pnorm_ref, pid_ref, scales_ref, cs_ref, cn_ref, own_cs_ref, own_cn_ref,
    own_ids_ref, finv_ref, sinv_ref, mid_ref, own_panels_ref, sel_ref, out_ref,
):
    signal = consts_ref[0]
    jitter = consts_ref[1]
    tile = pts_ref.shape[0] * pts_ref.shape[2]
    scaled = pts_ref[...].reshape(tile, FEAT) * scales_ref[...]
    pnorm = pnorm_ref[...]
    pid = pid_ref[...]
    cross = _nt(cs_ref[...], scaled)
    values = signal * jnp.exp(-0.5 * (cn_ref[...] + pnorm - 2.0 * cross))
    lead = lax.broadcasted_iota(jnp.int32, values.shape, 0)
    values = values + jnp.where(lead == pid, jitter, jnp.float32(0.0))
    first = lower_times(finv_ref, values[:PANEL]).astype(jnp.bfloat16)
    reduced = values[PANEL:] - jnp.dot(mid_ref[...], first, preferred_element_type=jnp.float32)
    second = lower_times(sinv_ref, reduced).astype(jnp.bfloat16)
    own_cross = _nt(own_cs_ref[...], scaled)
    own = signal * jnp.exp(-0.5 * (own_cn_ref[...] + pnorm - 2.0 * own_cross))
    own = own + jnp.where(own_ids_ref[...] == pid, jitter, jnp.float32(0.0))
    both = jnp.concatenate([first, second], axis=0)
    trailing = own - jnp.dot(own_panels_ref[...], both, preferred_element_type=jnp.float32)
    sel = sel_ref[...]
    out_ref[:BLK] = jnp.dot(sel, first, preferred_element_type=jnp.float32)
    out_ref[BLK : 2 * BLK] = jnp.dot(sel, second, preferred_element_type=jnp.float32)
    out_ref[2 * BLK :] = trailing


def panel_stage(consts, gathered, pnorm, pid, scales, cs, cn, own_cs, own_cn, own_ids, finv, sinv, mid, own_panels, sel):
    col_count, row_count, block_rows, _ = gathered.shape
    tile = col_count * block_rows
    grid_rows = tile * row_count
    out_rows = 2 * BLK + own_cs.shape[0]

    def whole(array):
        return pl.BlockSpec(array.shape, lambda i: (0,) * array.ndim)

    return pl.pallas_call(
        panel_kernel,
        grid=(row_count,),
        in_specs=[
            pl.BlockSpec(memory_space=pltpu.SMEM),
            pl.BlockSpec((col_count, 1, block_rows, FEAT), lambda i: (0, i, 0, 0)),
            pl.BlockSpec((1, tile), lambda i: (0, i)),
            pl.BlockSpec((1, tile), lambda i: (0, i)),
        ]
        + [whole(a) for a in (scales, cs, cn, own_cs, own_cn, own_ids, finv, sinv, mid, own_panels, sel)],
        out_specs=pl.BlockSpec((out_rows, tile), lambda i: (0, i)),
        out_shape=jax.ShapeDtypeStruct((out_rows, grid_rows), jnp.float32),
    )(consts, gathered, pnorm, pid, scales, cs, cn, own_cs, own_cn, own_ids, finv, sinv, mid, own_panels, sel)


def ridge_where(row_ids, col_ids, jitter):
    return jnp.where(row_ids[:, None] == col_ids[None, :], jitter, jnp.float32(0.0))


def gather_by_all_to_all(piece, axis_name):
    count = lax.axis_size(axis_name)
    copies = jnp.broadcast_to(piece[None], (count,) + piece.shape)
    return lax.all_to_all(copies, axis_name, 0, 0, tiled=True)


def on_device(points, feature_scales, amplitude, ridge):
    row_count = lax.axis_size("row")
    col_count = lax.axis_size("col")
    row = lax.axis_index("row")
    column = lax.axis_index("col")
    rows_one = points.shape[0]
    block_rows = rows_one // row_count
    col_blocks = SLAB // (BLK * col_count)
    panel_blocks = PANEL // (BLK * col_count)
    center_sources = SLAB // rows_one
    signal = amplitude[0]
    jitter = ridge[0]

    blocks = points.reshape(row_count, block_rows, FEAT)
    moved = lax.all_to_all(blocks, "row", 0, 0, tiled=True)

    first_slot = gather_by_all_to_all(moved[0], "col")[:center_sources]
    center_grid = gather_by_all_to_all(first_slot, "row")
    centers = center_grid.transpose(1, 0, 2, 3).reshape(SLAB, FEAT)

    moved, centers = lax.optimization_barrier((moved, centers))
    gathered = lax.all_gather(moved, "col", axis=0, tiled=False)
    grid_rows = gathered.shape[0] * gathered.shape[1] * block_rows

    center_scaled = centers * feature_scales
    center_norms = jnp.sum(center_scaled * center_scaled, axis=1)
    gathered_scaled = gathered * feature_scales
    point_norms = jnp.sum(gathered_scaled * gathered_scaled, axis=3).transpose(1, 0, 2).reshape(1, grid_rows)

    point_ids = (
        lax.broadcasted_iota(jnp.int32, (grid_rows // block_rows, block_rows), 0) * row_count
        + row
    ) * block_rows + lax.broadcasted_iota(jnp.int32, (grid_rows // block_rows, block_rows), 1)
    point_ids = point_ids.reshape(1, grid_rows)

    own_ids = (
        (
            lax.broadcasted_iota(jnp.int32, (col_blocks, BLK), 0) * col_count + column
        )
        * BLK
        + lax.broadcasted_iota(jnp.int32, (col_blocks, BLK), 1)
    )[2 * panel_blocks :].reshape(-1)
    own_scaled = jnp.take(center_scaled, own_ids, axis=0)
    own_norms = jnp.take(center_norms, own_ids, axis=0)

    lead_ids = jnp.arange(PANEL, dtype=jnp.int32)
    k11 = kernel_block(
        center_scaled[:PANEL], center_norms[:PANEL], center_scaled[:PANEL], center_norms[:PANEL], signal
    ) + ridge_where(lead_ids, lead_ids, jitter)
    first_inverse = lower_inverse(k11)
    used_ids = jnp.concatenate([jnp.arange(PANEL, 2 * PANEL, dtype=jnp.int32), own_ids])
    used_scaled = jnp.concatenate([center_scaled[PANEL : 2 * PANEL], own_scaled])
    used_norms = jnp.concatenate([center_norms[PANEL : 2 * PANEL], own_norms])
    used_kernel = kernel_block(
        used_scaled, used_norms, center_scaled[: 2 * PANEL], center_norms[: 2 * PANEL], signal
    ) + ridge_where(used_ids, jnp.arange(2 * PANEL, dtype=jnp.int32), jitter)
    center_first = jnp.dot(
        used_kernel[:, :PANEL], first_inverse.T, precision=HIGHEST, preferred_element_type=jnp.float32
    ).astype(jnp.bfloat16)
    first_mid = center_first[:PANEL]
    center_second = used_kernel[:, PANEL:] - jnp.dot(
        center_first, first_mid.T, preferred_element_type=jnp.float32
    )
    second_inverse = lower_inverse(center_second[:PANEL])
    second_own = jnp.dot(
        center_second[PANEL:], second_inverse.T, precision=HIGHEST, preferred_element_type=jnp.float32
    ).astype(jnp.bfloat16)
    own_panels = jnp.concatenate([center_first[PANEL:], second_own], axis=1)

    select = jnp.where(
        lax.broadcasted_iota(jnp.int32, (BLK, PANEL), 1)
        == column * BLK + lax.broadcasted_iota(jnp.int32, (BLK, PANEL), 0),
        1.0,
        0.0,
    ).astype(jnp.bfloat16)
    consts = jnp.stack([signal, jitter])
    finished = panel_stage(
        consts,
        gathered,
        point_norms,
        point_ids,
        feature_scales.reshape(1, FEAT),
        center_scaled[: 2 * PANEL],
        center_norms[: 2 * PANEL].reshape(-1, 1),
        own_scaled,
        own_norms.reshape(-1, 1),
        own_ids.reshape(-1, 1),
        first_inverse,
        second_inverse,
        first_mid,
        own_panels,
        select,
    )
    return finished.reshape(col_blocks, 1, BLK, 1, grid_rows)


def solution(mesh):
    placed = (P(("row", "col"), None), P(), P(), P())
    return jax.shard_map(
        on_device,
        mesh=mesh,
        in_specs=placed,
        out_specs=P(None, "col", None, "row", None),
        check_vma=False,
    )
```

```python
import jax
import jax.numpy as jnp
from jax import lax
from jax.sharding import PartitionSpec as P
from jax.experimental import pallas as pl
from jax.experimental.pallas import tpu as pltpu

FEAT = 64
SLAB = 1536
PANEL = 256
BLK = 16

HIGHEST = lax.Precision.HIGHEST


def kernel_block(left, left_norms, right, right_norms, signal):
    cross = jnp.dot(left, right.T, precision=HIGHEST, preferred_element_type=jnp.float32)
    return signal * jnp.exp(-0.5 * (left_norms[:, None] + right_norms[None, :] - 2.0 * cross))


def _nt(left, right):
    return lax.dot_general(
        left, right, (((1,), (1,)), ((), ())), precision=HIGHEST, preferred_element_type=jnp.float32
    )


def lower_inverse_kernel(a_ref, o_ref, s_ref, x_ref):
    half = a_ref.shape[0] // 2
    lanes = lax.broadcasted_iota(jnp.int32, (half, half), 1)
    rows = lax.broadcasted_iota(jnp.int32, (half, 1), 0)
    lane_row = lax.broadcasted_iota(jnp.int32, (1, half), 1)
    eye = jnp.where(lax.broadcasted_iota(jnp.int32, (half, half), 0) == lanes, 1.0, 0.0)

    def step(k, carry):
        s = s_ref[...]
        x = x_ref[...]
        row = s_ref[pl.ds(k, 1), :]
        col = jnp.sum(jnp.where(lanes == k, s, 0.0), axis=1, keepdims=True)
        root = jnp.sqrt(jnp.sum(jnp.where(lane_row == k, row, 0.0), axis=1, keepdims=True))
        col = jnp.where(rows >= k, col / root, 0.0)
        row = jnp.where(lane_row >= k, row / root, 0.0)
        s_ref[...] = s - col * row
        xk = x_ref[pl.ds(k, 1), :] / root
        x_ref[...] = jnp.where(rows == k, xk, x - jnp.where(rows > k, col, 0.0) * xk)
        return carry

    def base(block):
        s_ref[...] = block
        x_ref[...] = eye.astype(jnp.float32)
        lax.fori_loop(0, half, step, 0)
        return x_ref[...]

    first = base(a_ref[:half, :half])
    lower = _nt(a_ref[half:, :half], first)
    schur = a_ref[half:, half:] - _nt(lower, lower)
    second = base((schur + schur.T) * 0.5)
    below = -jnp.dot(
        second,
        jnp.dot(lower, first, precision=HIGHEST, preferred_element_type=jnp.float32),
        precision=HIGHEST,
        preferred_element_type=jnp.float32,
    )
    o_ref[:half, :half] = first
    o_ref[:half, half:] = jnp.zeros((half, half), jnp.float32)
    o_ref[half:, :half] = below
    o_ref[half:, half:] = second


def lower_inverse(block):
    size = block.shape[0]
    half = size // 2
    block = (block + block.T) * 0.5
    return pl.pallas_call(
        lower_inverse_kernel,
        out_shape=jax.ShapeDtypeStruct((size, size), jnp.float32),
        scratch_shapes=[pltpu.VMEM((half, half), jnp.float32), pltpu.VMEM((half, half), jnp.float32)],
    )(block)


def split_three(values):
    high = values.astype(jnp.bfloat16)
    rest = values - high.astype(jnp.float32)
    middle = rest.astype(jnp.bfloat16)
    low = (rest - middle.astype(jnp.float32)).astype(jnp.bfloat16)
    return high, middle, low


def pack_left(values):
    high = lax.reduce_precision(values, exponent_bits=8, mantissa_bits=7)
    rest = values - high
    middle = lax.reduce_precision(rest, exponent_bits=8, mantissa_bits=7)
    low = rest - middle
    high, middle, low = (piece.astype(jnp.bfloat16) for piece in (high, middle, low))
    return jnp.concatenate([high, high, middle, high, low, middle], axis=1)


def panel_kernel(
    consts_ref, pts_ref, pnorm_ref, pid_ref, scales_ref, cs_ref, cn_ref, own_cs_ref, own_cn_ref,
    own_ids_ref, finv_ref, sinv_ref, mid_ref, own_panels_ref, sel_ref, out_ref,
):
    signal = consts_ref[0]
    jitter = consts_ref[1]
    tile = pts_ref.shape[0] * pts_ref.shape[2]
    scaled = (pts_ref[...].reshape(tile, FEAT) * scales_ref[...]).T
    high, middle, low = split_three(scaled)
    packed = jnp.concatenate([high, middle, high, low, high, middle], axis=0)
    pnorm = pnorm_ref[...]
    pid = pid_ref[...]
    cross = jnp.dot(cs_ref[...], packed, preferred_element_type=jnp.float32)
    values = signal * jnp.exp(-0.5 * (cn_ref[...] + pnorm - 2.0 * cross))
    lead = lax.broadcasted_iota(jnp.int32, values.shape, 0)
    values = values + jnp.where(lead == pid, jitter, jnp.float32(0.0))
    first = jnp.dot(
        finv_ref[...], values[:PANEL], precision=HIGHEST, preferred_element_type=jnp.float32
    ).astype(jnp.bfloat16)
    reduced = values[PANEL:] - jnp.dot(mid_ref[...], first, preferred_element_type=jnp.float32)
    second = jnp.dot(
        sinv_ref[...], reduced, precision=HIGHEST, preferred_element_type=jnp.float32
    ).astype(jnp.bfloat16)
    own_cross = jnp.dot(own_cs_ref[...], packed, preferred_element_type=jnp.float32)
    own = signal * jnp.exp(-0.5 * (own_cn_ref[...] + pnorm - 2.0 * own_cross))
    own = own + jnp.where(own_ids_ref[...] == pid, jitter, jnp.float32(0.0))
    both = jnp.concatenate([first, second], axis=0)
    trailing = own - jnp.dot(own_panels_ref[...], both, preferred_element_type=jnp.float32)
    sel = sel_ref[...]
    out_ref[:BLK] = jnp.dot(sel, first, preferred_element_type=jnp.float32)
    out_ref[BLK : 2 * BLK] = jnp.dot(sel, second, preferred_element_type=jnp.float32)
    out_ref[2 * BLK :] = trailing


def panel_stage(consts, gathered, pnorm, pid, scales, cs, cn, own_cs, own_cn, own_ids, finv, sinv, mid, own_panels, sel):
    col_count, row_count, block_rows, _ = gathered.shape
    tile = col_count * block_rows
    grid_rows = tile * row_count
    out_rows = 2 * BLK + own_cs.shape[0]

    def whole(array):
        return pl.BlockSpec(array.shape, lambda i: (0,) * array.ndim)

    return pl.pallas_call(
        panel_kernel,
        grid=(row_count,),
        in_specs=[
            pl.BlockSpec(memory_space=pltpu.SMEM),
            pl.BlockSpec((col_count, 1, block_rows, FEAT), lambda i: (0, i, 0, 0)),
            pl.BlockSpec((1, tile), lambda i: (0, i)),
            pl.BlockSpec((1, tile), lambda i: (0, i)),
        ]
        + [whole(a) for a in (scales, cs, cn, own_cs, own_cn, own_ids, finv, sinv, mid, own_panels, sel)],
        out_specs=pl.BlockSpec((out_rows, tile), lambda i: (0, i)),
        out_shape=jax.ShapeDtypeStruct((out_rows, grid_rows), jnp.float32),
    )(consts, gathered, pnorm, pid, scales, cs, cn, own_cs, own_cn, own_ids, finv, sinv, mid, own_panels, sel)


def ridge_where(row_ids, col_ids, jitter):
    return jnp.where(row_ids[:, None] == col_ids[None, :], jitter, jnp.float32(0.0))


def gather_by_all_to_all(piece, axis_name):
    count = lax.axis_size(axis_name)
    copies = jnp.broadcast_to(piece[None], (count,) + piece.shape)
    return lax.all_to_all(copies, axis_name, 0, 0, tiled=True)


def on_device(points, feature_scales, amplitude, ridge):
    row_count = lax.axis_size("row")
    col_count = lax.axis_size("col")
    row = lax.axis_index("row")
    column = lax.axis_index("col")
    rows_one = points.shape[0]
    block_rows = rows_one // row_count
    col_blocks = SLAB // (BLK * col_count)
    panel_blocks = PANEL // (BLK * col_count)
    center_sources = SLAB // rows_one
    signal = amplitude[0]
    jitter = ridge[0]

    blocks = points.reshape(row_count, block_rows, FEAT)
    moved = lax.all_to_all(blocks, "row", 0, 0, tiled=True)

    first_slot = gather_by_all_to_all(moved[0], "col")[:center_sources]
    center_grid = gather_by_all_to_all(first_slot, "row")
    centers = center_grid.transpose(1, 0, 2, 3).reshape(SLAB, FEAT)

    moved, centers = lax.optimization_barrier((moved, centers))
    gathered = lax.all_gather(moved, "col", axis=0, tiled=False)
    grid_rows = gathered.shape[0] * gathered.shape[1] * block_rows

    center_scaled = centers * feature_scales
    center_norms = jnp.sum(center_scaled * center_scaled, axis=1)
    gathered_scaled = gathered * feature_scales
    point_norms = jnp.sum(gathered_scaled * gathered_scaled, axis=3).transpose(1, 0, 2).reshape(1, grid_rows)

    point_ids = (
        lax.broadcasted_iota(jnp.int32, (grid_rows // block_rows, block_rows), 0) * row_count
        + row
    ) * block_rows + lax.broadcasted_iota(jnp.int32, (grid_rows // block_rows, block_rows), 1)
    point_ids = point_ids.reshape(1, grid_rows)

    own_ids = (
        (
            lax.broadcasted_iota(jnp.int32, (col_blocks, BLK), 0) * col_count + column
        )
        * BLK
        + lax.broadcasted_iota(jnp.int32, (col_blocks, BLK), 1)
    )[2 * panel_blocks :].reshape(-1)
    own_scaled = jnp.take(center_scaled, own_ids, axis=0)
    own_norms = jnp.take(center_norms, own_ids, axis=0)

    lead_ids = jnp.arange(PANEL, dtype=jnp.int32)
    k11 = kernel_block(
        center_scaled[:PANEL], center_norms[:PANEL], center_scaled[:PANEL], center_norms[:PANEL], signal
    ) + ridge_where(lead_ids, lead_ids, jitter)
    first_inverse = lower_inverse(k11)
    used_ids = jnp.concatenate([jnp.arange(PANEL, 2 * PANEL, dtype=jnp.int32), own_ids])
    used_scaled = jnp.concatenate([center_scaled[PANEL : 2 * PANEL], own_scaled])
    used_norms = jnp.concatenate([center_norms[PANEL : 2 * PANEL], own_norms])
    used_kernel = kernel_block(
        used_scaled, used_norms, center_scaled[: 2 * PANEL], center_norms[: 2 * PANEL], signal
    ) + ridge_where(used_ids, jnp.arange(2 * PANEL, dtype=jnp.int32), jitter)
    center_first = jnp.dot(
        used_kernel[:, :PANEL], first_inverse.T, precision=HIGHEST, preferred_element_type=jnp.float32
    ).astype(jnp.bfloat16)
    first_mid = center_first[:PANEL]
    center_second = used_kernel[:, PANEL:] - jnp.dot(
        center_first, first_mid.T, preferred_element_type=jnp.float32
    )
    second_inverse = lower_inverse(center_second[:PANEL])
    second_own = jnp.dot(
        center_second[PANEL:], second_inverse.T, precision=HIGHEST, preferred_element_type=jnp.float32
    ).astype(jnp.bfloat16)
    own_panels = jnp.concatenate([center_first[PANEL:], second_own], axis=1)

    select = jnp.where(
        lax.broadcasted_iota(jnp.int32, (BLK, PANEL), 1)
        == column * BLK + lax.broadcasted_iota(jnp.int32, (BLK, PANEL), 0),
        1.0,
        0.0,
    ).astype(jnp.bfloat16)
    consts = jnp.stack([signal, jitter])
    finished = panel_stage(
        consts,
        gathered,
        point_norms,
        point_ids,
        feature_scales.reshape(1, FEAT),
        pack_left(center_scaled[: 2 * PANEL]),
        center_norms[: 2 * PANEL].reshape(-1, 1),
        pack_left(own_scaled),
        own_norms.reshape(-1, 1),
        own_ids.reshape(-1, 1),
        first_inverse,
        second_inverse,
        first_mid,
        own_panels,
        select,
    )
    return finished.reshape(col_blocks, 1, BLK, 1, grid_rows)


def solution(mesh):
    placed = (P(("row", "col"), None), P(), P(), P())
    return jax.shard_map(
        on_device,
        mesh=mesh,
        in_specs=placed,
        out_specs=P(None, "col", None, "row", None),
        check_vma=False,
    )
```

```python
import jax
import jax.numpy as jnp
from jax import lax
from jax.sharding import PartitionSpec as P
from jax.experimental import pallas as pl
from jax.experimental.pallas import tpu as pltpu

FEAT = 64
SLAB = 1536
PANEL = 256
BLK = 16

HIGHEST = lax.Precision.HIGHEST


def kernel_block(left, left_norms, right, right_norms, signal):
    cross = jnp.dot(left, right.T, precision=HIGHEST, preferred_element_type=jnp.float32)
    return signal * jnp.exp(-0.5 * (left_norms[:, None] + right_norms[None, :] - 2.0 * cross))


def _nt(left, right):
    return lax.dot_general(
        left, right, (((1,), (1,)), ((), ())), precision=HIGHEST, preferred_element_type=jnp.float32
    )


def lower_inverse_kernel(a_ref, o_ref, s_ref, x_ref):
    half = a_ref.shape[0] // 2
    lanes = lax.broadcasted_iota(jnp.int32, (half, half), 1)
    rows = lax.broadcasted_iota(jnp.int32, (half, 1), 0)
    lane_row = lax.broadcasted_iota(jnp.int32, (1, half), 1)
    eye = jnp.where(lax.broadcasted_iota(jnp.int32, (half, half), 0) == lanes, 1.0, 0.0)

    def pick(values, index):
        return jnp.sum(jnp.where(lane_row == index, values, 0.0), axis=1, keepdims=True)

    def step(j, carry):
        k = 2 * j
        s = s_ref[...]
        x = x_ref[...]
        row0 = s_ref[pl.ds(k, 1), :]
        row1 = s_ref[pl.ds(k + 1, 1), :]
        col0 = jnp.sum(jnp.where(lanes == k, s, 0.0), axis=1, keepdims=True)
        col1 = jnp.sum(jnp.where(lanes == k + 1, s, 0.0), axis=1, keepdims=True)
        root0 = jnp.sqrt(pick(row0, k))
        cross = pick(row1, k) / root0
        root1 = jnp.sqrt(pick(row1, k + 1) - cross * cross)
        col0 = jnp.where(rows >= k, col0 / root0, 0.0)
        row0 = jnp.where(lane_row >= k, row0 / root0, 0.0)
        col1 = jnp.where(rows >= k + 1, (col1 - col0 * cross) / root1, 0.0)
        row1 = jnp.where(lane_row >= k + 1, (row1 - cross * row0) / root1, 0.0)
        s_ref[...] = s - col0 * row0 - col1 * row1
        x0 = x_ref[pl.ds(k, 1), :] / root0
        x1 = (x_ref[pl.ds(k + 1, 1), :] - cross * x0) / root1
        rest = x - jnp.where(rows > k, col0, 0.0) * x0 - jnp.where(rows > k + 1, col1, 0.0) * x1
        x_ref[...] = jnp.where(rows == k, x0, jnp.where(rows == k + 1, x1, rest))
        return carry

    def base(block):
        s_ref[...] = block
        x_ref[...] = eye.astype(jnp.float32)
        lax.fori_loop(0, half // 2, step, 0)
        return x_ref[...]

    first = base(a_ref[:half, :half])
    lower = _nt(a_ref[half:, :half], first)
    schur = a_ref[half:, half:] - _nt(lower, lower)
    second = base((schur + schur.T) * 0.5)
    below = -jnp.dot(
        second,
        jnp.dot(lower, first, precision=HIGHEST, preferred_element_type=jnp.float32),
        precision=HIGHEST,
        preferred_element_type=jnp.float32,
    )
    o_ref[:half, :half] = first
    o_ref[:half, half:] = jnp.zeros((half, half), jnp.float32)
    o_ref[half:, :half] = below
    o_ref[half:, half:] = second


def lower_inverse(block):
    size = block.shape[0]
    half = size // 2
    block = (block + block.T) * 0.5
    return pl.pallas_call(
        lower_inverse_kernel,
        out_shape=jax.ShapeDtypeStruct((size, size), jnp.float32),
        scratch_shapes=[pltpu.VMEM((half, half), jnp.float32), pltpu.VMEM((half, half), jnp.float32)],
    )(block)


def split_three(values):
    high = values.astype(jnp.bfloat16)
    rest = values - high.astype(jnp.float32)
    middle = rest.astype(jnp.bfloat16)
    low = (rest - middle.astype(jnp.float32)).astype(jnp.bfloat16)
    return high, middle, low


def pack_left(values):
    high = lax.reduce_precision(values, exponent_bits=8, mantissa_bits=7)
    rest = values - high
    middle = lax.reduce_precision(rest, exponent_bits=8, mantissa_bits=7)
    low = rest - middle
    high, middle, low = (piece.astype(jnp.bfloat16) for piece in (high, middle, low))
    return jnp.concatenate([high, high, middle, high, low, middle], axis=1)


def panel_kernel(
    consts_ref, pts_ref, pnorm_ref, pid_ref, scales_ref, cs_ref, cn_ref, own_cs_ref, own_cn_ref,
    own_ids_ref, finv_ref, sinv_ref, mid_ref, own_panels_ref, sel_ref, out_ref,
):
    signal = consts_ref[0]
    jitter = consts_ref[1]
    tile = pts_ref.shape[0] * pts_ref.shape[2]
    scaled = (pts_ref[...].reshape(tile, FEAT) * scales_ref[...]).T
    high, middle, low = split_three(scaled)
    packed = jnp.concatenate([high, middle, high, low, high, middle], axis=0)
    pnorm = pnorm_ref[...]
    pid = pid_ref[...]
    cross = jnp.dot(cs_ref[...], packed, preferred_element_type=jnp.float32)
    values = signal * jnp.exp(-0.5 * (cn_ref[...] + pnorm - 2.0 * cross))
    lead = lax.broadcasted_iota(jnp.int32, values.shape, 0)
    values = values + jnp.where(lead == pid, jitter, jnp.float32(0.0))
    first = jnp.dot(
        finv_ref[...], values[:PANEL], precision=HIGHEST, preferred_element_type=jnp.float32
    ).astype(jnp.bfloat16)
    reduced = values[PANEL:] - jnp.dot(mid_ref[...], first, preferred_element_type=jnp.float32)
    second = jnp.dot(
        sinv_ref[...], reduced, precision=HIGHEST, preferred_element_type=jnp.float32
    ).astype(jnp.bfloat16)
    own_cross = jnp.dot(own_cs_ref[...], packed, preferred_element_type=jnp.float32)
    own = signal * jnp.exp(-0.5 * (own_cn_ref[...] + pnorm - 2.0 * own_cross))
    own = own + jnp.where(own_ids_ref[...] == pid, jitter, jnp.float32(0.0))
    both = jnp.concatenate([first, second], axis=0)
    trailing = own - jnp.dot(own_panels_ref[...], both, preferred_element_type=jnp.float32)
    sel = sel_ref[...]
    out_ref[:BLK] = jnp.dot(sel, first, preferred_element_type=jnp.float32)
    out_ref[BLK : 2 * BLK] = jnp.dot(sel, second, preferred_element_type=jnp.float32)
    out_ref[2 * BLK :] = trailing


def panel_stage(consts, gathered, pnorm, pid, scales, cs, cn, own_cs, own_cn, own_ids, finv, sinv, mid, own_panels, sel):
    col_count, row_count, block_rows, _ = gathered.shape
    tile = col_count * block_rows
    grid_rows = tile * row_count
    out_rows = 2 * BLK + own_cs.shape[0]

    def whole(array):
        return pl.BlockSpec(array.shape, lambda i: (0,) * array.ndim)

    return pl.pallas_call(
        panel_kernel,
        grid=(row_count,),
        in_specs=[
            pl.BlockSpec(memory_space=pltpu.SMEM),
            pl.BlockSpec((col_count, 1, block_rows, FEAT), lambda i: (0, i, 0, 0)),
            pl.BlockSpec((1, tile), lambda i: (0, i)),
            pl.BlockSpec((1, tile), lambda i: (0, i)),
        ]
        + [whole(a) for a in (scales, cs, cn, own_cs, own_cn, own_ids, finv, sinv, mid, own_panels, sel)],
        out_specs=pl.BlockSpec((out_rows, tile), lambda i: (0, i)),
        out_shape=jax.ShapeDtypeStruct((out_rows, grid_rows), jnp.float32),
    )(consts, gathered, pnorm, pid, scales, cs, cn, own_cs, own_cn, own_ids, finv, sinv, mid, own_panels, sel)


def ridge_where(row_ids, col_ids, jitter):
    return jnp.where(row_ids[:, None] == col_ids[None, :], jitter, jnp.float32(0.0))


def gather_by_all_to_all(piece, axis_name):
    count = lax.axis_size(axis_name)
    copies = jnp.broadcast_to(piece[None], (count,) + piece.shape)
    return lax.all_to_all(copies, axis_name, 0, 0, tiled=True)


def on_device(points, feature_scales, amplitude, ridge):
    row_count = lax.axis_size("row")
    col_count = lax.axis_size("col")
    row = lax.axis_index("row")
    column = lax.axis_index("col")
    rows_one = points.shape[0]
    block_rows = rows_one // row_count
    col_blocks = SLAB // (BLK * col_count)
    panel_blocks = PANEL // (BLK * col_count)
    center_sources = SLAB // rows_one
    signal = amplitude[0]
    jitter = ridge[0]

    blocks = points.reshape(row_count, block_rows, FEAT)
    moved = lax.all_to_all(blocks, "row", 0, 0, tiled=True)

    first_slot = gather_by_all_to_all(moved[0], "col")[:center_sources]
    center_grid = gather_by_all_to_all(first_slot, "row")
    centers = center_grid.transpose(1, 0, 2, 3).reshape(SLAB, FEAT)

    moved, centers = lax.optimization_barrier((moved, centers))
    gathered = lax.all_gather(moved, "col", axis=0, tiled=False)
    grid_rows = gathered.shape[0] * gathered.shape[1] * block_rows

    center_scaled = centers * feature_scales
    center_norms = jnp.sum(center_scaled * center_scaled, axis=1)
    gathered_scaled = gathered * feature_scales
    point_norms = jnp.sum(gathered_scaled * gathered_scaled, axis=3).transpose(1, 0, 2).reshape(1, grid_rows)

    point_ids = (
        lax.broadcasted_iota(jnp.int32, (grid_rows // block_rows, block_rows), 0) * row_count
        + row
    ) * block_rows + lax.broadcasted_iota(jnp.int32, (grid_rows // block_rows, block_rows), 1)
    point_ids = point_ids.reshape(1, grid_rows)

    own_ids = (
        (
            lax.broadcasted_iota(jnp.int32, (col_blocks, BLK), 0) * col_count + column
        )
        * BLK
        + lax.broadcasted_iota(jnp.int32, (col_blocks, BLK), 1)
    )[2 * panel_blocks :].reshape(-1)
    own_scaled = jnp.take(center_scaled, own_ids, axis=0)
    own_norms = jnp.take(center_norms, own_ids, axis=0)

    lead_ids = jnp.arange(PANEL, dtype=jnp.int32)
    k11 = kernel_block(
        center_scaled[:PANEL], center_norms[:PANEL], center_scaled[:PANEL], center_norms[:PANEL], signal
    ) + ridge_where(lead_ids, lead_ids, jitter)
    first_inverse = lower_inverse(k11)
    used_ids = jnp.concatenate([jnp.arange(PANEL, 2 * PANEL, dtype=jnp.int32), own_ids])
    used_scaled = jnp.concatenate([center_scaled[PANEL : 2 * PANEL], own_scaled])
    used_norms = jnp.concatenate([center_norms[PANEL : 2 * PANEL], own_norms])
    used_kernel = kernel_block(
        used_scaled, used_norms, center_scaled[: 2 * PANEL], center_norms[: 2 * PANEL], signal
    ) + ridge_where(used_ids, jnp.arange(2 * PANEL, dtype=jnp.int32), jitter)
    center_first = jnp.dot(
        used_kernel[:, :PANEL], first_inverse.T, precision=HIGHEST, preferred_element_type=jnp.float32
    ).astype(jnp.bfloat16)
    first_mid = center_first[:PANEL]
    center_second = used_kernel[:, PANEL:] - jnp.dot(
        center_first, first_mid.T, preferred_element_type=jnp.float32
    )
    second_inverse = lower_inverse(center_second[:PANEL])
    second_own = jnp.dot(
        center_second[PANEL:], second_inverse.T, precision=HIGHEST, preferred_element_type=jnp.float32
    ).astype(jnp.bfloat16)
    own_panels = jnp.concatenate([center_first[PANEL:], second_own], axis=1)

    select = jnp.where(
        lax.broadcasted_iota(jnp.int32, (BLK, PANEL), 1)
        == column * BLK + lax.broadcasted_iota(jnp.int32, (BLK, PANEL), 0),
        1.0,
        0.0,
    ).astype(jnp.bfloat16)
    consts = jnp.stack([signal, jitter])
    finished = panel_stage(
        consts,
        gathered,
        point_norms,
        point_ids,
        feature_scales.reshape(1, FEAT),
        pack_left(center_scaled[: 2 * PANEL]),
        center_norms[: 2 * PANEL].reshape(-1, 1),
        pack_left(own_scaled),
        own_norms.reshape(-1, 1),
        own_ids.reshape(-1, 1),
        first_inverse,
        second_inverse,
        first_mid,
        own_panels,
        select,
    )
    return finished.reshape(col_blocks, 1, BLK, 1, grid_rows)


def solution(mesh):
    placed = (P(("row", "col"), None), P(), P(), P())
    return jax.shard_map(
        on_device,
        mesh=mesh,
        in_specs=placed,
        out_specs=P(None, "col", None, "row", None),
        check_vma=False,
    )
```

```python
import jax
import jax.numpy as jnp
from jax import lax
from jax.sharding import PartitionSpec as P
from jax.experimental import pallas as pl
from jax.experimental.pallas import tpu as pltpu

FEAT = 64
SLAB = 1536
PANEL = 256
BLK = 16

HIGHEST = lax.Precision.HIGHEST
WIDTH = 4


def kernel_block(left, left_norms, right, right_norms, signal):
    cross = jnp.dot(left, right.T, precision=HIGHEST, preferred_element_type=jnp.float32)
    return signal * jnp.exp(-0.5 * (left_norms[:, None] + right_norms[None, :] - 2.0 * cross))


def _nt(left, right):
    return lax.dot_general(
        left, right, (((1,), (1,)), ((), ())), precision=HIGHEST, preferred_element_type=jnp.float32
    )


def lower_inverse_kernel(a_ref, o_ref, s_ref, x_ref):
    half = a_ref.shape[0] // 2
    lanes = lax.broadcasted_iota(jnp.int32, (half, half), 1)
    rows = lax.broadcasted_iota(jnp.int32, (half, 1), 0)
    lane_row = lax.broadcasted_iota(jnp.int32, (1, half), 1)
    eye = jnp.where(lax.broadcasted_iota(jnp.int32, (half, half), 0) == lanes, 1.0, 0.0)

    def pick(values, index):
        return jnp.sum(jnp.where(lane_row == index, values, 0.0), axis=1, keepdims=True)

    def step(j, carry):
        k = WIDTH * j
        s = s_ref[...]
        x = x_ref[...]
        cols, rows_out, xs = [], [], []
        update = s
        rest = x
        for m in range(WIDTH):
            col = jnp.sum(jnp.where(lanes == k + m, s, 0.0), axis=1, keepdims=True)
            row = s_ref[pl.ds(k + m, 1), :]
            xm = x_ref[pl.ds(k + m, 1), :]
            for p in range(m):
                factor = pick(rows_out[p], k + m)
                col = col - cols[p] * factor
                row = row - factor * rows_out[p]
                xm = xm - factor * xs[p]
            root = jnp.sqrt(pick(row, k + m))
            col = jnp.where(rows >= k + m, col / root, 0.0)
            row = jnp.where(lane_row >= k + m, row / root, 0.0)
            xm = xm / root
            cols.append(col)
            rows_out.append(row)
            xs.append(xm)
            update = update - col * row
            rest = rest - jnp.where(rows > k + m, col, 0.0) * xm
        s_ref[...] = update
        for m in range(WIDTH):
            rest = jnp.where(rows == k + m, xs[m], rest)
        x_ref[...] = rest
        return carry

    def base(block):
        s_ref[...] = block
        x_ref[...] = eye.astype(jnp.float32)
        lax.fori_loop(0, half // WIDTH, step, 0)
        return x_ref[...]

    first = base(a_ref[:half, :half])
    lower = _nt(a_ref[half:, :half], first)
    schur = a_ref[half:, half:] - _nt(lower, lower)
    second = base((schur + schur.T) * 0.5)
    below = -jnp.dot(
        second,
        jnp.dot(lower, first, precision=HIGHEST, preferred_element_type=jnp.float32),
        precision=HIGHEST,
        preferred_element_type=jnp.float32,
    )
    o_ref[:half, :half] = first
    o_ref[:half, half:] = jnp.zeros((half, half), jnp.float32)
    o_ref[half:, :half] = below
    o_ref[half:, half:] = second


def lower_inverse(block):
    size = block.shape[0]
    half = size // 2
    block = (block + block.T) * 0.5
    return pl.pallas_call(
        lower_inverse_kernel,
        out_shape=jax.ShapeDtypeStruct((size, size), jnp.float32),
        scratch_shapes=[pltpu.VMEM((half, half), jnp.float32), pltpu.VMEM((half, half), jnp.float32)],
    )(block)


def split_three(values):
    high = values.astype(jnp.bfloat16)
    rest = values - high.astype(jnp.float32)
    middle = rest.astype(jnp.bfloat16)
    low = (rest - middle.astype(jnp.float32)).astype(jnp.bfloat16)
    return high, middle, low


def pack_left(values):
    high = lax.reduce_precision(values, exponent_bits=8, mantissa_bits=7)
    rest = values - high
    middle = lax.reduce_precision(rest, exponent_bits=8, mantissa_bits=7)
    low = rest - middle
    high, middle, low = (piece.astype(jnp.bfloat16) for piece in (high, middle, low))
    return jnp.concatenate([high, high, middle, high, low, middle], axis=1)


def panel_kernel(
    consts_ref, pts_ref, pnorm_ref, pid_ref, scales_ref, cs_ref, cn_ref, own_cs_ref, own_cn_ref,
    own_ids_ref, finv_ref, sinv_ref, mid_ref, own_panels_ref, sel_ref, out_ref,
):
    signal = consts_ref[0]
    jitter = consts_ref[1]
    tile = pts_ref.shape[0] * pts_ref.shape[2]
    scaled = (pts_ref[...].reshape(tile, FEAT) * scales_ref[...]).T
    high, middle, low = split_three(scaled)
    packed = jnp.concatenate([high, middle, high, low, high, middle], axis=0)
    pnorm = pnorm_ref[...]
    pid = pid_ref[...]
    cross = jnp.dot(cs_ref[...], packed, preferred_element_type=jnp.float32)
    values = signal * jnp.exp(-0.5 * (cn_ref[...] + pnorm - 2.0 * cross))
    lead = lax.broadcasted_iota(jnp.int32, values.shape, 0)
    values = values + jnp.where(lead == pid, jitter, jnp.float32(0.0))
    first = jnp.dot(
        finv_ref[...], values[:PANEL], precision=HIGHEST, preferred_element_type=jnp.float32
    ).astype(jnp.bfloat16)
    reduced = values[PANEL:] - jnp.dot(mid_ref[...], first, preferred_element_type=jnp.float32)
    second = jnp.dot(
        sinv_ref[...], reduced, precision=HIGHEST, preferred_element_type=jnp.float32
    ).astype(jnp.bfloat16)
    own_cross = jnp.dot(own_cs_ref[...], packed, preferred_element_type=jnp.float32)
    own = signal * jnp.exp(-0.5 * (own_cn_ref[...] + pnorm - 2.0 * own_cross))
    own = own + jnp.where(own_ids_ref[...] == pid, jitter, jnp.float32(0.0))
    both = jnp.concatenate([first, second], axis=0)
    trailing = own - jnp.dot(own_panels_ref[...], both, preferred_element_type=jnp.float32)
    sel = sel_ref[...]
    out_ref[:BLK] = jnp.dot(sel, first, preferred_element_type=jnp.float32)
    out_ref[BLK : 2 * BLK] = jnp.dot(sel, second, preferred_element_type=jnp.float32)
    out_ref[2 * BLK :] = trailing


def panel_stage(consts, gathered, pnorm, pid, scales, cs, cn, own_cs, own_cn, own_ids, finv, sinv, mid, own_panels, sel):
    col_count, row_count, block_rows, _ = gathered.shape
    tile = col_count * block_rows
    grid_rows = tile * row_count
    out_rows = 2 * BLK + own_cs.shape[0]

    def whole(array):
        return pl.BlockSpec(array.shape, lambda i: (0,) * array.ndim)

    return pl.pallas_call(
        panel_kernel,
        grid=(row_count,),
        in_specs=[
            pl.BlockSpec(memory_space=pltpu.SMEM),
            pl.BlockSpec((col_count, 1, block_rows, FEAT), lambda i: (0, i, 0, 0)),
            pl.BlockSpec((1, tile), lambda i: (0, i)),
            pl.BlockSpec((1, tile), lambda i: (0, i)),
        ]
        + [whole(a) for a in (scales, cs, cn, own_cs, own_cn, own_ids, finv, sinv, mid, own_panels, sel)],
        out_specs=pl.BlockSpec((out_rows, tile), lambda i: (0, i)),
        out_shape=jax.ShapeDtypeStruct((out_rows, grid_rows), jnp.float32),
    )(consts, gathered, pnorm, pid, scales, cs, cn, own_cs, own_cn, own_ids, finv, sinv, mid, own_panels, sel)


def ridge_where(row_ids, col_ids, jitter):
    return jnp.where(row_ids[:, None] == col_ids[None, :], jitter, jnp.float32(0.0))


def gather_by_all_to_all(piece, axis_name):
    count = lax.axis_size(axis_name)
    copies = jnp.broadcast_to(piece[None], (count,) + piece.shape)
    return lax.all_to_all(copies, axis_name, 0, 0, tiled=True)


def on_device(points, feature_scales, amplitude, ridge):
    row_count = lax.axis_size("row")
    col_count = lax.axis_size("col")
    row = lax.axis_index("row")
    column = lax.axis_index("col")
    rows_one = points.shape[0]
    block_rows = rows_one // row_count
    col_blocks = SLAB // (BLK * col_count)
    panel_blocks = PANEL // (BLK * col_count)
    center_sources = SLAB // rows_one
    signal = amplitude[0]
    jitter = ridge[0]

    blocks = points.reshape(row_count, block_rows, FEAT)
    moved = lax.all_to_all(blocks, "row", 0, 0, tiled=True)

    first_slot = gather_by_all_to_all(moved[0], "col")[:center_sources]
    center_grid = gather_by_all_to_all(first_slot, "row")
    centers = center_grid.transpose(1, 0, 2, 3).reshape(SLAB, FEAT)

    moved, centers = lax.optimization_barrier((moved, centers))
    gathered = lax.all_gather(moved, "col", axis=0, tiled=False)
    grid_rows = gathered.shape[0] * gathered.shape[1] * block_rows

    center_scaled = centers * feature_scales
    center_norms = jnp.sum(center_scaled * center_scaled, axis=1)
    gathered_scaled = gathered * feature_scales
    point_norms = jnp.sum(gathered_scaled * gathered_scaled, axis=3).transpose(1, 0, 2).reshape(1, grid_rows)

    point_ids = (
        lax.broadcasted_iota(jnp.int32, (grid_rows // block_rows, block_rows), 0) * row_count
        + row
    ) * block_rows + lax.broadcasted_iota(jnp.int32, (grid_rows // block_rows, block_rows), 1)
    point_ids = point_ids.reshape(1, grid_rows)

    own_ids = (
        (
            lax.broadcasted_iota(jnp.int32, (col_blocks, BLK), 0) * col_count + column
        )
        * BLK
        + lax.broadcasted_iota(jnp.int32, (col_blocks, BLK), 1)
    )[2 * panel_blocks :].reshape(-1)
    own_scaled = jnp.take(center_scaled, own_ids, axis=0)
    own_norms = jnp.take(center_norms, own_ids, axis=0)

    lead_ids = jnp.arange(PANEL, dtype=jnp.int32)
    k11 = kernel_block(
        center_scaled[:PANEL], center_norms[:PANEL], center_scaled[:PANEL], center_norms[:PANEL], signal
    ) + ridge_where(lead_ids, lead_ids, jitter)
    first_inverse = lower_inverse(k11)
    used_ids = jnp.concatenate([jnp.arange(PANEL, 2 * PANEL, dtype=jnp.int32), own_ids])
    used_scaled = jnp.concatenate([center_scaled[PANEL : 2 * PANEL], own_scaled])
    used_norms = jnp.concatenate([center_norms[PANEL : 2 * PANEL], own_norms])
    used_kernel = kernel_block(
        used_scaled, used_norms, center_scaled[: 2 * PANEL], center_norms[: 2 * PANEL], signal
    ) + ridge_where(used_ids, jnp.arange(2 * PANEL, dtype=jnp.int32), jitter)
    center_first = jnp.dot(
        used_kernel[:, :PANEL], first_inverse.T, precision=HIGHEST, preferred_element_type=jnp.float32
    ).astype(jnp.bfloat16)
    first_mid = center_first[:PANEL]
    center_second = used_kernel[:, PANEL:] - jnp.dot(
        center_first, first_mid.T, preferred_element_type=jnp.float32
    )
    second_inverse = lower_inverse(center_second[:PANEL])
    second_own = jnp.dot(
        center_second[PANEL:], second_inverse.T, precision=HIGHEST, preferred_element_type=jnp.float32
    ).astype(jnp.bfloat16)
    own_panels = jnp.concatenate([center_first[PANEL:], second_own], axis=1)

    select = jnp.where(
        lax.broadcasted_iota(jnp.int32, (BLK, PANEL), 1)
        == column * BLK + lax.broadcasted_iota(jnp.int32, (BLK, PANEL), 0),
        1.0,
        0.0,
    ).astype(jnp.bfloat16)
    consts = jnp.stack([signal, jitter])
    finished = panel_stage(
        consts,
        gathered,
        point_norms,
        point_ids,
        feature_scales.reshape(1, FEAT),
        pack_left(center_scaled[: 2 * PANEL]),
        center_norms[: 2 * PANEL].reshape(-1, 1),
        pack_left(own_scaled),
        own_norms.reshape(-1, 1),
        own_ids.reshape(-1, 1),
        first_inverse,
        second_inverse,
        first_mid,
        own_panels,
        select,
    )
    return finished.reshape(col_blocks, 1, BLK, 1, grid_rows)


def solution(mesh):
    placed = (P(("row", "col"), None), P(), P(), P())
    return jax.shard_map(
        on_device,
        mesh=mesh,
        in_specs=placed,
        out_specs=P(None, "col", None, "row", None),
        check_vma=False,
    )
```

```python
import jax
import jax.numpy as jnp
from jax import lax
from jax.sharding import PartitionSpec as P
from jax.experimental import pallas as pl
from jax.experimental.pallas import tpu as pltpu

FEAT = 64
SLAB = 1536
PANEL = 256
BLK = 16

HIGHEST = lax.Precision.HIGHEST


def kernel_block(left, left_norms, right, right_norms, signal):
    cross = jnp.dot(left, right.T, precision=HIGHEST, preferred_element_type=jnp.float32)
    return signal * jnp.exp(-0.5 * (left_norms[:, None] + right_norms[None, :] - 2.0 * cross))


def _nt(left, right):
    return lax.dot_general(
        left, right, (((1,), (1,)), ((), ())), precision=HIGHEST, preferred_element_type=jnp.float32
    )


def lower_inverse_kernel(a_ref, o_ref, s_ref, x_ref):
    half = a_ref.shape[0] // 2
    lanes = lax.broadcasted_iota(jnp.int32, (half, half), 1)
    rows = lax.broadcasted_iota(jnp.int32, (half, 1), 0)
    lane_row = lax.broadcasted_iota(jnp.int32, (1, half), 1)
    eye = jnp.where(lax.broadcasted_iota(jnp.int32, (half, half), 0) == lanes, 1.0, 0.0)

    def pick(values, index):
        return jnp.sum(jnp.where(lane_row == index, values, 0.0), axis=1, keepdims=True)

    def step(j, carry):
        k = 2 * j
        s = s_ref[...]
        x = x_ref[...]
        row0 = s_ref[pl.ds(k, 1), :]
        row1 = s_ref[pl.ds(k + 1, 1), :]
        col0 = jnp.sum(jnp.where(lanes == k, s, 0.0), axis=1, keepdims=True)
        col1 = jnp.sum(jnp.where(lanes == k + 1, s, 0.0), axis=1, keepdims=True)
        root0 = jnp.sqrt(pick(row0, k))
        cross = pick(row1, k) / root0
        root1 = jnp.sqrt(pick(row1, k + 1) - cross * cross)
        col0 = jnp.where(rows >= k, col0 / root0, 0.0)
        row0 = jnp.where(lane_row >= k, row0 / root0, 0.0)
        col1 = jnp.where(rows >= k + 1, (col1 - col0 * cross) / root1, 0.0)
        row1 = jnp.where(lane_row >= k + 1, (row1 - cross * row0) / root1, 0.0)
        s_ref[...] = s - col0 * row0 - col1 * row1
        x0 = x_ref[pl.ds(k, 1), :] / root0
        x1 = (x_ref[pl.ds(k + 1, 1), :] - cross * x0) / root1
        rest = x - jnp.where(rows > k, col0, 0.0) * x0 - jnp.where(rows > k + 1, col1, 0.0) * x1
        x_ref[...] = jnp.where(rows == k, x0, jnp.where(rows == k + 1, x1, rest))
        return carry

    def base(block):
        s_ref[...] = block
        x_ref[...] = eye.astype(jnp.float32)
        lax.fori_loop(0, half // 2, step, 0)
        return x_ref[...]

    first = base(a_ref[:half, :half])
    lower = _nt(a_ref[half:, :half], first)
    schur = a_ref[half:, half:] - _nt(lower, lower)
    second = base((schur + schur.T) * 0.5)
    below = -jnp.dot(
        second,
        jnp.dot(lower, first, precision=HIGHEST, preferred_element_type=jnp.float32),
        precision=HIGHEST,
        preferred_element_type=jnp.float32,
    )
    o_ref[:half, :half] = first
    o_ref[:half, half:] = jnp.zeros((half, half), jnp.float32)
    o_ref[half:, :half] = below
    o_ref[half:, half:] = second


def lower_inverse(block):
    size = block.shape[0]
    half = size // 2
    block = (block + block.T) * 0.5
    return pl.pallas_call(
        lower_inverse_kernel,
        out_shape=jax.ShapeDtypeStruct((size, size), jnp.float32),
        scratch_shapes=[pltpu.VMEM((half, half), jnp.float32), pltpu.VMEM((half, half), jnp.float32)],
    )(block)


def split_three(values):
    high = values.astype(jnp.bfloat16)
    rest = values - high.astype(jnp.float32)
    middle = rest.astype(jnp.bfloat16)
    low = (rest - middle.astype(jnp.float32)).astype(jnp.bfloat16)
    return high, middle, low


def pack_left(values):
    high = lax.reduce_precision(values, exponent_bits=8, mantissa_bits=7)
    rest = values - high
    middle = lax.reduce_precision(rest, exponent_bits=8, mantissa_bits=7)
    low = rest - middle
    high, middle, low = (piece.astype(jnp.bfloat16) for piece in (high, middle, low))
    return jnp.concatenate([high, high, middle, high, low, middle], axis=1)


def panel_kernel(
    consts_ref, pts_ref, pnorm_ref, pid_ref, scales_ref, cs_ref, cn_ref, own_cs_ref, own_cn_ref,
    own_ids_ref, finv_ref, sinv_ref, mid_ref, own_panels_ref, sel_ref, out_ref,
):
    signal = consts_ref[0]
    jitter = consts_ref[1]
    tile = pts_ref.shape[0] * pts_ref.shape[2]
    scaled = (pts_ref[...].reshape(tile, FEAT) * scales_ref[...]).T
    high, middle, low = split_three(scaled)
    packed = jnp.concatenate([high, middle, high, low, high, middle], axis=0)
    pnorm = pnorm_ref[...]
    pid = pid_ref[...]
    cross = jnp.dot(cs_ref[...], packed, preferred_element_type=jnp.float32)
    values = signal * jnp.exp(-0.5 * (cn_ref[...] + pnorm - 2.0 * cross))
    lead = lax.broadcasted_iota(jnp.int32, values.shape, 0)
    values = values + jnp.where(lead == pid, jitter, jnp.float32(0.0))
    first = jnp.dot(
        finv_ref[...], values[:PANEL], precision=HIGHEST, preferred_element_type=jnp.float32
    ).astype(jnp.bfloat16)
    reduced = values[PANEL:] - jnp.dot(mid_ref[...], first, preferred_element_type=jnp.float32)
    second = jnp.dot(
        sinv_ref[...], reduced, precision=HIGHEST, preferred_element_type=jnp.float32
    ).astype(jnp.bfloat16)
    own_cross = jnp.dot(own_cs_ref[...], packed, preferred_element_type=jnp.float32)
    own = signal * jnp.exp(-0.5 * (own_cn_ref[...] + pnorm - 2.0 * own_cross))
    own = own + jnp.where(own_ids_ref[...] == pid, jitter, jnp.float32(0.0))
    both = jnp.concatenate([first, second], axis=0)
    trailing = own - jnp.dot(own_panels_ref[...], both, preferred_element_type=jnp.float32)
    sel = sel_ref[...]
    result = jnp.concatenate(
        [
            jnp.dot(sel, first, preferred_element_type=jnp.float32),
            jnp.dot(sel, second, preferred_element_type=jnp.float32),
            trailing,
        ],
        axis=0,
    )
    lanes = out_ref.shape[2]
    for chunk in range(out_ref.shape[1]):
        out_ref[:, chunk, :] = result[:, chunk * lanes : (chunk + 1) * lanes]


def panel_stage(consts, gathered, pnorm, pid, scales, cs, cn, own_cs, own_cn, own_ids, finv, sinv, mid, own_panels, sel):
    col_count, row_count, block_rows, _ = gathered.shape
    tile = col_count * block_rows
    grid_rows = tile * row_count
    out_rows = 2 * BLK + own_cs.shape[0]

    def whole(array):
        return pl.BlockSpec(array.shape, lambda i: (0,) * array.ndim)

    return pl.pallas_call(
        panel_kernel,
        grid=(row_count,),
        in_specs=[
            pl.BlockSpec(memory_space=pltpu.SMEM),
            pl.BlockSpec((col_count, 1, block_rows, FEAT), lambda i: (0, i, 0, 0)),
            pl.BlockSpec((1, tile), lambda i: (0, i)),
            pl.BlockSpec((1, tile), lambda i: (0, i)),
        ]
        + [whole(a) for a in (scales, cs, cn, own_cs, own_cn, own_ids, finv, sinv, mid, own_panels, sel)],
        out_specs=pl.BlockSpec((out_rows, tile // 128, 128), lambda i: (0, i, 0)),
        out_shape=jax.ShapeDtypeStruct((out_rows, grid_rows // 128, 128), jnp.float32),
    )(consts, gathered, pnorm, pid, scales, cs, cn, own_cs, own_cn, own_ids, finv, sinv, mid, own_panels, sel)


def ridge_where(row_ids, col_ids, jitter):
    return jnp.where(row_ids[:, None] == col_ids[None, :], jitter, jnp.float32(0.0))


def gather_by_all_to_all(piece, axis_name):
    count = lax.axis_size(axis_name)
    copies = jnp.broadcast_to(piece[None], (count,) + piece.shape)
    return lax.all_to_all(copies, axis_name, 0, 0, tiled=True)


def on_device(points, feature_scales, amplitude, ridge):
    row_count = lax.axis_size("row")
    col_count = lax.axis_size("col")
    row = lax.axis_index("row")
    column = lax.axis_index("col")
    rows_one = points.shape[0]
    block_rows = rows_one // row_count
    col_blocks = SLAB // (BLK * col_count)
    panel_blocks = PANEL // (BLK * col_count)
    center_sources = SLAB // rows_one
    signal = amplitude[0]
    jitter = ridge[0]

    blocks = points.reshape(row_count, block_rows, FEAT)
    moved = lax.all_to_all(blocks, "row", 0, 0, tiled=True)

    first_slot = gather_by_all_to_all(moved[0], "col")[:center_sources]
    center_grid = gather_by_all_to_all(first_slot, "row")
    centers = center_grid.transpose(1, 0, 2, 3).reshape(SLAB, FEAT)

    moved, centers = lax.optimization_barrier((moved, centers))
    gathered = lax.all_gather(moved, "col", axis=0, tiled=False)
    grid_rows = gathered.shape[0] * gathered.shape[1] * block_rows

    center_scaled = centers * feature_scales
    center_norms = jnp.sum(center_scaled * center_scaled, axis=1)
    gathered_scaled = gathered * feature_scales
    point_norms = jnp.sum(gathered_scaled * gathered_scaled, axis=3).transpose(1, 0, 2).reshape(1, grid_rows)

    point_ids = (
        lax.broadcasted_iota(jnp.int32, (grid_rows // block_rows, block_rows), 0) * row_count
        + row
    ) * block_rows + lax.broadcasted_iota(jnp.int32, (grid_rows // block_rows, block_rows), 1)
    point_ids = point_ids.reshape(1, grid_rows)

    own_ids = (
        (
            lax.broadcasted_iota(jnp.int32, (col_blocks, BLK), 0) * col_count + column
        )
        * BLK
        + lax.broadcasted_iota(jnp.int32, (col_blocks, BLK), 1)
    )[2 * panel_blocks :].reshape(-1)
    own_scaled = jnp.take(center_scaled, own_ids, axis=0)
    own_norms = jnp.take(center_norms, own_ids, axis=0)

    lead_ids = jnp.arange(PANEL, dtype=jnp.int32)
    k11 = kernel_block(
        center_scaled[:PANEL], center_norms[:PANEL], center_scaled[:PANEL], center_norms[:PANEL], signal
    ) + ridge_where(lead_ids, lead_ids, jitter)
    first_inverse = lower_inverse(k11)
    used_ids = jnp.concatenate([jnp.arange(PANEL, 2 * PANEL, dtype=jnp.int32), own_ids])
    used_scaled = jnp.concatenate([center_scaled[PANEL : 2 * PANEL], own_scaled])
    used_norms = jnp.concatenate([center_norms[PANEL : 2 * PANEL], own_norms])
    used_kernel = kernel_block(
        used_scaled, used_norms, center_scaled[: 2 * PANEL], center_norms[: 2 * PANEL], signal
    ) + ridge_where(used_ids, jnp.arange(2 * PANEL, dtype=jnp.int32), jitter)
    center_first = jnp.dot(
        used_kernel[:, :PANEL], first_inverse.T, precision=HIGHEST, preferred_element_type=jnp.float32
    ).astype(jnp.bfloat16)
    first_mid = center_first[:PANEL]
    center_second = used_kernel[:, PANEL:] - jnp.dot(
        center_first, first_mid.T, preferred_element_type=jnp.float32
    )
    second_inverse = lower_inverse(center_second[:PANEL])
    second_own = jnp.dot(
        center_second[PANEL:], second_inverse.T, precision=HIGHEST, preferred_element_type=jnp.float32
    ).astype(jnp.bfloat16)
    own_panels = jnp.concatenate([center_first[PANEL:], second_own], axis=1)

    select = jnp.where(
        lax.broadcasted_iota(jnp.int32, (BLK, PANEL), 1)
        == column * BLK + lax.broadcasted_iota(jnp.int32, (BLK, PANEL), 0),
        1.0,
        0.0,
    ).astype(jnp.bfloat16)
    consts = jnp.stack([signal, jitter])
    finished = panel_stage(
        consts,
        gathered,
        point_norms,
        point_ids,
        feature_scales.reshape(1, FEAT),
        pack_left(center_scaled[: 2 * PANEL]),
        center_norms[: 2 * PANEL].reshape(-1, 1),
        pack_left(own_scaled),
        own_norms.reshape(-1, 1),
        own_ids.reshape(-1, 1),
        first_inverse,
        second_inverse,
        first_mid,
        own_panels,
        select,
    )
    return finished.reshape(col_blocks, 1, BLK, 1, grid_rows)


def solution(mesh):
    placed = (P(("row", "col"), None), P(), P(), P())
    return jax.shard_map(
        on_device,
        mesh=mesh,
        in_specs=placed,
        out_specs=P(None, "col", None, "row", None),
        check_vma=False,
    )
```

```python
import jax
import jax.numpy as jnp
from jax import lax
from jax.sharding import PartitionSpec as P
from jax.experimental import pallas as pl
from jax.experimental.pallas import tpu as pltpu

FEAT = 64
SLAB = 1536
PANEL = 256
BLK = 16

HIGHEST = lax.Precision.HIGHEST
PHASES = 4


def kernel_block(left, left_norms, right, right_norms, signal):
    cross = jnp.dot(left, right.T, precision=HIGHEST, preferred_element_type=jnp.float32)
    return signal * jnp.exp(-0.5 * (left_norms[:, None] + right_norms[None, :] - 2.0 * cross))


def _nt(left, right):
    return lax.dot_general(
        left, right, (((1,), (1,)), ((), ())), precision=HIGHEST, preferred_element_type=jnp.float32
    )


def lower_inverse_kernel(a_ref, o_ref, s_ref, x_ref):
    half = a_ref.shape[0] // 2
    lane_row = lax.broadcasted_iota(jnp.int32, (1, half), 1)
    eye = jnp.where(
        lax.broadcasted_iota(jnp.int32, (half, half), 0)
        == lax.broadcasted_iota(jnp.int32, (half, half), 1),
        1.0,
        0.0,
    )

    def pick(values, index):
        return jnp.sum(jnp.where(lane_row == index, values, 0.0), axis=1, keepdims=True)

    def make_step(top):
        count = half - top
        lanes = lax.broadcasted_iota(jnp.int32, (count, half), 1)
        rows = lax.broadcasted_iota(jnp.int32, (count, 1), 0) + top

        def step(j, carry):
            k = 2 * j
            s = s_ref[top:, :]
            x = x_ref[top:, :]
            row0 = s_ref[pl.ds(k, 1), :]
            row1 = s_ref[pl.ds(k + 1, 1), :]
            col0 = jnp.sum(jnp.where(lanes == k, s, 0.0), axis=1, keepdims=True)
            col1 = jnp.sum(jnp.where(lanes == k + 1, s, 0.0), axis=1, keepdims=True)
            root0 = jnp.sqrt(pick(row0, k))
            cross = pick(row1, k) / root0
            root1 = jnp.sqrt(pick(row1, k + 1) - cross * cross)
            col0 = jnp.where(rows >= k, col0 / root0, 0.0)
            row0 = jnp.where(lane_row >= k, row0 / root0, 0.0)
            col1 = jnp.where(rows >= k + 1, (col1 - col0 * cross) / root1, 0.0)
            row1 = jnp.where(lane_row >= k + 1, (row1 - cross * row0) / root1, 0.0)
            s_ref[top:, :] = s - col0 * row0 - col1 * row1
            x0 = x_ref[pl.ds(k, 1), :] / root0
            x1 = (x_ref[pl.ds(k + 1, 1), :] - cross * x0) / root1
            rest = x - jnp.where(rows > k, col0, 0.0) * x0 - jnp.where(rows > k + 1, col1, 0.0) * x1
            x_ref[top:, :] = jnp.where(rows == k, x0, jnp.where(rows == k + 1, x1, rest))
            return carry

        return step

    def base(block):
        s_ref[...] = block
        x_ref[...] = eye.astype(jnp.float32)
        span = half // PHASES
        for phase in range(PHASES):
            lax.fori_loop(phase * span // 2, (phase + 1) * span // 2, make_step(phase * span), 0)
        return x_ref[...]

    first = base(a_ref[:half, :half])
    lower = _nt(a_ref[half:, :half], first)
    schur = a_ref[half:, half:] - _nt(lower, lower)
    second = base((schur + schur.T) * 0.5)
    below = -jnp.dot(
        second,
        jnp.dot(lower, first, precision=HIGHEST, preferred_element_type=jnp.float32),
        precision=HIGHEST,
        preferred_element_type=jnp.float32,
    )
    o_ref[:half, :half] = first
    o_ref[:half, half:] = jnp.zeros((half, half), jnp.float32)
    o_ref[half:, :half] = below
    o_ref[half:, half:] = second


def lower_inverse(block):
    size = block.shape[0]
    half = size // 2
    block = (block + block.T) * 0.5
    return pl.pallas_call(
        lower_inverse_kernel,
        out_shape=jax.ShapeDtypeStruct((size, size), jnp.float32),
        scratch_shapes=[pltpu.VMEM((half, half), jnp.float32), pltpu.VMEM((half, half), jnp.float32)],
    )(block)


def split_three(values):
    high = values.astype(jnp.bfloat16)
    rest = values - high.astype(jnp.float32)
    middle = rest.astype(jnp.bfloat16)
    low = (rest - middle.astype(jnp.float32)).astype(jnp.bfloat16)
    return high, middle, low


def pack_left(values):
    high = lax.reduce_precision(values, exponent_bits=8, mantissa_bits=7)
    rest = values - high
    middle = lax.reduce_precision(rest, exponent_bits=8, mantissa_bits=7)
    low = rest - middle
    high, middle, low = (piece.astype(jnp.bfloat16) for piece in (high, middle, low))
    return jnp.concatenate([high, high, middle, high, low, middle], axis=1)


def panel_kernel(
    consts_ref, pts_ref, pid_ref, scales_ref, cs_ref, cn_ref, own_cs_ref, own_cn_ref,
    own_ids_ref, finv_ref, sinv_ref, mid_ref, own_panels_ref, sel_ref, out_ref,
):
    signal = consts_ref[0]
    jitter = consts_ref[1]
    tile = pts_ref.shape[0] * pts_ref.shape[2]
    scaled = (pts_ref[...].reshape(tile, FEAT) * scales_ref[...]).T
    high, middle, low = split_three(scaled)
    packed = jnp.concatenate([high, middle, high, low, high, middle], axis=0)
    pnorm = jnp.sum(scaled * scaled, axis=0, keepdims=True)
    pid = pid_ref[...]
    cross = jnp.dot(cs_ref[...], packed, preferred_element_type=jnp.float32)
    values = signal * jnp.exp(-0.5 * (cn_ref[...] + pnorm - 2.0 * cross))
    lead = lax.broadcasted_iota(jnp.int32, values.shape, 0)
    values = values + jnp.where(lead == pid, jitter, jnp.float32(0.0))
    first = jnp.dot(
        finv_ref[...], values[:PANEL], precision=HIGHEST, preferred_element_type=jnp.float32
    ).astype(jnp.bfloat16)
    reduced = values[PANEL:] - jnp.dot(mid_ref[...], first, preferred_element_type=jnp.float32)
    second = jnp.dot(
        sinv_ref[...], reduced, precision=HIGHEST, preferred_element_type=jnp.float32
    ).astype(jnp.bfloat16)
    own_cross = jnp.dot(own_cs_ref[...], packed, preferred_element_type=jnp.float32)
    own = signal * jnp.exp(-0.5 * (own_cn_ref[...] + pnorm - 2.0 * own_cross))
    own = own + jnp.where(own_ids_ref[...] == pid, jitter, jnp.float32(0.0))
    both = jnp.concatenate([first, second], axis=0)
    trailing = own - jnp.dot(own_panels_ref[...], both, preferred_element_type=jnp.float32)
    sel = sel_ref[...]
    result = jnp.concatenate(
        [
            jnp.dot(sel, first, preferred_element_type=jnp.float32),
            jnp.dot(sel, second, preferred_element_type=jnp.float32),
            trailing,
        ],
        axis=0,
    )
    lanes = out_ref.shape[2]
    for chunk in range(out_ref.shape[1]):
        out_ref[:, chunk, :] = result[:, chunk * lanes : (chunk + 1) * lanes]


def panel_stage(consts, gathered, pid, scales, cs, cn, own_cs, own_cn, own_ids, finv, sinv, mid, own_panels, sel):
    col_count, row_count, block_rows, _ = gathered.shape
    tile = col_count * block_rows
    grid_rows = tile * row_count
    out_rows = 2 * BLK + own_cs.shape[0]

    def whole(array):
        return pl.BlockSpec(array.shape, lambda i: (0,) * array.ndim)

    return pl.pallas_call(
        panel_kernel,
        grid=(row_count,),
        in_specs=[
            pl.BlockSpec(memory_space=pltpu.SMEM),
            pl.BlockSpec((col_count, 1, block_rows, FEAT), lambda i: (0, i, 0, 0)),
            pl.BlockSpec((1, tile), lambda i: (0, i)),
        ]
        + [whole(a) for a in (scales, cs, cn, own_cs, own_cn, own_ids, finv, sinv, mid, own_panels, sel)],
        out_specs=pl.BlockSpec((out_rows, tile // 128, 128), lambda i: (0, i, 0)),
        out_shape=jax.ShapeDtypeStruct((out_rows, grid_rows // 128, 128), jnp.float32),
    )(consts, gathered, pid, scales, cs, cn, own_cs, own_cn, own_ids, finv, sinv, mid, own_panels, sel)


def ridge_where(row_ids, col_ids, jitter):
    return jnp.where(row_ids[:, None] == col_ids[None, :], jitter, jnp.float32(0.0))


def gather_by_all_to_all(piece, axis_name):
    count = lax.axis_size(axis_name)
    copies = jnp.broadcast_to(piece[None], (count,) + piece.shape)
    return lax.all_to_all(copies, axis_name, 0, 0, tiled=True)


def on_device(points, feature_scales, amplitude, ridge):
    row_count = lax.axis_size("row")
    col_count = lax.axis_size("col")
    row = lax.axis_index("row")
    column = lax.axis_index("col")
    rows_one = points.shape[0]
    block_rows = rows_one // row_count
    col_blocks = SLAB // (BLK * col_count)
    panel_blocks = PANEL // (BLK * col_count)
    center_sources = SLAB // rows_one
    signal = amplitude[0]
    jitter = ridge[0]

    blocks = points.reshape(row_count, block_rows, FEAT)
    moved = lax.all_to_all(blocks, "row", 0, 0, tiled=True)

    first_slot = gather_by_all_to_all(moved[0], "col")[:center_sources]
    center_grid = gather_by_all_to_all(first_slot, "row")
    centers = center_grid.transpose(1, 0, 2, 3).reshape(SLAB, FEAT)

    moved, centers = lax.optimization_barrier((moved, centers))
    gathered = lax.all_gather(moved, "col", axis=0, tiled=False)
    grid_rows = gathered.shape[0] * gathered.shape[1] * block_rows

    center_scaled = centers * feature_scales
    center_norms = jnp.sum(center_scaled * center_scaled, axis=1)

    point_ids = (
        lax.broadcasted_iota(jnp.int32, (grid_rows // block_rows, block_rows), 0) * row_count
        + row
    ) * block_rows + lax.broadcasted_iota(jnp.int32, (grid_rows // block_rows, block_rows), 1)
    point_ids = point_ids.reshape(1, grid_rows)

    own_ids = (
        (
            lax.broadcasted_iota(jnp.int32, (col_blocks, BLK), 0) * col_count + column
        )
        * BLK
        + lax.broadcasted_iota(jnp.int32, (col_blocks, BLK), 1)
    )[2 * panel_blocks :].reshape(-1)
    own_scaled = jnp.take(center_scaled, own_ids, axis=0)
    own_norms = jnp.take(center_norms, own_ids, axis=0)

    lead_ids = jnp.arange(PANEL, dtype=jnp.int32)
    k11 = kernel_block(
        center_scaled[:PANEL], center_norms[:PANEL], center_scaled[:PANEL], center_norms[:PANEL], signal
    ) + ridge_where(lead_ids, lead_ids, jitter)
    first_inverse = lower_inverse(k11)
    used_ids = jnp.concatenate([jnp.arange(PANEL, 2 * PANEL, dtype=jnp.int32), own_ids])
    used_scaled = jnp.concatenate([center_scaled[PANEL : 2 * PANEL], own_scaled])
    used_norms = jnp.concatenate([center_norms[PANEL : 2 * PANEL], own_norms])
    used_kernel = kernel_block(
        used_scaled, used_norms, center_scaled[: 2 * PANEL], center_norms[: 2 * PANEL], signal
    ) + ridge_where(used_ids, jnp.arange(2 * PANEL, dtype=jnp.int32), jitter)
    center_first = jnp.dot(
        used_kernel[:, :PANEL], first_inverse.T, precision=HIGHEST, preferred_element_type=jnp.float32
    ).astype(jnp.bfloat16)
    first_mid = center_first[:PANEL]
    center_second = used_kernel[:, PANEL:] - jnp.dot(
        center_first, first_mid.T, preferred_element_type=jnp.float32
    )
    second_inverse = lower_inverse(center_second[:PANEL])
    second_own = jnp.dot(
        center_second[PANEL:], second_inverse.T, precision=HIGHEST, preferred_element_type=jnp.float32
    ).astype(jnp.bfloat16)
    own_panels = jnp.concatenate([center_first[PANEL:], second_own], axis=1)

    select = jnp.where(
        lax.broadcasted_iota(jnp.int32, (BLK, PANEL), 1)
        == column * BLK + lax.broadcasted_iota(jnp.int32, (BLK, PANEL), 0),
        1.0,
        0.0,
    ).astype(jnp.bfloat16)
    consts = jnp.stack([signal, jitter])
    finished = panel_stage(
        consts,
        gathered,
        point_ids,
        feature_scales.reshape(1, FEAT),
        pack_left(center_scaled[: 2 * PANEL]),
        center_norms[: 2 * PANEL].reshape(-1, 1),
        pack_left(own_scaled),
        own_norms.reshape(-1, 1),
        own_ids.reshape(-1, 1),
        first_inverse,
        second_inverse,
        first_mid,
        own_panels,
        select,
    )
    return finished.reshape(col_blocks, 1, BLK, 1, grid_rows)


def solution(mesh):
    placed = (P(("row", "col"), None), P(), P(), P())
    return jax.shard_map(
        on_device,
        mesh=mesh,
        in_specs=placed,
        out_specs=P(None, "col", None, "row", None),
        check_vma=False,
    )
```

```python
import jax
import jax.numpy as jnp
from jax import lax
from jax.sharding import PartitionSpec as P
from jax.experimental import pallas as pl
from jax.experimental.pallas import tpu as pltpu

FEAT = 64
SLAB = 1536
PANEL = 256
BLK = 16

HIGHEST = lax.Precision.HIGHEST
PHASES = 4


def kernel_block(left, left_norms, right, right_norms, signal):
    cross = jnp.dot(left, right.T, precision=HIGHEST, preferred_element_type=jnp.float32)
    return signal * jnp.exp(-0.5 * (left_norms[:, None] + right_norms[None, :] - 2.0 * cross))


def _nt(left, right):
    return lax.dot_general(
        left, right, (((1,), (1,)), ((), ())), precision=HIGHEST, preferred_element_type=jnp.float32
    )


def lower_inverse_kernel(a_ref, o_ref, s_ref, x_ref):
    half = a_ref.shape[0] // 2
    lane_row = lax.broadcasted_iota(jnp.int32, (1, half), 1)
    eye = jnp.where(
        lax.broadcasted_iota(jnp.int32, (half, half), 0)
        == lax.broadcasted_iota(jnp.int32, (half, half), 1),
        1.0,
        0.0,
    )

    def pick(values, index):
        return jnp.sum(jnp.where(lane_row == index, values, 0.0), axis=1, keepdims=True)

    def make_step(top):
        count = half - top
        lanes = lax.broadcasted_iota(jnp.int32, (count, half), 1)
        rows = lax.broadcasted_iota(jnp.int32, (count, 1), 0) + top

        def step(j, carry):
            k = 2 * j
            s = s_ref[top:, :]
            x = x_ref[top:, :]
            row0 = s_ref[pl.ds(k, 1), :]
            row1 = s_ref[pl.ds(k + 1, 1), :]
            col0 = jnp.sum(jnp.where(lanes == k, s, 0.0), axis=1, keepdims=True)
            col1 = jnp.sum(jnp.where(lanes == k + 1, s, 0.0), axis=1, keepdims=True)
            root0 = jnp.sqrt(pick(row0, k))
            cross = pick(row1, k) / root0
            root1 = jnp.sqrt(pick(row1, k + 1) - cross * cross)
            col0 = jnp.where(rows >= k, col0 / root0, 0.0)
            row0 = jnp.where(lane_row >= k, row0 / root0, 0.0)
            col1 = jnp.where(rows >= k + 1, (col1 - col0 * cross) / root1, 0.0)
            row1 = jnp.where(lane_row >= k + 1, (row1 - cross * row0) / root1, 0.0)
            s_ref[top:, :] = s - col0 * row0 - col1 * row1
            x0 = x_ref[pl.ds(k, 1), :] / root0
            x1 = (x_ref[pl.ds(k + 1, 1), :] - cross * x0) / root1
            rest = x - jnp.where(rows > k, col0, 0.0) * x0 - jnp.where(rows > k + 1, col1, 0.0) * x1
            x_ref[top:, :] = jnp.where(rows == k, x0, jnp.where(rows == k + 1, x1, rest))
            return carry

        return step

    def base(block):
        s_ref[...] = block
        x_ref[...] = eye.astype(jnp.float32)
        span = half // PHASES
        for phase in range(PHASES):
            lax.fori_loop(phase * span // 2, (phase + 1) * span // 2, make_step(phase * span), 0)
        return x_ref[...]

    first = base(a_ref[:half, :half])
    lower = _nt(a_ref[half:, :half], first)
    schur = a_ref[half:, half:] - _nt(lower, lower)
    second = base((schur + schur.T) * 0.5)
    below = -jnp.dot(
        second,
        jnp.dot(lower, first, precision=HIGHEST, preferred_element_type=jnp.float32),
        precision=HIGHEST,
        preferred_element_type=jnp.float32,
    )
    o_ref[:half, :half] = first
    o_ref[:half, half:] = jnp.zeros((half, half), jnp.float32)
    o_ref[half:, :half] = below
    o_ref[half:, half:] = second


def lower_inverse(block):
    size = block.shape[0]
    half = size // 2
    block = (block + block.T) * 0.5
    return pl.pallas_call(
        lower_inverse_kernel,
        out_shape=jax.ShapeDtypeStruct((size, size), jnp.float32),
        scratch_shapes=[pltpu.VMEM((half, half), jnp.float32), pltpu.VMEM((half, half), jnp.float32)],
    )(block)


def split_three(values):
    high = values.astype(jnp.bfloat16)
    rest = values - high.astype(jnp.float32)
    middle = rest.astype(jnp.bfloat16)
    low = (rest - middle.astype(jnp.float32)).astype(jnp.bfloat16)
    return high, middle, low


def pack_left(values):
    high = lax.reduce_precision(values, exponent_bits=8, mantissa_bits=7)
    rest = values - high
    middle = lax.reduce_precision(rest, exponent_bits=8, mantissa_bits=7)
    low = rest - middle
    high, middle, low = (piece.astype(jnp.bfloat16) for piece in (high, middle, low))
    return jnp.concatenate([high, high, middle, high, low, middle], axis=1)


def panel_kernel(
    consts_ref, pts_ref, pid_ref, scales_ref, cs_ref, cn_ref, own_cs_ref, own_cn_ref,
    own_ids_ref, finv_ref, sinv_ref, mid_ref, own_panels_ref, sel_ref, out_ref,
):
    signal = consts_ref[0]
    jitter = consts_ref[1]
    tile = pts_ref.shape[0] * pts_ref.shape[2]
    scaled = (pts_ref[...].reshape(tile, FEAT) * scales_ref[...]).T
    high, middle, low = split_three(scaled)
    packed = jnp.concatenate([high, middle, high, low, high, middle], axis=0)
    pnorm = jnp.sum(scaled * scaled, axis=0, keepdims=True)
    pid = pid_ref[...]
    cross = jnp.dot(cs_ref[...], packed, preferred_element_type=jnp.float32)
    values = signal * jnp.exp(-0.5 * (cn_ref[...] + pnorm - 2.0 * cross))
    lead = lax.broadcasted_iota(jnp.int32, values.shape, 0)
    values = values + jnp.where(lead == pid, jitter, jnp.float32(0.0))
    first = jnp.dot(
        finv_ref[...], values[:PANEL], precision=HIGHEST, preferred_element_type=jnp.float32
    ).astype(jnp.bfloat16)
    reduced = values[PANEL:] - jnp.dot(mid_ref[...], first, preferred_element_type=jnp.float32)
    second = jnp.dot(
        sinv_ref[...], reduced, precision=HIGHEST, preferred_element_type=jnp.float32
    ).astype(jnp.bfloat16)
    own_cross = jnp.dot(own_cs_ref[...], packed, preferred_element_type=jnp.float32)
    own = signal * jnp.exp(-0.5 * (own_cn_ref[...] + pnorm - 2.0 * own_cross))
    own = own + jnp.where(own_ids_ref[...] == pid, jitter, jnp.float32(0.0))
    both = jnp.concatenate([first, second], axis=0)
    trailing = own - jnp.dot(own_panels_ref[...], both, preferred_element_type=jnp.float32)
    sel = sel_ref[...]
    result = jnp.concatenate(
        [
            jnp.dot(sel, first, preferred_element_type=jnp.float32),
            jnp.dot(sel, second, preferred_element_type=jnp.float32),
            trailing,
        ],
        axis=0,
    )
    lanes = out_ref.shape[2]
    for chunk in range(out_ref.shape[1]):
        out_ref[:, chunk, :] = result[:, chunk * lanes : (chunk + 1) * lanes]


def panel_stage(consts, gathered, pid, scales, cs, cn, own_cs, own_cn, own_ids, finv, sinv, mid, own_panels, sel):
    col_count, row_count, block_rows, _ = gathered.shape
    tile = col_count * block_rows
    grid_rows = tile * row_count
    out_rows = 2 * BLK + own_cs.shape[0]

    def whole(array):
        return pl.BlockSpec(array.shape, lambda i: (0,) * array.ndim)

    return pl.pallas_call(
        panel_kernel,
        grid=(row_count,),
        in_specs=[
            pl.BlockSpec(memory_space=pltpu.SMEM),
            pl.BlockSpec((col_count, 1, block_rows, FEAT), lambda i: (0, i, 0, 0)),
            pl.BlockSpec((1, tile), lambda i: (0, i)),
        ]
        + [whole(a) for a in (scales, cs, cn, own_cs, own_cn, own_ids, finv, sinv, mid, own_panels, sel)],
        out_specs=pl.BlockSpec((out_rows, tile // 128, 128), lambda i: (0, i, 0)),
        out_shape=jax.ShapeDtypeStruct((out_rows, grid_rows // 128, 128), jnp.float32),
    )(consts, gathered, pid, scales, cs, cn, own_cs, own_cn, own_ids, finv, sinv, mid, own_panels, sel)


def ridge_where(row_ids, col_ids, jitter):
    return jnp.where(row_ids[:, None] == col_ids[None, :], jitter, jnp.float32(0.0))


def gather_by_all_to_all(piece, axis_name):
    count = lax.axis_size(axis_name)
    copies = jnp.broadcast_to(piece[None], (count,) + piece.shape)
    return lax.all_to_all(copies, axis_name, 0, 0, tiled=True)


def on_device(points, feature_scales, amplitude, ridge):
    row_count = lax.axis_size("row")
    col_count = lax.axis_size("col")
    row = lax.axis_index("row")
    column = lax.axis_index("col")
    rows_one = points.shape[0]
    block_rows = rows_one // row_count
    col_blocks = SLAB // (BLK * col_count)
    panel_blocks = PANEL // (BLK * col_count)
    center_sources = SLAB // rows_one
    signal = amplitude[0]
    jitter = ridge[0]

    blocks = points.reshape(row_count, block_rows, FEAT)
    moved = lax.all_to_all(blocks, "row", 0, 0, tiled=True)

    first_slot = gather_by_all_to_all(moved[0], "col")[:center_sources]
    center_grid = gather_by_all_to_all(first_slot, "row")
    centers = center_grid.transpose(1, 0, 2, 3).reshape(SLAB, FEAT)

    moved, centers = lax.optimization_barrier((moved, centers))
    gathered = gather_by_all_to_all(moved, "col")
    grid_rows = gathered.shape[0] * gathered.shape[1] * block_rows

    center_scaled = centers * feature_scales
    center_norms = jnp.sum(center_scaled * center_scaled, axis=1)

    point_ids = (
        lax.broadcasted_iota(jnp.int32, (grid_rows // block_rows, block_rows), 0) * row_count
        + row
    ) * block_rows + lax.broadcasted_iota(jnp.int32, (grid_rows // block_rows, block_rows), 1)
    point_ids = point_ids.reshape(1, grid_rows)

    own_ids = (
        (
            lax.broadcasted_iota(jnp.int32, (col_blocks, BLK), 0) * col_count + column
        )
        * BLK
        + lax.broadcasted_iota(jnp.int32, (col_blocks, BLK), 1)
    )[2 * panel_blocks :].reshape(-1)
    own_scaled = jnp.take(center_scaled, own_ids, axis=0)
    own_norms = jnp.take(center_norms, own_ids, axis=0)

    lead_ids = jnp.arange(PANEL, dtype=jnp.int32)
    k11 = kernel_block(
        center_scaled[:PANEL], center_norms[:PANEL], center_scaled[:PANEL], center_norms[:PANEL], signal
    ) + ridge_where(lead_ids, lead_ids, jitter)
    first_inverse = lower_inverse(k11)
    used_ids = jnp.concatenate([jnp.arange(PANEL, 2 * PANEL, dtype=jnp.int32), own_ids])
    used_scaled = jnp.concatenate([center_scaled[PANEL : 2 * PANEL], own_scaled])
    used_norms = jnp.concatenate([center_norms[PANEL : 2 * PANEL], own_norms])
    used_kernel = kernel_block(
        used_scaled, used_norms, center_scaled[: 2 * PANEL], center_norms[: 2 * PANEL], signal
    ) + ridge_where(used_ids, jnp.arange(2 * PANEL, dtype=jnp.int32), jitter)
    center_first = jnp.dot(
        used_kernel[:, :PANEL], first_inverse.T, precision=HIGHEST, preferred_element_type=jnp.float32
    ).astype(jnp.bfloat16)
    first_mid = center_first[:PANEL]
    center_second = used_kernel[:, PANEL:] - jnp.dot(
        center_first, first_mid.T, preferred_element_type=jnp.float32
    )
    second_inverse = lower_inverse(center_second[:PANEL])
    second_own = jnp.dot(
        center_second[PANEL:], second_inverse.T, precision=HIGHEST, preferred_element_type=jnp.float32
    ).astype(jnp.bfloat16)
    own_panels = jnp.concatenate([center_first[PANEL:], second_own], axis=1)

    select = jnp.where(
        lax.broadcasted_iota(jnp.int32, (BLK, PANEL), 1)
        == column * BLK + lax.broadcasted_iota(jnp.int32, (BLK, PANEL), 0),
        1.0,
        0.0,
    ).astype(jnp.bfloat16)
    consts = jnp.stack([signal, jitter])
    finished = panel_stage(
        consts,
        gathered,
        point_ids,
        feature_scales.reshape(1, FEAT),
        pack_left(center_scaled[: 2 * PANEL]),
        center_norms[: 2 * PANEL].reshape(-1, 1),
        pack_left(own_scaled),
        own_norms.reshape(-1, 1),
        own_ids.reshape(-1, 1),
        first_inverse,
        second_inverse,
        first_mid,
        own_panels,
        select,
    )
    return finished.reshape(col_blocks, 1, BLK, 1, grid_rows)


def solution(mesh):
    placed = (P(("row", "col"), None), P(), P(), P())
    return jax.shard_map(
        on_device,
        mesh=mesh,
        in_specs=placed,
        out_specs=P(None, "col", None, "row", None),
        check_vma=False,
    )
```

```python
import jax
import jax.numpy as jnp
from jax import lax
from jax.sharding import PartitionSpec as P
from jax.experimental import pallas as pl
from jax.experimental.pallas import tpu as pltpu

FEAT = 64
SLAB = 1536
PANEL = 256
BLK = 16

HIGHEST = lax.Precision.HIGHEST
PHASES = 4


def kernel_block(left, left_norms, right, right_norms, signal):
    cross = jnp.dot(left, right.T, precision=HIGHEST, preferred_element_type=jnp.float32)
    return signal * jnp.exp(-0.5 * (left_norms[:, None] + right_norms[None, :] - 2.0 * cross))


def _nt(left, right):
    return lax.dot_general(
        left, right, (((1,), (1,)), ((), ())), precision=HIGHEST, preferred_element_type=jnp.float32
    )


def lower_inverse_body(block, s_ref, x_ref):
    half = block.shape[0] // 2
    lane_row = lax.broadcasted_iota(jnp.int32, (1, half), 1)
    eye = jnp.where(
        lax.broadcasted_iota(jnp.int32, (half, half), 0)
        == lax.broadcasted_iota(jnp.int32, (half, half), 1),
        1.0,
        0.0,
    )

    def pick(values, index):
        return jnp.sum(jnp.where(lane_row == index, values, 0.0), axis=1, keepdims=True)

    def make_step(top):
        count = half - top
        lanes = lax.broadcasted_iota(jnp.int32, (count, half), 1)
        rows = lax.broadcasted_iota(jnp.int32, (count, 1), 0) + top

        def step(j, carry):
            k = 2 * j
            s = s_ref[top:, :]
            x = x_ref[top:, :]
            row0 = s_ref[pl.ds(k, 1), :]
            row1 = s_ref[pl.ds(k + 1, 1), :]
            col0 = jnp.sum(jnp.where(lanes == k, s, 0.0), axis=1, keepdims=True)
            col1 = jnp.sum(jnp.where(lanes == k + 1, s, 0.0), axis=1, keepdims=True)
            root0 = jnp.sqrt(pick(row0, k))
            cross = pick(row1, k) / root0
            root1 = jnp.sqrt(pick(row1, k + 1) - cross * cross)
            col0 = jnp.where(rows >= k, col0 / root0, 0.0)
            row0 = jnp.where(lane_row >= k, row0 / root0, 0.0)
            col1 = jnp.where(rows >= k + 1, (col1 - col0 * cross) / root1, 0.0)
            row1 = jnp.where(lane_row >= k + 1, (row1 - cross * row0) / root1, 0.0)
            s_ref[top:, :] = s - col0 * row0 - col1 * row1
            x0 = x_ref[pl.ds(k, 1), :] / root0
            x1 = (x_ref[pl.ds(k + 1, 1), :] - cross * x0) / root1
            rest = x - jnp.where(rows > k, col0, 0.0) * x0 - jnp.where(rows > k + 1, col1, 0.0) * x1
            x_ref[top:, :] = jnp.where(rows == k, x0, jnp.where(rows == k + 1, x1, rest))
            return carry

        return step

    def base(block):
        s_ref[...] = block
        x_ref[...] = eye.astype(jnp.float32)
        span = half // PHASES
        for phase in range(PHASES):
            lax.fori_loop(phase * span // 2, (phase + 1) * span // 2, make_step(phase * span), 0)
        return x_ref[...]

    first = base(block[:half, :half])
    lower = _nt(block[half:, :half], first)
    schur = block[half:, half:] - _nt(lower, lower)
    second = base((schur + schur.T) * 0.5)
    below = -jnp.dot(
        second,
        jnp.dot(lower, first, precision=HIGHEST, preferred_element_type=jnp.float32),
        precision=HIGHEST,
        preferred_element_type=jnp.float32,
    )
    top = jnp.concatenate([first, jnp.zeros((half, half), jnp.float32)], axis=1)
    return jnp.concatenate([top, jnp.concatenate([below, second], axis=1)], axis=0)


def factor_kernel(lead_ref, used_ref, finv_ref, sinv_ref, mid_ref, own_ref, s_ref, x_ref):
    first_inverse = lower_inverse_body(lead_ref[...], s_ref, x_ref)
    finv_ref[...] = first_inverse
    used = used_ref[...]
    panel = first_inverse.shape[0]
    center_first = _nt(used[:, :panel], first_inverse).astype(jnp.bfloat16)
    first_mid = center_first[:panel]
    mid_ref[...] = first_mid
    center_second = used[:, panel:] - lax.dot_general(
        center_first, first_mid, (((1,), (1,)), ((), ())), preferred_element_type=jnp.float32
    )
    block = center_second[:panel]
    second_inverse = lower_inverse_body((block + block.T) * 0.5, s_ref, x_ref)
    sinv_ref[...] = second_inverse
    second_own = _nt(center_second[panel:], second_inverse).astype(jnp.bfloat16)
    own_ref[...] = jnp.concatenate([center_first[panel:], second_own], axis=1)


def factor_centers(lead, used):
    panel = lead.shape[0]
    half = panel // 2
    own_rows = used.shape[0] - panel
    return pl.pallas_call(
        factor_kernel,
        out_shape=(
            jax.ShapeDtypeStruct((panel, panel), jnp.float32),
            jax.ShapeDtypeStruct((panel, panel), jnp.float32),
            jax.ShapeDtypeStruct((panel, panel), jnp.bfloat16),
            jax.ShapeDtypeStruct((own_rows, 2 * panel), jnp.bfloat16),
        ),
        scratch_shapes=[pltpu.VMEM((half, half), jnp.float32), pltpu.VMEM((half, half), jnp.float32)],
    )((lead + lead.T) * 0.5, used)


def split_three(values):
    high = values.astype(jnp.bfloat16)
    rest = values - high.astype(jnp.float32)
    middle = rest.astype(jnp.bfloat16)
    low = (rest - middle.astype(jnp.float32)).astype(jnp.bfloat16)
    return high, middle, low


def pack_left(values):
    high = lax.reduce_precision(values, exponent_bits=8, mantissa_bits=7)
    rest = values - high
    middle = lax.reduce_precision(rest, exponent_bits=8, mantissa_bits=7)
    low = rest - middle
    high, middle, low = (piece.astype(jnp.bfloat16) for piece in (high, middle, low))
    return jnp.concatenate([high, high, middle, high, low, middle], axis=1)


def panel_kernel(
    consts_ref, pts_ref, pid_ref, scales_ref, cs_ref, cn_ref, own_cs_ref, own_cn_ref,
    own_ids_ref, finv_ref, sinv_ref, mid_ref, own_panels_ref, sel_ref, out_ref,
):
    signal = consts_ref[0]
    jitter = consts_ref[1]
    tile = pts_ref.shape[0] * pts_ref.shape[2]
    scaled = (pts_ref[...].reshape(tile, FEAT) * scales_ref[...]).T
    high, middle, low = split_three(scaled)
    packed = jnp.concatenate([high, middle, high, low, high, middle], axis=0)
    pnorm = jnp.sum(scaled * scaled, axis=0, keepdims=True)
    pid = pid_ref[...]
    cross = jnp.dot(cs_ref[...], packed, preferred_element_type=jnp.float32)
    values = signal * jnp.exp(-0.5 * (cn_ref[...] + pnorm - 2.0 * cross))
    lead = lax.broadcasted_iota(jnp.int32, values.shape, 0)
    values = values + jnp.where(lead == pid, jitter, jnp.float32(0.0))
    first = jnp.dot(
        finv_ref[...], values[:PANEL], precision=HIGHEST, preferred_element_type=jnp.float32
    ).astype(jnp.bfloat16)
    reduced = values[PANEL:] - jnp.dot(mid_ref[...], first, preferred_element_type=jnp.float32)
    second = jnp.dot(
        sinv_ref[...], reduced, precision=HIGHEST, preferred_element_type=jnp.float32
    ).astype(jnp.bfloat16)
    own_cross = jnp.dot(own_cs_ref[...], packed, preferred_element_type=jnp.float32)
    own = signal * jnp.exp(-0.5 * (own_cn_ref[...] + pnorm - 2.0 * own_cross))
    own = own + jnp.where(own_ids_ref[...] == pid, jitter, jnp.float32(0.0))
    both = jnp.concatenate([first, second], axis=0)
    trailing = own - jnp.dot(own_panels_ref[...], both, preferred_element_type=jnp.float32)
    sel = sel_ref[...]
    result = jnp.concatenate(
        [
            jnp.dot(sel, first, preferred_element_type=jnp.float32),
            jnp.dot(sel, second, preferred_element_type=jnp.float32),
            trailing,
        ],
        axis=0,
    )
    lanes = out_ref.shape[2]
    for chunk in range(out_ref.shape[1]):
        out_ref[:, chunk, :] = result[:, chunk * lanes : (chunk + 1) * lanes]


def panel_stage(consts, gathered, pid, scales, cs, cn, own_cs, own_cn, own_ids, finv, sinv, mid, own_panels, sel):
    col_count, row_count, block_rows, _ = gathered.shape
    tile = col_count * block_rows
    grid_rows = tile * row_count
    out_rows = 2 * BLK + own_cs.shape[0]

    def whole(array):
        return pl.BlockSpec(array.shape, lambda i: (0,) * array.ndim)

    return pl.pallas_call(
        panel_kernel,
        grid=(row_count,),
        in_specs=[
            pl.BlockSpec(memory_space=pltpu.SMEM),
            pl.BlockSpec((col_count, 1, block_rows, FEAT), lambda i: (0, i, 0, 0)),
            pl.BlockSpec((1, tile), lambda i: (0, i)),
        ]
        + [whole(a) for a in (scales, cs, cn, own_cs, own_cn, own_ids, finv, sinv, mid, own_panels, sel)],
        out_specs=pl.BlockSpec((out_rows, tile // 128, 128), lambda i: (0, i, 0)),
        out_shape=jax.ShapeDtypeStruct((out_rows, grid_rows // 128, 128), jnp.float32),
    )(consts, gathered, pid, scales, cs, cn, own_cs, own_cn, own_ids, finv, sinv, mid, own_panels, sel)


def ridge_where(row_ids, col_ids, jitter):
    return jnp.where(row_ids[:, None] == col_ids[None, :], jitter, jnp.float32(0.0))


def gather_by_all_to_all(piece, axis_name):
    count = lax.axis_size(axis_name)
    copies = jnp.broadcast_to(piece[None], (count,) + piece.shape)
    return lax.all_to_all(copies, axis_name, 0, 0, tiled=True)


def on_device(points, feature_scales, amplitude, ridge):
    row_count = lax.axis_size("row")
    col_count = lax.axis_size("col")
    row = lax.axis_index("row")
    column = lax.axis_index("col")
    rows_one = points.shape[0]
    block_rows = rows_one // row_count
    col_blocks = SLAB // (BLK * col_count)
    panel_blocks = PANEL // (BLK * col_count)
    center_sources = SLAB // rows_one
    signal = amplitude[0]
    jitter = ridge[0]

    blocks = points.reshape(row_count, block_rows, FEAT)
    moved = lax.all_to_all(blocks, "row", 0, 0, tiled=True)

    first_slot = gather_by_all_to_all(moved[0], "col")[:center_sources]
    center_grid = gather_by_all_to_all(first_slot, "row")
    centers = center_grid.transpose(1, 0, 2, 3).reshape(SLAB, FEAT)

    moved, centers = lax.optimization_barrier((moved, centers))
    gathered = lax.all_gather(moved, "col", axis=0, tiled=False)
    grid_rows = gathered.shape[0] * gathered.shape[1] * block_rows

    center_scaled = centers * feature_scales
    center_norms = jnp.sum(center_scaled * center_scaled, axis=1)

    point_ids = (
        lax.broadcasted_iota(jnp.int32, (grid_rows // block_rows, block_rows), 0) * row_count
        + row
    ) * block_rows + lax.broadcasted_iota(jnp.int32, (grid_rows // block_rows, block_rows), 1)
    point_ids = point_ids.reshape(1, grid_rows)

    own_ids = (
        (
            lax.broadcasted_iota(jnp.int32, (col_blocks, BLK), 0) * col_count + column
        )
        * BLK
        + lax.broadcasted_iota(jnp.int32, (col_blocks, BLK), 1)
    )[2 * panel_blocks :].reshape(-1)
    own_scaled = jnp.take(center_scaled, own_ids, axis=0)
    own_norms = jnp.take(center_norms, own_ids, axis=0)

    lead_ids = jnp.arange(PANEL, dtype=jnp.int32)
    k11 = kernel_block(
        center_scaled[:PANEL], center_norms[:PANEL], center_scaled[:PANEL], center_norms[:PANEL], signal
    ) + ridge_where(lead_ids, lead_ids, jitter)
    used_ids = jnp.concatenate([jnp.arange(PANEL, 2 * PANEL, dtype=jnp.int32), own_ids])
    used_scaled = jnp.concatenate([center_scaled[PANEL : 2 * PANEL], own_scaled])
    used_norms = jnp.concatenate([center_norms[PANEL : 2 * PANEL], own_norms])
    used_kernel = kernel_block(
        used_scaled, used_norms, center_scaled[: 2 * PANEL], center_norms[: 2 * PANEL], signal
    ) + ridge_where(used_ids, jnp.arange(2 * PANEL, dtype=jnp.int32), jitter)
    first_inverse, second_inverse, first_mid, own_panels = factor_centers(k11, used_kernel)

    select = jnp.where(
        lax.broadcasted_iota(jnp.int32, (BLK, PANEL), 1)
        == column * BLK + lax.broadcasted_iota(jnp.int32, (BLK, PANEL), 0),
        1.0,
        0.0,
    ).astype(jnp.bfloat16)
    consts = jnp.stack([signal, jitter])
    finished = panel_stage(
        consts,
        gathered,
        point_ids,
        feature_scales.reshape(1, FEAT),
        pack_left(center_scaled[: 2 * PANEL]),
        center_norms[: 2 * PANEL].reshape(-1, 1),
        pack_left(own_scaled),
        own_norms.reshape(-1, 1),
        own_ids.reshape(-1, 1),
        first_inverse,
        second_inverse,
        first_mid,
        own_panels,
        select,
    )
    return finished.reshape(col_blocks, 1, BLK, 1, grid_rows)


def solution(mesh):
    placed = (P(("row", "col"), None), P(), P(), P())
    return jax.shard_map(
        on_device,
        mesh=mesh,
        in_specs=placed,
        out_specs=P(None, "col", None, "row", None),
        check_vma=False,
    )
```

```python
import jax
import jax.numpy as jnp
from jax import lax
from jax.sharding import PartitionSpec as P
from jax.experimental import pallas as pl
from jax.experimental.pallas import tpu as pltpu

FEAT = 64
SLAB = 1536
PANEL = 256
BLK = 16

HIGHEST = lax.Precision.HIGHEST
PHASES = 8


def kernel_block(left, left_norms, right, right_norms, signal):
    cross = jnp.dot(left, right.T, precision=HIGHEST, preferred_element_type=jnp.float32)
    return signal * jnp.exp(-0.5 * (left_norms[:, None] + right_norms[None, :] - 2.0 * cross))


def _nt(left, right):
    return lax.dot_general(
        left, right, (((1,), (1,)), ((), ())), precision=HIGHEST, preferred_element_type=jnp.float32
    )


def lower_inverse_body(block, s_ref, x_ref):
    half = block.shape[0] // 2
    lane_row = lax.broadcasted_iota(jnp.int32, (1, half), 1)
    eye = jnp.where(
        lax.broadcasted_iota(jnp.int32, (half, half), 0)
        == lax.broadcasted_iota(jnp.int32, (half, half), 1),
        1.0,
        0.0,
    )

    def pick(values, index):
        return jnp.sum(jnp.where(lane_row == index, values, 0.0), axis=1, keepdims=True)

    def make_step(top):
        count = half - top
        lanes = lax.broadcasted_iota(jnp.int32, (count, half), 1)
        rows = lax.broadcasted_iota(jnp.int32, (count, 1), 0) + top

        def step(j, carry):
            k = 2 * j
            s = s_ref[top:, :]
            x = x_ref[top:, :]
            row0 = s_ref[pl.ds(k, 1), :]
            row1 = s_ref[pl.ds(k + 1, 1), :]
            col0 = jnp.sum(jnp.where(lanes == k, s, 0.0), axis=1, keepdims=True)
            col1 = jnp.sum(jnp.where(lanes == k + 1, s, 0.0), axis=1, keepdims=True)
            root0 = jnp.sqrt(pick(row0, k))
            cross = pick(row1, k) / root0
            root1 = jnp.sqrt(pick(row1, k + 1) - cross * cross)
            col0 = jnp.where(rows >= k, col0 / root0, 0.0)
            row0 = jnp.where(lane_row >= k, row0 / root0, 0.0)
            col1 = jnp.where(rows >= k + 1, (col1 - col0 * cross) / root1, 0.0)
            row1 = jnp.where(lane_row >= k + 1, (row1 - cross * row0) / root1, 0.0)
            s_ref[top:, :] = s - col0 * row0 - col1 * row1
            x0 = x_ref[pl.ds(k, 1), :] / root0
            x1 = (x_ref[pl.ds(k + 1, 1), :] - cross * x0) / root1
            rest = x - jnp.where(rows > k, col0, 0.0) * x0 - jnp.where(rows > k + 1, col1, 0.0) * x1
            x_ref[top:, :] = jnp.where(rows == k, x0, jnp.where(rows == k + 1, x1, rest))
            return carry

        return step

    def base(block):
        s_ref[...] = block
        x_ref[...] = eye.astype(jnp.float32)
        span = half // PHASES
        for phase in range(PHASES):
            lax.fori_loop(phase * span // 2, (phase + 1) * span // 2, make_step(phase * span), 0)
        return x_ref[...]

    first = base(block[:half, :half])
    lower = _nt(block[half:, :half], first)
    schur = block[half:, half:] - _nt(lower, lower)
    second = base((schur + schur.T) * 0.5)
    below = -jnp.dot(
        second,
        jnp.dot(lower, first, precision=HIGHEST, preferred_element_type=jnp.float32),
        precision=HIGHEST,
        preferred_element_type=jnp.float32,
    )
    top = jnp.concatenate([first, jnp.zeros((half, half), jnp.float32)], axis=1)
    return jnp.concatenate([top, jnp.concatenate([below, second], axis=1)], axis=0)


def factor_kernel(lead_ref, used_ref, finv_ref, sinv_ref, mid_ref, own_ref, s_ref, x_ref):
    first_inverse = lower_inverse_body(lead_ref[...], s_ref, x_ref)
    finv_ref[...] = first_inverse
    used = used_ref[...]
    panel = first_inverse.shape[0]
    center_first = _nt(used[:, :panel], first_inverse).astype(jnp.bfloat16)
    first_mid = center_first[:panel]
    mid_ref[...] = first_mid
    center_second = used[:, panel:] - lax.dot_general(
        center_first, first_mid, (((1,), (1,)), ((), ())), preferred_element_type=jnp.float32
    )
    block = center_second[:panel]
    second_inverse = lower_inverse_body((block + block.T) * 0.5, s_ref, x_ref)
    sinv_ref[...] = second_inverse
    second_own = _nt(center_second[panel:], second_inverse).astype(jnp.bfloat16)
    own_ref[...] = jnp.concatenate([center_first[panel:], second_own], axis=1)


def factor_centers(lead, used):
    panel = lead.shape[0]
    half = panel // 2
    own_rows = used.shape[0] - panel
    return pl.pallas_call(
        factor_kernel,
        out_shape=(
            jax.ShapeDtypeStruct((panel, panel), jnp.float32),
            jax.ShapeDtypeStruct((panel, panel), jnp.float32),
            jax.ShapeDtypeStruct((panel, panel), jnp.bfloat16),
            jax.ShapeDtypeStruct((own_rows, 2 * panel), jnp.bfloat16),
        ),
        scratch_shapes=[pltpu.VMEM((half, half), jnp.float32), pltpu.VMEM((half, half), jnp.float32)],
    )((lead + lead.T) * 0.5, used)


def split_three(values):
    high = values.astype(jnp.bfloat16)
    rest = values - high.astype(jnp.float32)
    middle = rest.astype(jnp.bfloat16)
    low = (rest - middle.astype(jnp.float32)).astype(jnp.bfloat16)
    return high, middle, low


def pack_left(values):
    high = lax.reduce_precision(values, exponent_bits=8, mantissa_bits=7)
    rest = values - high
    middle = lax.reduce_precision(rest, exponent_bits=8, mantissa_bits=7)
    low = rest - middle
    high, middle, low = (piece.astype(jnp.bfloat16) for piece in (high, middle, low))
    return jnp.concatenate([high, high, middle, high, low, middle], axis=1)


def panel_kernel(
    consts_ref, pts_ref, pid_ref, scales_ref, cs_ref, cn_ref, own_cs_ref, own_cn_ref,
    own_ids_ref, finv_ref, sinv_ref, mid_ref, own_panels_ref, sel_ref, out_ref,
):
    signal = consts_ref[0]
    jitter = consts_ref[1]
    tile = pts_ref.shape[0] * pts_ref.shape[2]
    scaled = (pts_ref[...].reshape(tile, FEAT) * scales_ref[...]).T
    high, middle, low = split_three(scaled)
    packed = jnp.concatenate([high, middle, high, low, high, middle], axis=0)
    pnorm = jnp.sum(scaled * scaled, axis=0, keepdims=True)
    pid = pid_ref[...]
    cross = jnp.dot(cs_ref[...], packed, preferred_element_type=jnp.float32)
    values = signal * jnp.exp(-0.5 * (cn_ref[...] + pnorm - 2.0 * cross))
    head = values[:, :128] + jnp.where(
        lax.broadcasted_iota(jnp.int32, (values.shape[0], 128), 0) == pid[:, :128], jitter, jnp.float32(0.0)
    )
    values = jnp.concatenate([head, values[:, 128:]], axis=1)
    first = jnp.dot(
        finv_ref[...], values[:PANEL], precision=HIGHEST, preferred_element_type=jnp.float32
    ).astype(jnp.bfloat16)
    reduced = values[PANEL:] - jnp.dot(mid_ref[...], first, preferred_element_type=jnp.float32)
    second = jnp.dot(
        sinv_ref[...], reduced, precision=HIGHEST, preferred_element_type=jnp.float32
    ).astype(jnp.bfloat16)
    own_cross = jnp.dot(own_cs_ref[...], packed, preferred_element_type=jnp.float32)
    own = signal * jnp.exp(-0.5 * (own_cn_ref[...] + pnorm - 2.0 * own_cross))
    own_head = own[:, :256] + jnp.where(own_ids_ref[...] == pid[:, :256], jitter, jnp.float32(0.0))
    own = jnp.concatenate([own_head, own[:, 256:]], axis=1)
    both = jnp.concatenate([first, second], axis=0)
    trailing = own - jnp.dot(own_panels_ref[...], both, preferred_element_type=jnp.float32)
    sel = sel_ref[...]
    result = jnp.concatenate(
        [
            jnp.dot(sel, first, preferred_element_type=jnp.float32),
            jnp.dot(sel, second, preferred_element_type=jnp.float32),
            trailing,
        ],
        axis=0,
    )
    lanes = out_ref.shape[2]
    for chunk in range(out_ref.shape[1]):
        out_ref[:, chunk, :] = result[:, chunk * lanes : (chunk + 1) * lanes]


def panel_stage(consts, gathered, pid, scales, cs, cn, own_cs, own_cn, own_ids, finv, sinv, mid, own_panels, sel):
    col_count, row_count, block_rows, _ = gathered.shape
    tile = col_count * block_rows
    grid_rows = tile * row_count
    out_rows = 2 * BLK + own_cs.shape[0]

    def whole(array):
        return pl.BlockSpec(array.shape, lambda i: (0,) * array.ndim)

    return pl.pallas_call(
        panel_kernel,
        grid=(row_count,),
        in_specs=[
            pl.BlockSpec(memory_space=pltpu.SMEM),
            pl.BlockSpec((col_count, 1, block_rows, FEAT), lambda i: (0, i, 0, 0)),
            pl.BlockSpec((1, tile), lambda i: (0, i)),
        ]
        + [whole(a) for a in (scales, cs, cn, own_cs, own_cn, own_ids, finv, sinv, mid, own_panels, sel)],
        out_specs=pl.BlockSpec((out_rows, tile // 128, 128), lambda i: (0, i, 0)),
        out_shape=jax.ShapeDtypeStruct((out_rows, grid_rows // 128, 128), jnp.float32),
    )(consts, gathered, pid, scales, cs, cn, own_cs, own_cn, own_ids, finv, sinv, mid, own_panels, sel)


def ridge_where(row_ids, col_ids, jitter):
    return jnp.where(row_ids[:, None] == col_ids[None, :], jitter, jnp.float32(0.0))


def gather_by_all_to_all(piece, axis_name):
    count = lax.axis_size(axis_name)
    copies = jnp.broadcast_to(piece[None], (count,) + piece.shape)
    return lax.all_to_all(copies, axis_name, 0, 0, tiled=True)


def on_device(points, feature_scales, amplitude, ridge):
    row_count = lax.axis_size("row")
    col_count = lax.axis_size("col")
    row = lax.axis_index("row")
    column = lax.axis_index("col")
    rows_one = points.shape[0]
    block_rows = rows_one // row_count
    col_blocks = SLAB // (BLK * col_count)
    panel_blocks = PANEL // (BLK * col_count)
    center_sources = SLAB // rows_one
    signal = amplitude[0]
    jitter = ridge[0]

    blocks = points.reshape(row_count, block_rows, FEAT)
    moved = lax.all_to_all(blocks, "row", 0, 0, tiled=True)

    first_slot = gather_by_all_to_all(moved[0], "col")[:center_sources]
    center_grid = gather_by_all_to_all(first_slot, "row")
    centers = center_grid.transpose(1, 0, 2, 3).reshape(SLAB, FEAT)

    moved, centers = lax.optimization_barrier((moved, centers))
    gathered = lax.all_gather(moved, "col", axis=0, tiled=False)
    grid_rows = gathered.shape[0] * gathered.shape[1] * block_rows

    center_scaled = centers * feature_scales
    center_norms = jnp.sum(center_scaled * center_scaled, axis=1)

    point_ids = (
        lax.broadcasted_iota(jnp.int32, (grid_rows // block_rows, block_rows), 0) * row_count
        + row
    ) * block_rows + lax.broadcasted_iota(jnp.int32, (grid_rows // block_rows, block_rows), 1)
    point_ids = point_ids.reshape(1, grid_rows)

    own_ids = (
        (
            lax.broadcasted_iota(jnp.int32, (col_blocks, BLK), 0) * col_count + column
        )
        * BLK
        + lax.broadcasted_iota(jnp.int32, (col_blocks, BLK), 1)
    )[2 * panel_blocks :].reshape(-1)
    own_scaled = jnp.take(center_scaled, own_ids, axis=0)
    own_norms = jnp.take(center_norms, own_ids, axis=0)

    lead_ids = jnp.arange(PANEL, dtype=jnp.int32)
    k11 = kernel_block(
        center_scaled[:PANEL], center_norms[:PANEL], center_scaled[:PANEL], center_norms[:PANEL], signal
    ) + ridge_where(lead_ids, lead_ids, jitter)
    used_ids = jnp.concatenate([jnp.arange(PANEL, 2 * PANEL, dtype=jnp.int32), own_ids])
    used_scaled = jnp.concatenate([center_scaled[PANEL : 2 * PANEL], own_scaled])
    used_norms = jnp.concatenate([center_norms[PANEL : 2 * PANEL], own_norms])
    used_kernel = kernel_block(
        used_scaled, used_norms, center_scaled[: 2 * PANEL], center_norms[: 2 * PANEL], signal
    ) + ridge_where(used_ids, jnp.arange(2 * PANEL, dtype=jnp.int32), jitter)
    first_inverse, second_inverse, first_mid, own_panels = factor_centers(k11, used_kernel)

    select = jnp.where(
        lax.broadcasted_iota(jnp.int32, (BLK, PANEL), 1)
        == column * BLK + lax.broadcasted_iota(jnp.int32, (BLK, PANEL), 0),
        1.0,
        0.0,
    ).astype(jnp.bfloat16)
    consts = jnp.stack([signal, jitter])
    finished = panel_stage(
        consts,
        gathered,
        point_ids,
        feature_scales.reshape(1, FEAT),
        pack_left(center_scaled[: 2 * PANEL]),
        center_norms[: 2 * PANEL].reshape(-1, 1),
        pack_left(own_scaled),
        own_norms.reshape(-1, 1),
        own_ids.reshape(-1, 1),
        first_inverse,
        second_inverse,
        first_mid,
        own_panels,
        select,
    )
    return finished.reshape(col_blocks, 1, BLK, 1, grid_rows)


def solution(mesh):
    placed = (P(("row", "col"), None), P(), P(), P())
    return jax.shard_map(
        on_device,
        mesh=mesh,
        in_specs=placed,
        out_specs=P(None, "col", None, "row", None),
        check_vma=False,
    )
```

```python
import jax
import jax.numpy as jnp
from jax import lax
from jax.sharding import PartitionSpec as P
from jax.experimental import pallas as pl
from jax.experimental.pallas import tpu as pltpu

FEAT = 64
SLAB = 1536
PANEL = 256
BLK = 16

HIGHEST = lax.Precision.HIGHEST
PHASES = 8


def kernel_block(left, left_norms, right, right_norms, signal):
    cross = jnp.dot(left, right.T, precision=HIGHEST, preferred_element_type=jnp.float32)
    return signal * jnp.exp(-0.5 * (left_norms[:, None] + right_norms[None, :] - 2.0 * cross))


def _nt(left, right):
    return lax.dot_general(
        left, right, (((1,), (1,)), ((), ())), precision=HIGHEST, preferred_element_type=jnp.float32
    )


def lower_inverse_body(block, s_ref, x_ref):
    half = block.shape[0] // 2
    lane_row = lax.broadcasted_iota(jnp.int32, (1, half), 1)
    eye = jnp.where(
        lax.broadcasted_iota(jnp.int32, (half, half), 0)
        == lax.broadcasted_iota(jnp.int32, (half, half), 1),
        1.0,
        0.0,
    )

    def pick(values, index):
        return jnp.sum(jnp.where(lane_row == index, values, 0.0), axis=1, keepdims=True)

    def make_step(top):
        count = half - top
        lanes = lax.broadcasted_iota(jnp.int32, (count, half), 1)
        rows = lax.broadcasted_iota(jnp.int32, (count, 1), 0) + top

        def step(j, carry):
            k = 2 * j
            s = s_ref[top:, :]
            x = x_ref[top:, :]
            row0 = s_ref[pl.ds(k, 1), :]
            row1 = s_ref[pl.ds(k + 1, 1), :]
            col0 = jnp.sum(jnp.where(lanes == k, s, 0.0), axis=1, keepdims=True)
            col1 = jnp.sum(jnp.where(lanes == k + 1, s, 0.0), axis=1, keepdims=True)
            root0 = jnp.sqrt(pick(row0, k))
            cross = pick(row1, k) / root0
            root1 = jnp.sqrt(pick(row1, k + 1) - cross * cross)
            col0 = jnp.where(rows >= k, col0 / root0, 0.0)
            row0 = jnp.where(lane_row >= k, row0 / root0, 0.0)
            col1 = jnp.where(rows >= k + 1, (col1 - col0 * cross) / root1, 0.0)
            row1 = jnp.where(lane_row >= k + 1, (row1 - cross * row0) / root1, 0.0)
            s_ref[top:, :] = s - col0 * row0 - col1 * row1
            x0 = x_ref[pl.ds(k, 1), :] / root0
            x1 = (x_ref[pl.ds(k + 1, 1), :] - cross * x0) / root1
            rest = x - jnp.where(rows > k, col0, 0.0) * x0 - jnp.where(rows > k + 1, col1, 0.0) * x1
            x_ref[top:, :] = jnp.where(rows == k, x0, jnp.where(rows == k + 1, x1, rest))
            return carry

        return step

    def base(block):
        s_ref[...] = block
        x_ref[...] = eye.astype(jnp.float32)
        span = half // PHASES
        for phase in range(PHASES):
            lax.fori_loop(phase * span // 2, (phase + 1) * span // 2, make_step(phase * span), 0)
        return x_ref[...]

    first = base(block[:half, :half])
    lower = _nt(block[half:, :half], first)
    schur = block[half:, half:] - _nt(lower, lower)
    second = base((schur + schur.T) * 0.5)
    below = -jnp.dot(
        second,
        jnp.dot(lower, first, precision=HIGHEST, preferred_element_type=jnp.float32),
        precision=HIGHEST,
        preferred_element_type=jnp.float32,
    )
    top = jnp.concatenate([first, jnp.zeros((half, half), jnp.float32)], axis=1)
    return jnp.concatenate([top, jnp.concatenate([below, second], axis=1)], axis=0)


def factor_kernel(lead_ref, used_ref, finv_ref, sinv_ref, mid_ref, own_ref, s_ref, x_ref):
    first_inverse = lower_inverse_body(lead_ref[...], s_ref, x_ref)
    finv_ref[...] = first_inverse
    used = used_ref[...]
    panel = first_inverse.shape[0]
    center_first = _nt(used[:, :panel], first_inverse).astype(jnp.bfloat16)
    first_mid = center_first[:panel]
    mid_ref[...] = first_mid
    center_second = used[:, panel:] - lax.dot_general(
        center_first, first_mid, (((1,), (1,)), ((), ())), preferred_element_type=jnp.float32
    )
    block = center_second[:panel]
    second_inverse = lower_inverse_body((block + block.T) * 0.5, s_ref, x_ref)
    sinv_ref[...] = second_inverse
    second_own = _nt(center_second[panel:], second_inverse).astype(jnp.bfloat16)
    own_ref[...] = jnp.concatenate([center_first[panel:], second_own], axis=1)


def factor_centers(lead, used):
    panel = lead.shape[0]
    half = panel // 2
    own_rows = used.shape[0] - panel
    return pl.pallas_call(
        factor_kernel,
        out_shape=(
            jax.ShapeDtypeStruct((panel, panel), jnp.float32),
            jax.ShapeDtypeStruct((panel, panel), jnp.float32),
            jax.ShapeDtypeStruct((panel, panel), jnp.bfloat16),
            jax.ShapeDtypeStruct((own_rows, 2 * panel), jnp.bfloat16),
        ),
        scratch_shapes=[pltpu.VMEM((half, half), jnp.float32), pltpu.VMEM((half, half), jnp.float32)],
    )((lead + lead.T) * 0.5, used)


def split_three(values):
    high = values.astype(jnp.bfloat16)
    rest = values - high.astype(jnp.float32)
    middle = rest.astype(jnp.bfloat16)
    low = (rest - middle.astype(jnp.float32)).astype(jnp.bfloat16)
    return high, middle, low


def pack_left(values):
    high = lax.reduce_precision(values, exponent_bits=8, mantissa_bits=7)
    rest = values - high
    middle = lax.reduce_precision(rest, exponent_bits=8, mantissa_bits=7)
    low = rest - middle
    high, middle, low = (piece.astype(jnp.bfloat16) for piece in (high, middle, low))
    return jnp.concatenate([high, high, middle, high, low, middle], axis=1)


def panel_kernel(
    consts_ref, pts_ref, pid_ref, scales_ref, cs_ref, cn_ref, own_cs_ref, own_cn_ref,
    own_ids_ref, finv_ref, sinv_ref, mid_ref, own_panels_ref, sel_ref, out_ref,
):
    signal = consts_ref[0]
    jitter = consts_ref[1]
    tile = pts_ref.shape[0] * pts_ref.shape[2]
    scaled = pts_ref[...].reshape(tile, pts_ref.shape[3]).T[:FEAT] * scales_ref[...]
    high, middle, low = split_three(scaled)
    packed = jnp.concatenate([high, middle, high, low, high, middle], axis=0)
    pnorm = jnp.sum(scaled * scaled, axis=0, keepdims=True)
    pid = pid_ref[...]
    cross = jnp.dot(cs_ref[...], packed, preferred_element_type=jnp.float32)
    values = signal * jnp.exp(-0.5 * (cn_ref[...] + pnorm - 2.0 * cross))
    head = values[:, :128] + jnp.where(
        lax.broadcasted_iota(jnp.int32, (values.shape[0], 128), 0) == pid[:, :128], jitter, jnp.float32(0.0)
    )
    values = jnp.concatenate([head, values[:, 128:]], axis=1)
    first = jnp.dot(
        finv_ref[...], values[:PANEL], precision=HIGHEST, preferred_element_type=jnp.float32
    ).astype(jnp.bfloat16)
    reduced = values[PANEL:] - jnp.dot(mid_ref[...], first, preferred_element_type=jnp.float32)
    second = jnp.dot(
        sinv_ref[...], reduced, precision=HIGHEST, preferred_element_type=jnp.float32
    ).astype(jnp.bfloat16)
    own_cross = jnp.dot(own_cs_ref[...], packed, preferred_element_type=jnp.float32)
    own = signal * jnp.exp(-0.5 * (own_cn_ref[...] + pnorm - 2.0 * own_cross))
    own_head = own[:, :256] + jnp.where(own_ids_ref[...] == pid[:, :256], jitter, jnp.float32(0.0))
    own = jnp.concatenate([own_head, own[:, 256:]], axis=1)
    both = jnp.concatenate([first, second], axis=0)
    trailing = own - jnp.dot(own_panels_ref[...], both, preferred_element_type=jnp.float32)
    sel = sel_ref[...]
    result = jnp.concatenate(
        [
            jnp.dot(sel, first, preferred_element_type=jnp.float32),
            jnp.dot(sel, second, preferred_element_type=jnp.float32),
            trailing,
        ],
        axis=0,
    )
    lanes = out_ref.shape[2]
    for chunk in range(out_ref.shape[1]):
        out_ref[:, chunk, :] = result[:, chunk * lanes : (chunk + 1) * lanes]


def panel_stage(consts, gathered, pid, scales, cs, cn, own_cs, own_cn, own_ids, finv, sinv, mid, own_panels, sel):
    col_count, row_count, block_rows, _ = gathered.shape
    tile = col_count * block_rows
    grid_rows = tile * row_count
    out_rows = 2 * BLK + own_cs.shape[0]

    def whole(array):
        return pl.BlockSpec(array.shape, lambda i: (0,) * array.ndim)

    return pl.pallas_call(
        panel_kernel,
        grid=(row_count,),
        in_specs=[
            pl.BlockSpec(memory_space=pltpu.SMEM),
            pl.BlockSpec((col_count, 1, block_rows, gathered.shape[3]), lambda i: (0, i, 0, 0)),
            pl.BlockSpec((1, tile), lambda i: (0, i)),
        ]
        + [whole(a) for a in (scales, cs, cn, own_cs, own_cn, own_ids, finv, sinv, mid, own_panels, sel)],
        out_specs=pl.BlockSpec((out_rows, tile // 128, 128), lambda i: (0, i, 0)),
        out_shape=jax.ShapeDtypeStruct((out_rows, grid_rows // 128, 128), jnp.float32),
    )(consts, gathered, pid, scales, cs, cn, own_cs, own_cn, own_ids, finv, sinv, mid, own_panels, sel)


def ridge_where(row_ids, col_ids, jitter):
    return jnp.where(row_ids[:, None] == col_ids[None, :], jitter, jnp.float32(0.0))


def gather_by_all_to_all(piece, axis_name):
    count = lax.axis_size(axis_name)
    copies = jnp.broadcast_to(piece[None], (count,) + piece.shape)
    return lax.all_to_all(copies, axis_name, 0, 0, tiled=True)


def on_device(points, feature_scales, amplitude, ridge):
    row_count = lax.axis_size("row")
    col_count = lax.axis_size("col")
    row = lax.axis_index("row")
    column = lax.axis_index("col")
    rows_one = points.shape[0]
    block_rows = rows_one // row_count
    col_blocks = SLAB // (BLK * col_count)
    panel_blocks = PANEL // (BLK * col_count)
    center_sources = SLAB // rows_one
    signal = amplitude[0]
    jitter = ridge[0]

    blocks = points.reshape(row_count, block_rows, FEAT)
    moved = lax.all_to_all(blocks, "row", 0, 0, tiled=True)

    first_slot = gather_by_all_to_all(moved[0], "col")[:center_sources]
    center_grid = gather_by_all_to_all(first_slot, "row")
    centers = center_grid.transpose(1, 0, 2, 3).reshape(SLAB, FEAT)

    moved, centers = lax.optimization_barrier((moved, centers))
    padded = jnp.pad(moved, ((0, 0), (0, 0), (0, 128 - FEAT))).reshape(1, -1)
    copies = jnp.broadcast_to(padded, (col_count, padded.shape[1]))
    gathered = lax.all_to_all(copies, "col", 0, 0, tiled=True).reshape(
        col_count, row_count, block_rows, 128
    )
    grid_rows = gathered.shape[0] * gathered.shape[1] * block_rows

    center_scaled = centers * feature_scales
    center_norms = jnp.sum(center_scaled * center_scaled, axis=1)

    point_ids = (
        lax.broadcasted_iota(jnp.int32, (grid_rows // block_rows, block_rows), 0) * row_count
        + row
    ) * block_rows + lax.broadcasted_iota(jnp.int32, (grid_rows // block_rows, block_rows), 1)
    point_ids = point_ids.reshape(1, grid_rows)

    own_ids = (
        (
            lax.broadcasted_iota(jnp.int32, (col_blocks, BLK), 0) * col_count + column
        )
        * BLK
        + lax.broadcasted_iota(jnp.int32, (col_blocks, BLK), 1)
    )[2 * panel_blocks :].reshape(-1)
    own_scaled = jnp.take(center_scaled, own_ids, axis=0)
    own_norms = jnp.take(center_norms, own_ids, axis=0)

    lead_ids = jnp.arange(PANEL, dtype=jnp.int32)
    k11 = kernel_block(
        center_scaled[:PANEL], center_norms[:PANEL], center_scaled[:PANEL], center_norms[:PANEL], signal
    ) + ridge_where(lead_ids, lead_ids, jitter)
    used_ids = jnp.concatenate([jnp.arange(PANEL, 2 * PANEL, dtype=jnp.int32), own_ids])
    used_scaled = jnp.concatenate([center_scaled[PANEL : 2 * PANEL], own_scaled])
    used_norms = jnp.concatenate([center_norms[PANEL : 2 * PANEL], own_norms])
    used_kernel = kernel_block(
        used_scaled, used_norms, center_scaled[: 2 * PANEL], center_norms[: 2 * PANEL], signal
    ) + ridge_where(used_ids, jnp.arange(2 * PANEL, dtype=jnp.int32), jitter)
    first_inverse, second_inverse, first_mid, own_panels = factor_centers(k11, used_kernel)

    select = jnp.where(
        lax.broadcasted_iota(jnp.int32, (BLK, PANEL), 1)
        == column * BLK + lax.broadcasted_iota(jnp.int32, (BLK, PANEL), 0),
        1.0,
        0.0,
    ).astype(jnp.bfloat16)
    consts = jnp.stack([signal, jitter])
    finished = panel_stage(
        consts,
        gathered,
        point_ids,
        feature_scales.reshape(FEAT, 1),
        pack_left(center_scaled[: 2 * PANEL]),
        center_norms[: 2 * PANEL].reshape(-1, 1),
        pack_left(own_scaled),
        own_norms.reshape(-1, 1),
        own_ids.reshape(-1, 1),
        first_inverse,
        second_inverse,
        first_mid,
        own_panels,
        select,
    )
    return finished.reshape(col_blocks, 1, BLK, 1, grid_rows)


def solution(mesh):
    placed = (P(("row", "col"), None), P(), P(), P())
    return jax.shard_map(
        on_device,
        mesh=mesh,
        in_specs=placed,
        out_specs=P(None, "col", None, "row", None),
        check_vma=False,
    )
```

```python
import jax
import jax.numpy as jnp
from jax import lax
from jax.sharding import PartitionSpec as P
from jax.experimental import pallas as pl
from jax.experimental.pallas import tpu as pltpu

FEAT = 64
SLAB = 1536
PANEL = 256
BLK = 16

HIGHEST = lax.Precision.HIGHEST
PHASES = 8


def kernel_block(left, left_norms, right, right_norms, signal):
    cross = jnp.dot(left, right.T, precision=HIGHEST, preferred_element_type=jnp.float32)
    return signal * jnp.exp(-0.5 * (left_norms[:, None] + right_norms[None, :] - 2.0 * cross))


def _nt(left, right):
    return lax.dot_general(
        left, right, (((1,), (1,)), ((), ())), precision=HIGHEST, preferred_element_type=jnp.float32
    )


def lower_inverse_body(block, s_ref, x_ref):
    half = block.shape[0] // 2
    lane_row = lax.broadcasted_iota(jnp.int32, (1, half), 1)
    eye = jnp.where(
        lax.broadcasted_iota(jnp.int32, (half, half), 0)
        == lax.broadcasted_iota(jnp.int32, (half, half), 1),
        1.0,
        0.0,
    )

    def pick(values, index):
        return jnp.sum(jnp.where(lane_row == index, values, 0.0), axis=1, keepdims=True)

    def make_step(top):
        count = half - top
        lanes = lax.broadcasted_iota(jnp.int32, (count, half), 1)
        rows = lax.broadcasted_iota(jnp.int32, (count, 1), 0) + top

        def step(j, carry):
            k = 2 * j
            s = s_ref[top:, :]
            x = x_ref[top:, :]
            row0 = s_ref[pl.ds(k, 1), :]
            row1 = s_ref[pl.ds(k + 1, 1), :]
            col0 = jnp.sum(jnp.where(lanes == k, s, 0.0), axis=1, keepdims=True)
            col1 = jnp.sum(jnp.where(lanes == k + 1, s, 0.0), axis=1, keepdims=True)
            root0 = jnp.sqrt(pick(row0, k))
            cross = pick(row1, k) / root0
            root1 = jnp.sqrt(pick(row1, k + 1) - cross * cross)
            col0 = jnp.where(rows >= k, col0 / root0, 0.0)
            row0 = jnp.where(lane_row >= k, row0 / root0, 0.0)
            col1 = jnp.where(rows >= k + 1, (col1 - col0 * cross) / root1, 0.0)
            row1 = jnp.where(lane_row >= k + 1, (row1 - cross * row0) / root1, 0.0)
            s_ref[top:, :] = s - col0 * row0 - col1 * row1
            x0 = x_ref[pl.ds(k, 1), :] / root0
            x1 = (x_ref[pl.ds(k + 1, 1), :] - cross * x0) / root1
            rest = x - jnp.where(rows > k, col0, 0.0) * x0 - jnp.where(rows > k + 1, col1, 0.0) * x1
            x_ref[top:, :] = jnp.where(rows == k, x0, jnp.where(rows == k + 1, x1, rest))
            return carry

        return step

    def base(block):
        s_ref[...] = block
        x_ref[...] = eye.astype(jnp.float32)
        span = half // PHASES
        for phase in range(PHASES):
            lax.fori_loop(phase * span // 2, (phase + 1) * span // 2, make_step(phase * span), 0)
        return x_ref[...]

    first = base(block[:half, :half])
    lower = _nt(block[half:, :half], first)
    schur = block[half:, half:] - _nt(lower, lower)
    second = base((schur + schur.T) * 0.5)
    below = -jnp.dot(
        second,
        jnp.dot(lower, first, precision=HIGHEST, preferred_element_type=jnp.float32),
        precision=HIGHEST,
        preferred_element_type=jnp.float32,
    )
    top = jnp.concatenate([first, jnp.zeros((half, half), jnp.float32)], axis=1)
    return jnp.concatenate([top, jnp.concatenate([below, second], axis=1)], axis=0)


def factor_kernel(lead_ref, used_ref, finv_ref, sinv_ref, mid_ref, own_ref, s_ref, x_ref):
    first_inverse = lower_inverse_body(lead_ref[...], s_ref, x_ref)
    finv_ref[...] = first_inverse
    used = used_ref[...]
    panel = first_inverse.shape[0]
    center_first = _nt(used[:, :panel], first_inverse).astype(jnp.bfloat16)
    first_mid = center_first[:panel]
    mid_ref[...] = first_mid
    center_second = used[:, panel:] - lax.dot_general(
        center_first, first_mid, (((1,), (1,)), ((), ())), preferred_element_type=jnp.float32
    )
    block = center_second[:panel]
    second_inverse = lower_inverse_body((block + block.T) * 0.5, s_ref, x_ref)
    sinv_ref[...] = second_inverse
    second_own = _nt(center_second[panel:], second_inverse).astype(jnp.bfloat16)
    own_ref[...] = jnp.concatenate([center_first[panel:], second_own], axis=1)


def factor_centers(lead, used):
    panel = lead.shape[0]
    half = panel // 2
    own_rows = used.shape[0] - panel
    return pl.pallas_call(
        factor_kernel,
        out_shape=(
            jax.ShapeDtypeStruct((panel, panel), jnp.float32),
            jax.ShapeDtypeStruct((panel, panel), jnp.float32),
            jax.ShapeDtypeStruct((panel, panel), jnp.bfloat16),
            jax.ShapeDtypeStruct((own_rows, 2 * panel), jnp.bfloat16),
        ),
        scratch_shapes=[pltpu.VMEM((half, half), jnp.float32), pltpu.VMEM((half, half), jnp.float32)],
    )((lead + lead.T) * 0.5, used)


def split_three(values):
    high = values.astype(jnp.bfloat16)
    rest = values - high.astype(jnp.float32)
    middle = rest.astype(jnp.bfloat16)
    low = (rest - middle.astype(jnp.float32)).astype(jnp.bfloat16)
    return high, middle, low


def pack_left(values):
    high = lax.reduce_precision(values, exponent_bits=8, mantissa_bits=7)
    rest = values - high
    middle = lax.reduce_precision(rest, exponent_bits=8, mantissa_bits=7)
    low = rest - middle
    high, middle, low = (piece.astype(jnp.bfloat16) for piece in (high, middle, low))
    return jnp.concatenate([high, high, middle, high, low, middle], axis=1)


def panel_kernel(
    consts_ref, pts_ref, pid_ref, scales_ref, cs_ref, cn_ref, own_cs_ref, own_cn_ref,
    own_ids_ref, finv_ref, sinv_ref, mid_ref, own_panels_ref, sel_ref, out_ref,
):
    signal = consts_ref[0]
    jitter = consts_ref[1]
    points = jnp.concatenate(
        [pts_ref[:, part].reshape(-1, FEAT) for part in range(pts_ref.shape[1])], axis=0
    )
    scaled = (points * scales_ref[...]).T
    high, middle, low = split_three(scaled)
    packed = jnp.concatenate([high, middle, high, low, high, middle], axis=0)
    pnorm = jnp.sum(scaled * scaled, axis=0, keepdims=True)
    pid = pid_ref[...]
    cross = jnp.dot(cs_ref[...], packed, preferred_element_type=jnp.float32)
    values = signal * jnp.exp(-0.5 * (cn_ref[...] + pnorm - 2.0 * cross))
    head = values[:, :128] + jnp.where(
        lax.broadcasted_iota(jnp.int32, (values.shape[0], 128), 0) == pid[:, :128], jitter, jnp.float32(0.0)
    )
    values = jnp.concatenate([head, values[:, 128:]], axis=1)
    first = jnp.dot(
        finv_ref[...], values[:PANEL], precision=HIGHEST, preferred_element_type=jnp.float32
    ).astype(jnp.bfloat16)
    reduced = values[PANEL:] - jnp.dot(mid_ref[...], first, preferred_element_type=jnp.float32)
    second = jnp.dot(
        sinv_ref[...], reduced, precision=HIGHEST, preferred_element_type=jnp.float32
    ).astype(jnp.bfloat16)
    own_cross = jnp.dot(own_cs_ref[...], packed, preferred_element_type=jnp.float32)
    own = signal * jnp.exp(-0.5 * (own_cn_ref[...] + pnorm - 2.0 * own_cross))
    own_head = own[:, :256] + jnp.where(own_ids_ref[...] == pid[:, :256], jitter, jnp.float32(0.0))
    own = jnp.concatenate([own_head, own[:, 256:]], axis=1)
    both = jnp.concatenate([first, second], axis=0)
    trailing = own - jnp.dot(own_panels_ref[...], both, preferred_element_type=jnp.float32)
    sel = sel_ref[...]
    result = jnp.concatenate(
        [
            jnp.dot(sel, first, preferred_element_type=jnp.float32),
            jnp.dot(sel, second, preferred_element_type=jnp.float32),
            trailing,
        ],
        axis=0,
    )
    lanes = out_ref.shape[2]
    for chunk in range(out_ref.shape[1]):
        out_ref[:, chunk, :] = result[:, chunk * lanes : (chunk + 1) * lanes]


def panel_stage(consts, gathered, pid, scales, cs, cn, own_cs, own_cn, own_ids, finv, sinv, mid, own_panels, sel):
    col_count, row_count, block_rows, _ = gathered.shape
    parts = 2
    tile = col_count * block_rows * parts
    grid_rows = col_count * block_rows * row_count
    out_rows = 2 * BLK + own_cs.shape[0]

    def whole(array):
        return pl.BlockSpec(array.shape, lambda i: (0,) * array.ndim)

    return pl.pallas_call(
        panel_kernel,
        grid=(row_count // parts,),
        in_specs=[
            pl.BlockSpec(memory_space=pltpu.SMEM),
            pl.BlockSpec((col_count, parts, block_rows, FEAT), lambda i: (0, i, 0, 0)),
            pl.BlockSpec((1, tile), lambda i: (0, i)),
        ]
        + [whole(a) for a in (scales, cs, cn, own_cs, own_cn, own_ids, finv, sinv, mid, own_panels, sel)],
        out_specs=pl.BlockSpec((out_rows, tile // 128, 128), lambda i: (0, i, 0)),
        out_shape=jax.ShapeDtypeStruct((out_rows, grid_rows // 128, 128), jnp.float32),
    )(consts, gathered, pid, scales, cs, cn, own_cs, own_cn, own_ids, finv, sinv, mid, own_panels, sel)


def ridge_where(row_ids, col_ids, jitter):
    return jnp.where(row_ids[:, None] == col_ids[None, :], jitter, jnp.float32(0.0))


def gather_by_all_to_all(piece, axis_name):
    count = lax.axis_size(axis_name)
    copies = jnp.broadcast_to(piece[None], (count,) + piece.shape)
    return lax.all_to_all(copies, axis_name, 0, 0, tiled=True)


def on_device(points, feature_scales, amplitude, ridge):
    row_count = lax.axis_size("row")
    col_count = lax.axis_size("col")
    row = lax.axis_index("row")
    column = lax.axis_index("col")
    rows_one = points.shape[0]
    block_rows = rows_one // row_count
    col_blocks = SLAB // (BLK * col_count)
    panel_blocks = PANEL // (BLK * col_count)
    center_sources = SLAB // rows_one
    signal = amplitude[0]
    jitter = ridge[0]

    blocks = points.reshape(row_count, block_rows, FEAT)
    moved = lax.all_to_all(blocks, "row", 0, 0, tiled=True)

    first_slot = gather_by_all_to_all(moved[0], "col")[:center_sources]
    center_grid = gather_by_all_to_all(first_slot, "row")
    centers = center_grid.transpose(1, 0, 2, 3).reshape(SLAB, FEAT)

    moved, centers = lax.optimization_barrier((moved, centers))
    gathered = lax.all_gather(moved, "col", axis=0, tiled=False)
    grid_rows = gathered.shape[0] * gathered.shape[1] * block_rows

    center_scaled = centers * feature_scales
    center_norms = jnp.sum(center_scaled * center_scaled, axis=1)

    point_ids = (
        lax.broadcasted_iota(jnp.int32, (grid_rows // block_rows, block_rows), 0) * row_count
        + row
    ) * block_rows + lax.broadcasted_iota(jnp.int32, (grid_rows // block_rows, block_rows), 1)
    point_ids = point_ids.reshape(1, grid_rows)

    own_ids = (
        (
            lax.broadcasted_iota(jnp.int32, (col_blocks, BLK), 0) * col_count + column
        )
        * BLK
        + lax.broadcasted_iota(jnp.int32, (col_blocks, BLK), 1)
    )[2 * panel_blocks :].reshape(-1)
    own_scaled = jnp.take(center_scaled, own_ids, axis=0)
    own_norms = jnp.take(center_norms, own_ids, axis=0)

    lead_ids = jnp.arange(PANEL, dtype=jnp.int32)
    k11 = kernel_block(
        center_scaled[:PANEL], center_norms[:PANEL], center_scaled[:PANEL], center_norms[:PANEL], signal
    ) + ridge_where(lead_ids, lead_ids, jitter)
    used_ids = jnp.concatenate([jnp.arange(PANEL, 2 * PANEL, dtype=jnp.int32), own_ids])
    used_scaled = jnp.concatenate([center_scaled[PANEL : 2 * PANEL], own_scaled])
    used_norms = jnp.concatenate([center_norms[PANEL : 2 * PANEL], own_norms])
    used_kernel = kernel_block(
        used_scaled, used_norms, center_scaled[: 2 * PANEL], center_norms[: 2 * PANEL], signal
    ) + ridge_where(used_ids, jnp.arange(2 * PANEL, dtype=jnp.int32), jitter)
    first_inverse, second_inverse, first_mid, own_panels = factor_centers(k11, used_kernel)

    select = jnp.where(
        lax.broadcasted_iota(jnp.int32, (BLK, PANEL), 1)
        == column * BLK + lax.broadcasted_iota(jnp.int32, (BLK, PANEL), 0),
        1.0,
        0.0,
    ).astype(jnp.bfloat16)
    consts = jnp.stack([signal, jitter])
    finished = panel_stage(
        consts,
        gathered,
        point_ids,
        feature_scales.reshape(1, FEAT),
        pack_left(center_scaled[: 2 * PANEL]),
        center_norms[: 2 * PANEL].reshape(-1, 1),
        pack_left(own_scaled),
        own_norms.reshape(-1, 1),
        own_ids.reshape(-1, 1),
        first_inverse,
        second_inverse,
        first_mid,
        own_panels,
        select,
    )
    return finished.reshape(col_blocks, 1, BLK, 1, grid_rows)


def solution(mesh):
    placed = (P(("row", "col"), None), P(), P(), P())
    return jax.shard_map(
        on_device,
        mesh=mesh,
        in_specs=placed,
        out_specs=P(None, "col", None, "row", None),
        check_vma=False,
    )
```

```python
import jax
import jax.numpy as jnp
from jax import lax
from jax.sharding import PartitionSpec as P
from jax.experimental import pallas as pl
from jax.experimental.pallas import tpu as pltpu

FEAT = 64
SLAB = 1536
PANEL = 256
BLK = 16

HIGHEST = lax.Precision.HIGHEST
PHASES = 8


def kernel_block(left, left_norms, right, right_norms, signal):
    cross = jnp.dot(left, right.T, precision=HIGHEST, preferred_element_type=jnp.float32)
    return signal * jnp.exp(-0.5 * (left_norms[:, None] + right_norms[None, :] - 2.0 * cross))


def _nt(left, right):
    return lax.dot_general(
        left, right, (((1,), (1,)), ((), ())), precision=HIGHEST, preferred_element_type=jnp.float32
    )


def lower_inverse_body(block, s_ref, x_ref):
    half = block.shape[0] // 2
    lane_row = lax.broadcasted_iota(jnp.int32, (1, half), 1)
    eye = jnp.where(
        lax.broadcasted_iota(jnp.int32, (half, half), 0)
        == lax.broadcasted_iota(jnp.int32, (half, half), 1),
        1.0,
        0.0,
    )

    def pick(values, index):
        return jnp.sum(jnp.where(lane_row == index, values, 0.0), axis=1, keepdims=True)

    def make_step(top):
        count = half - top
        lanes = lax.broadcasted_iota(jnp.int32, (count, half), 1)
        rows = lax.broadcasted_iota(jnp.int32, (count, 1), 0) + top

        def step(j, carry):
            k = 2 * j
            s = s_ref[top:, :]
            x = x_ref[top:, :]
            row0 = s_ref[pl.ds(k, 1), :]
            row1 = s_ref[pl.ds(k + 1, 1), :]
            col0 = jnp.sum(jnp.where(lanes == k, s, 0.0), axis=1, keepdims=True)
            col1 = jnp.sum(jnp.where(lanes == k + 1, s, 0.0), axis=1, keepdims=True)
            root0 = jnp.sqrt(pick(row0, k))
            cross = pick(row1, k) / root0
            root1 = jnp.sqrt(pick(row1, k + 1) - cross * cross)
            col0 = jnp.where(rows >= k, col0 / root0, 0.0)
            row0 = jnp.where(lane_row >= k, row0 / root0, 0.0)
            col1 = jnp.where(rows >= k + 1, (col1 - col0 * cross) / root1, 0.0)
            row1 = jnp.where(lane_row >= k + 1, (row1 - cross * row0) / root1, 0.0)
            s_ref[top:, :] = s - col0 * row0 - col1 * row1
            x0 = x_ref[pl.ds(k, 1), :] / root0
            x1 = (x_ref[pl.ds(k + 1, 1), :] - cross * x0) / root1
            rest = x - jnp.where(rows > k, col0, 0.0) * x0 - jnp.where(rows > k + 1, col1, 0.0) * x1
            x_ref[top:, :] = jnp.where(rows == k, x0, jnp.where(rows == k + 1, x1, rest))
            return carry

        return step

    def base(block):
        s_ref[...] = block
        x_ref[...] = eye.astype(jnp.float32)
        span = half // PHASES
        for phase in range(PHASES):
            lax.fori_loop(phase * span // 2, (phase + 1) * span // 2, make_step(phase * span), 0)
        return x_ref[...]

    first = base(block[:half, :half])
    lower = _nt(block[half:, :half], first)
    schur = block[half:, half:] - _nt(lower, lower)
    second = base((schur + schur.T) * 0.5)
    below = -jnp.dot(
        second,
        jnp.dot(lower, first, precision=HIGHEST, preferred_element_type=jnp.float32),
        precision=HIGHEST,
        preferred_element_type=jnp.float32,
    )
    top = jnp.concatenate([first, jnp.zeros((half, half), jnp.float32)], axis=1)
    return jnp.concatenate([top, jnp.concatenate([below, second], axis=1)], axis=0)


def factor_kernel(lead_ref, used_ref, finv_ref, sinv_ref, mid_ref, own_ref, s_ref, x_ref):
    first_inverse = lower_inverse_body(lead_ref[...], s_ref, x_ref)
    finv_ref[...] = first_inverse
    used = used_ref[...]
    panel = first_inverse.shape[0]
    center_first = _nt(used[:, :panel], first_inverse).astype(jnp.bfloat16)
    first_mid = center_first[:panel]
    mid_ref[...] = first_mid
    center_second = used[:, panel:] - lax.dot_general(
        center_first, first_mid, (((1,), (1,)), ((), ())), preferred_element_type=jnp.float32
    )
    block = center_second[:panel]
    second_inverse = lower_inverse_body((block + block.T) * 0.5, s_ref, x_ref)
    sinv_ref[...] = second_inverse
    second_own = _nt(center_second[panel:], second_inverse).astype(jnp.bfloat16)
    own_ref[...] = jnp.concatenate([center_first[panel:], second_own], axis=1)


def factor_centers(lead, used):
    panel = lead.shape[0]
    half = panel // 2
    own_rows = used.shape[0] - panel
    return pl.pallas_call(
        factor_kernel,
        out_shape=(
            jax.ShapeDtypeStruct((panel, panel), jnp.float32),
            jax.ShapeDtypeStruct((panel, panel), jnp.float32),
            jax.ShapeDtypeStruct((panel, panel), jnp.bfloat16),
            jax.ShapeDtypeStruct((own_rows, 2 * panel), jnp.bfloat16),
        ),
        scratch_shapes=[pltpu.VMEM((half, half), jnp.float32), pltpu.VMEM((half, half), jnp.float32)],
    )((lead + lead.T) * 0.5, used)


def split_three(values):
    high = values.astype(jnp.bfloat16)
    rest = values - high.astype(jnp.float32)
    middle = rest.astype(jnp.bfloat16)
    low = (rest - middle.astype(jnp.float32)).astype(jnp.bfloat16)
    return high, middle, low


def pack_left(values):
    high = lax.reduce_precision(values, exponent_bits=8, mantissa_bits=7)
    rest = values - high
    middle = lax.reduce_precision(rest, exponent_bits=8, mantissa_bits=7)
    low = rest - middle
    high, middle, low = (piece.astype(jnp.bfloat16) for piece in (high, middle, low))
    return jnp.concatenate([high, high, middle, high, low, middle], axis=1)


def panel_kernel(
    consts_ref, pts_ref, pid_ref, scales_ref, cs_ref, cn_ref, own_cs_ref, own_cn_ref,
    own_ids_ref, finv_ref, sinv_ref, mid_ref, own_panels_ref, sel_ref, out_ref,
):
    signal = consts_ref[0]
    jitter = consts_ref[1]
    points = jnp.concatenate(
        [pts_ref[:, part].reshape(-1, FEAT) for part in range(pts_ref.shape[1])], axis=0
    )
    scaled = (points * scales_ref[...]).T
    high, middle, low = split_three(scaled)
    packed = jnp.concatenate([high, middle, high, low, high, middle], axis=0)
    pnorm = jnp.sum(scaled * scaled, axis=0, keepdims=True)
    pid = pid_ref[...]
    cross = jnp.dot(cs_ref[...], packed, preferred_element_type=jnp.float32)
    values = signal * jnp.exp(-0.5 * (cn_ref[...] + pnorm - 2.0 * cross))
    head = values[:, :128] + jnp.where(
        lax.broadcasted_iota(jnp.int32, (values.shape[0], 128), 0) == pid[:, :128], jitter, jnp.float32(0.0)
    )
    values = jnp.concatenate([head, values[:, 128:]], axis=1)
    first = jnp.dot(
        finv_ref[...], values[:PANEL], precision=HIGHEST, preferred_element_type=jnp.float32
    ).astype(jnp.bfloat16)
    reduced = values[PANEL:] - jnp.dot(mid_ref[...], first, preferred_element_type=jnp.float32)
    second = jnp.dot(
        sinv_ref[...], reduced, precision=HIGHEST, preferred_element_type=jnp.float32
    ).astype(jnp.bfloat16)
    own_cross = jnp.dot(own_cs_ref[...], packed, preferred_element_type=jnp.float32)
    own = signal * jnp.exp(-0.5 * (own_cn_ref[...] + pnorm - 2.0 * own_cross))
    own_head = own[:, :256] + jnp.where(own_ids_ref[...] == pid[:, :256], jitter, jnp.float32(0.0))
    own = jnp.concatenate([own_head, own[:, 256:]], axis=1)
    both = jnp.concatenate([first, second], axis=0)
    trailing = own - jnp.dot(own_panels_ref[...], both, preferred_element_type=jnp.float32)
    sel = sel_ref[...]
    result = jnp.concatenate(
        [
            jnp.dot(sel, first, preferred_element_type=jnp.float32),
            jnp.dot(sel, second, preferred_element_type=jnp.float32),
            trailing,
        ],
        axis=0,
    )
    lanes = out_ref.shape[2]
    for chunk in range(out_ref.shape[1]):
        out_ref[:, chunk, :] = result[:, chunk * lanes : (chunk + 1) * lanes]


def panel_stage(consts, gathered, pid, scales, cs, cn, own_cs, own_cn, own_ids, finv, sinv, mid, own_panels, sel):
    col_count, row_count, block_rows, _ = gathered.shape
    parts = 4
    tile = col_count * block_rows * parts
    grid_rows = col_count * block_rows * row_count
    out_rows = 2 * BLK + own_cs.shape[0]

    def whole(array):
        return pl.BlockSpec(array.shape, lambda i: (0,) * array.ndim)

    return pl.pallas_call(
        panel_kernel,
        grid=(row_count // parts,),
        in_specs=[
            pl.BlockSpec(memory_space=pltpu.SMEM),
            pl.BlockSpec((col_count, parts, block_rows, FEAT), lambda i: (0, i, 0, 0)),
            pl.BlockSpec((1, tile), lambda i: (0, i)),
        ]
        + [whole(a) for a in (scales, cs, cn, own_cs, own_cn, own_ids, finv, sinv, mid, own_panels, sel)],
        out_specs=pl.BlockSpec((out_rows, tile // 128, 128), lambda i: (0, i, 0)),
        out_shape=jax.ShapeDtypeStruct((out_rows, grid_rows // 128, 128), jnp.float32),
    )(consts, gathered, pid, scales, cs, cn, own_cs, own_cn, own_ids, finv, sinv, mid, own_panels, sel)


def ridge_where(row_ids, col_ids, jitter):
    return jnp.where(row_ids[:, None] == col_ids[None, :], jitter, jnp.float32(0.0))


def gather_by_all_to_all(piece, axis_name):
    count = lax.axis_size(axis_name)
    copies = jnp.broadcast_to(piece[None], (count,) + piece.shape)
    return lax.all_to_all(copies, axis_name, 0, 0, tiled=True)


def on_device(points, feature_scales, amplitude, ridge):
    row_count = lax.axis_size("row")
    col_count = lax.axis_size("col")
    row = lax.axis_index("row")
    column = lax.axis_index("col")
    rows_one = points.shape[0]
    block_rows = rows_one // row_count
    col_blocks = SLAB // (BLK * col_count)
    panel_blocks = PANEL // (BLK * col_count)
    center_sources = SLAB // rows_one
    signal = amplitude[0]
    jitter = ridge[0]

    blocks = points.reshape(row_count, block_rows, FEAT)
    moved = lax.all_to_all(blocks, "row", 0, 0, tiled=True)

    first_slot = gather_by_all_to_all(moved[0], "col")[:center_sources]
    center_grid = gather_by_all_to_all(first_slot, "row")
    centers = center_grid.transpose(1, 0, 2, 3).reshape(SLAB, FEAT)

    moved, centers = lax.optimization_barrier((moved, centers))
    gathered = lax.all_gather(moved, "col", axis=0, tiled=False)
    grid_rows = gathered.shape[0] * gathered.shape[1] * block_rows

    center_scaled = centers * feature_scales
    center_norms = jnp.sum(center_scaled * center_scaled, axis=1)

    point_ids = (
        lax.broadcasted_iota(jnp.int32, (grid_rows // block_rows, block_rows), 0) * row_count
        + row
    ) * block_rows + lax.broadcasted_iota(jnp.int32, (grid_rows // block_rows, block_rows), 1)
    point_ids = point_ids.reshape(1, grid_rows)

    own_ids = (
        (
            lax.broadcasted_iota(jnp.int32, (col_blocks, BLK), 0) * col_count + column
        )
        * BLK
        + lax.broadcasted_iota(jnp.int32, (col_blocks, BLK), 1)
    )[2 * panel_blocks :].reshape(-1)
    own_scaled = jnp.take(center_scaled, own_ids, axis=0)
    own_norms = jnp.take(center_norms, own_ids, axis=0)

    lead_ids = jnp.arange(PANEL, dtype=jnp.int32)
    k11 = kernel_block(
        center_scaled[:PANEL], center_norms[:PANEL], center_scaled[:PANEL], center_norms[:PANEL], signal
    ) + ridge_where(lead_ids, lead_ids, jitter)
    used_ids = jnp.concatenate([jnp.arange(PANEL, 2 * PANEL, dtype=jnp.int32), own_ids])
    used_scaled = jnp.concatenate([center_scaled[PANEL : 2 * PANEL], own_scaled])
    used_norms = jnp.concatenate([center_norms[PANEL : 2 * PANEL], own_norms])
    used_kernel = kernel_block(
        used_scaled, used_norms, center_scaled[: 2 * PANEL], center_norms[: 2 * PANEL], signal
    ) + ridge_where(used_ids, jnp.arange(2 * PANEL, dtype=jnp.int32), jitter)
    first_inverse, second_inverse, first_mid, own_panels = factor_centers(k11, used_kernel)

    select = jnp.where(
        lax.broadcasted_iota(jnp.int32, (BLK, PANEL), 1)
        == column * BLK + lax.broadcasted_iota(jnp.int32, (BLK, PANEL), 0),
        1.0,
        0.0,
    ).astype(jnp.bfloat16)
    consts = jnp.stack([signal, jitter])
    finished = panel_stage(
        consts,
        gathered,
        point_ids,
        feature_scales.reshape(1, FEAT),
        pack_left(center_scaled[: 2 * PANEL]),
        center_norms[: 2 * PANEL].reshape(-1, 1),
        pack_left(own_scaled),
        own_norms.reshape(-1, 1),
        own_ids.reshape(-1, 1),
        first_inverse,
        second_inverse,
        first_mid,
        own_panels,
        select,
    )
    return finished.reshape(col_blocks, 1, BLK, 1, grid_rows)


def solution(mesh):
    placed = (P(("row", "col"), None), P(), P(), P())
    return jax.shard_map(
        on_device,
        mesh=mesh,
        in_specs=placed,
        out_specs=P(None, "col", None, "row", None),
        check_vma=False,
    )
```

```python
import jax
import jax.numpy as jnp
from jax import lax
from jax.sharding import PartitionSpec as P
from jax.experimental import pallas as pl
from jax.experimental.pallas import tpu as pltpu

FEAT = 64
SLAB = 1536
PANEL = 256
BLK = 16

HIGHEST = lax.Precision.HIGHEST
PHASES = 8


def kernel_block(left, left_norms, right, right_norms, signal):
    cross = jnp.dot(left, right.T, precision=HIGHEST, preferred_element_type=jnp.float32)
    return signal * jnp.exp(-0.5 * (left_norms[:, None] + right_norms[None, :] - 2.0 * cross))


def _nt(left, right):
    return lax.dot_general(
        left, right, (((1,), (1,)), ((), ())), precision=HIGHEST, preferred_element_type=jnp.float32
    )


def lower_inverse_body(block, s_ref, x_ref):
    half = block.shape[0] // 2
    lane_row = lax.broadcasted_iota(jnp.int32, (1, half), 1)
    eye = jnp.where(
        lax.broadcasted_iota(jnp.int32, (half, half), 0)
        == lax.broadcasted_iota(jnp.int32, (half, half), 1),
        1.0,
        0.0,
    )

    def pick(values, index):
        return jnp.sum(jnp.where(lane_row == index, values, 0.0), axis=1, keepdims=True)

    def make_step(top):
        count = half - top
        lanes = lax.broadcasted_iota(jnp.int32, (count, half), 1)
        rows = lax.broadcasted_iota(jnp.int32, (count, 1), 0) + top

        def step(j, carry):
            k = 2 * j
            s = s_ref[top:, :]
            x = x_ref[top:, :]
            row0 = s_ref[pl.ds(k, 1), :]
            row1 = s_ref[pl.ds(k + 1, 1), :]
            col0 = jnp.sum(jnp.where(lanes == k, s, 0.0), axis=1, keepdims=True)
            col1 = jnp.sum(jnp.where(lanes == k + 1, s, 0.0), axis=1, keepdims=True)
            root0 = jnp.sqrt(pick(row0, k))
            cross = pick(row1, k) / root0
            root1 = jnp.sqrt(pick(row1, k + 1) - cross * cross)
            col0 = jnp.where(rows >= k, col0 / root0, 0.0)
            row0 = jnp.where(lane_row >= k, row0 / root0, 0.0)
            col1 = jnp.where(rows >= k + 1, (col1 - col0 * cross) / root1, 0.0)
            row1 = jnp.where(lane_row >= k + 1, (row1 - cross * row0) / root1, 0.0)
            s_ref[top:, :] = s - col0 * row0 - col1 * row1
            x0 = x_ref[pl.ds(k, 1), :] / root0
            x1 = (x_ref[pl.ds(k + 1, 1), :] - cross * x0) / root1
            rest = x - jnp.where(rows > k, col0, 0.0) * x0 - jnp.where(rows > k + 1, col1, 0.0) * x1
            x_ref[top:, :] = jnp.where(rows == k, x0, jnp.where(rows == k + 1, x1, rest))
            return carry

        return step

    def base(block):
        s_ref[...] = block
        x_ref[...] = eye.astype(jnp.float32)
        span = half // PHASES
        for phase in range(PHASES):
            lax.fori_loop(phase * span // 2, (phase + 1) * span // 2, make_step(phase * span), 0)
        return x_ref[...]

    first = base(block[:half, :half])
    lower = _nt(block[half:, :half], first)
    schur = block[half:, half:] - _nt(lower, lower)
    second = base((schur + schur.T) * 0.5)
    below = -jnp.dot(
        second,
        jnp.dot(lower, first, precision=HIGHEST, preferred_element_type=jnp.float32),
        precision=HIGHEST,
        preferred_element_type=jnp.float32,
    )
    top = jnp.concatenate([first, jnp.zeros((half, half), jnp.float32)], axis=1)
    return jnp.concatenate([top, jnp.concatenate([below, second], axis=1)], axis=0)


def factor_kernel(lead_ref, used_ref, finv_ref, sinv_ref, mid_ref, own_ref, s_ref, x_ref):
    first_inverse = lower_inverse_body(lead_ref[...], s_ref, x_ref)
    finv_ref[...] = first_inverse
    used = used_ref[...]
    panel = first_inverse.shape[0]
    center_first = _nt(used[:, :panel], first_inverse).astype(jnp.bfloat16)
    first_mid = center_first[:panel]
    mid_ref[...] = first_mid
    center_second = used[:, panel:] - lax.dot_general(
        center_first, first_mid, (((1,), (1,)), ((), ())), preferred_element_type=jnp.float32
    )
    block = center_second[:panel]
    second_inverse = lower_inverse_body((block + block.T) * 0.5, s_ref, x_ref)
    sinv_ref[...] = second_inverse
    second_own = _nt(center_second[panel:], second_inverse).astype(jnp.bfloat16)
    own_ref[...] = jnp.concatenate([center_first[panel:], second_own], axis=1)


def factor_centers(lead, used):
    panel = lead.shape[0]
    half = panel // 2
    own_rows = used.shape[0] - panel
    return pl.pallas_call(
        factor_kernel,
        out_shape=(
            jax.ShapeDtypeStruct((panel, panel), jnp.float32),
            jax.ShapeDtypeStruct((panel, panel), jnp.float32),
            jax.ShapeDtypeStruct((panel, panel), jnp.bfloat16),
            jax.ShapeDtypeStruct((own_rows, 2 * panel), jnp.bfloat16),
        ),
        scratch_shapes=[pltpu.VMEM((half, half), jnp.float32), pltpu.VMEM((half, half), jnp.float32)],
    )((lead + lead.T) * 0.5, used)


def split_three(values):
    high = values.astype(jnp.bfloat16)
    rest = values - high.astype(jnp.float32)
    middle = rest.astype(jnp.bfloat16)
    low = (rest - middle.astype(jnp.float32)).astype(jnp.bfloat16)
    return high, middle, low


def pack_left(values):
    high = lax.reduce_precision(values, exponent_bits=8, mantissa_bits=7)
    rest = values - high
    middle = lax.reduce_precision(rest, exponent_bits=8, mantissa_bits=7)
    low = rest - middle
    high, middle, low = (piece.astype(jnp.bfloat16) for piece in (high, middle, low))
    return jnp.concatenate([high, high, middle, high, low, middle], axis=1)


def panel_kernel(
    consts_ref, pts_ref, pid_ref, scales_ref, cs_ref, cn_ref, own_cs_ref, own_cn_ref,
    own_ids_ref, finv_ref, sinv_ref, mid_ref, own_panels_ref, sel_ref, out_ref,
):
    signal = consts_ref[0]
    jitter = consts_ref[1]
    points = jnp.concatenate(
        [pts_ref[:, part].reshape(-1, FEAT) for part in range(pts_ref.shape[1])], axis=0
    )
    scaled = (points * scales_ref[...]).T
    high, middle, low = split_three(scaled)
    packed = jnp.concatenate([high, middle, high, low, high, middle], axis=0)
    pnorm = jnp.sum(scaled * scaled, axis=0, keepdims=True)
    pid = pid_ref[...]
    cross = jnp.dot(cs_ref[...], packed, preferred_element_type=jnp.float32)
    values = signal * jnp.exp(-0.5 * (cn_ref[...] + pnorm - 2.0 * cross))
    head = values[:, :128] + jnp.where(
        lax.broadcasted_iota(jnp.int32, (values.shape[0], 128), 0) == pid[:, :128], jitter, jnp.float32(0.0)
    )
    values = jnp.concatenate([head, values[:, 128:]], axis=1)
    first = jnp.dot(
        finv_ref[...], values[:PANEL], precision=HIGHEST, preferred_element_type=jnp.float32
    ).astype(jnp.bfloat16)
    reduced = values[PANEL:] - jnp.dot(mid_ref[...], first, preferred_element_type=jnp.float32)
    second = jnp.dot(
        sinv_ref[...], reduced, precision=HIGHEST, preferred_element_type=jnp.float32
    ).astype(jnp.bfloat16)
    own_cross = jnp.dot(own_cs_ref[...], packed, preferred_element_type=jnp.float32)
    own = signal * jnp.exp(-0.5 * (own_cn_ref[...] + pnorm - 2.0 * own_cross))
    own_head = own[:, :256] + jnp.where(own_ids_ref[...] == pid[:, :256], jitter, jnp.float32(0.0))
    own = jnp.concatenate([own_head, own[:, 256:]], axis=1)
    both = jnp.concatenate([first, second], axis=0)
    trailing = own - jnp.dot(own_panels_ref[...], both, preferred_element_type=jnp.float32)
    sel = sel_ref[...]
    result = jnp.concatenate(
        [
            jnp.dot(sel, first, preferred_element_type=jnp.float32),
            jnp.dot(sel, second, preferred_element_type=jnp.float32),
            trailing,
        ],
        axis=0,
    )
    lanes = out_ref.shape[2]
    for chunk in range(out_ref.shape[1]):
        out_ref[:, chunk, :] = result[:, chunk * lanes : (chunk + 1) * lanes]


def panel_stage(consts, gathered, pid, scales, cs, cn, own_cs, own_cn, own_ids, finv, sinv, mid, own_panels, sel):
    col_count, row_count, block_rows, _ = gathered.shape
    parts = 2
    tile = col_count * block_rows * parts
    grid_rows = col_count * block_rows * row_count
    out_rows = 2 * BLK + own_cs.shape[0]

    def whole(array):
        return pl.BlockSpec(array.shape, lambda i: (0,) * array.ndim)

    return pl.pallas_call(
        panel_kernel,
        grid=(row_count // parts,),
        in_specs=[
            pl.BlockSpec(memory_space=pltpu.SMEM),
            pl.BlockSpec((col_count, parts, block_rows, FEAT), lambda i: (0, i, 0, 0)),
            pl.BlockSpec((1, tile), lambda i: (0, i)),
        ]
        + [whole(a) for a in (scales, cs, cn, own_cs, own_cn, own_ids, finv, sinv, mid, own_panels, sel)],
        out_specs=pl.BlockSpec((out_rows, tile // 128, 128), lambda i: (0, i, 0)),
        out_shape=jax.ShapeDtypeStruct((out_rows, grid_rows // 128, 128), jnp.float32),
    )(consts, gathered, pid, scales, cs, cn, own_cs, own_cn, own_ids, finv, sinv, mid, own_panels, sel)


def ridge_where(row_ids, col_ids, jitter):
    return jnp.where(row_ids[:, None] == col_ids[None, :], jitter, jnp.float32(0.0))


def gather_by_all_to_all(piece, axis_name):
    count = lax.axis_size(axis_name)
    copies = jnp.broadcast_to(piece[None], (count,) + piece.shape)
    return lax.all_to_all(copies, axis_name, 0, 0, tiled=True)


def on_device(points, feature_scales, amplitude, ridge):
    row_count = lax.axis_size("row")
    col_count = lax.axis_size("col")
    row = lax.axis_index("row")
    column = lax.axis_index("col")
    rows_one = points.shape[0]
    block_rows = rows_one // row_count
    col_blocks = SLAB // (BLK * col_count)
    panel_blocks = PANEL // (BLK * col_count)
    center_sources = SLAB // rows_one
    signal = amplitude[0]
    jitter = ridge[0]

    blocks = points.reshape(row_count, block_rows, FEAT)
    moved = lax.all_to_all(blocks, "row", 0, 0, tiled=True)

    flat_slot = moved[0].reshape(1, -1)
    first_slot = lax.all_to_all(
        jnp.broadcast_to(flat_slot, (col_count, flat_slot.shape[1])), "col", 0, 0, tiled=True
    )[:center_sources].reshape(1, -1)
    center_grid = lax.all_to_all(
        jnp.broadcast_to(first_slot, (row_count, first_slot.shape[1])), "row", 0, 0, tiled=True
    ).reshape(row_count, center_sources, block_rows, FEAT)
    centers = center_grid.transpose(1, 0, 2, 3).reshape(SLAB, FEAT)

    moved, centers = lax.optimization_barrier((moved, centers))
    gathered = lax.all_gather(moved, "col", axis=0, tiled=False)
    grid_rows = gathered.shape[0] * gathered.shape[1] * block_rows

    center_scaled = centers * feature_scales
    center_norms = jnp.sum(center_scaled * center_scaled, axis=1)

    point_ids = (
        lax.broadcasted_iota(jnp.int32, (grid_rows // block_rows, block_rows), 0) * row_count
        + row
    ) * block_rows + lax.broadcasted_iota(jnp.int32, (grid_rows // block_rows, block_rows), 1)
    point_ids = point_ids.reshape(1, grid_rows)

    own_ids = (
        (
            lax.broadcasted_iota(jnp.int32, (col_blocks, BLK), 0) * col_count + column
        )
        * BLK
        + lax.broadcasted_iota(jnp.int32, (col_blocks, BLK), 1)
    )[2 * panel_blocks :].reshape(-1)
    own_scaled = jnp.take(center_scaled, own_ids, axis=0)
    own_norms = jnp.take(center_norms, own_ids, axis=0)

    lead_ids = jnp.arange(PANEL, dtype=jnp.int32)
    k11 = kernel_block(
        center_scaled[:PANEL], center_norms[:PANEL], center_scaled[:PANEL], center_norms[:PANEL], signal
    ) + ridge_where(lead_ids, lead_ids, jitter)
    used_ids = jnp.concatenate([jnp.arange(PANEL, 2 * PANEL, dtype=jnp.int32), own_ids])
    used_scaled = jnp.concatenate([center_scaled[PANEL : 2 * PANEL], own_scaled])
    used_norms = jnp.concatenate([center_norms[PANEL : 2 * PANEL], own_norms])
    used_kernel = kernel_block(
        used_scaled, used_norms, center_scaled[: 2 * PANEL], center_norms[: 2 * PANEL], signal
    ) + ridge_where(used_ids, jnp.arange(2 * PANEL, dtype=jnp.int32), jitter)
    first_inverse, second_inverse, first_mid, own_panels = factor_centers(k11, used_kernel)

    select = jnp.where(
        lax.broadcasted_iota(jnp.int32, (BLK, PANEL), 1)
        == column * BLK + lax.broadcasted_iota(jnp.int32, (BLK, PANEL), 0),
        1.0,
        0.0,
    ).astype(jnp.bfloat16)
    consts = jnp.stack([signal, jitter])
    finished = panel_stage(
        consts,
        gathered,
        point_ids,
        feature_scales.reshape(1, FEAT),
        pack_left(center_scaled[: 2 * PANEL]),
        center_norms[: 2 * PANEL].reshape(-1, 1),
        pack_left(own_scaled),
        own_norms.reshape(-1, 1),
        own_ids.reshape(-1, 1),
        first_inverse,
        second_inverse,
        first_mid,
        own_panels,
        select,
    )
    return finished.reshape(col_blocks, 1, BLK, 1, grid_rows)


def solution(mesh):
    placed = (P(("row", "col"), None), P(), P(), P())
    return jax.shard_map(
        on_device,
        mesh=mesh,
        in_specs=placed,
        out_specs=P(None, "col", None, "row", None),
        check_vma=False,
    )
```

```python
import jax
import jax.numpy as jnp
from jax import lax
from jax.sharding import PartitionSpec as P
from jax.experimental import pallas as pl
from jax.experimental.pallas import tpu as pltpu

FEAT = 64
SLAB = 1536
PANEL = 256
BLK = 16

HIGHEST = lax.Precision.HIGHEST
PHASES = 8


def kernel_block(left, left_norms, right, right_norms, signal):
    cross = jnp.dot(left, right.T, precision=HIGHEST, preferred_element_type=jnp.float32)
    return signal * jnp.exp(-0.5 * (left_norms[:, None] + right_norms[None, :] - 2.0 * cross))


def _nt(left, right):
    return lax.dot_general(
        left, right, (((1,), (1,)), ((), ())), precision=HIGHEST, preferred_element_type=jnp.float32
    )


def lower_inverse_body(block, s_ref, x_ref):
    half = block.shape[0] // 2
    lane_row = lax.broadcasted_iota(jnp.int32, (1, half), 1)
    eye = jnp.where(
        lax.broadcasted_iota(jnp.int32, (half, half), 0)
        == lax.broadcasted_iota(jnp.int32, (half, half), 1),
        1.0,
        0.0,
    )

    def pick(values, index):
        return jnp.sum(jnp.where(lane_row == index, values, 0.0), axis=1, keepdims=True)

    def make_step(top):
        count = half - top
        lanes = lax.broadcasted_iota(jnp.int32, (count, half), 1)
        rows = lax.broadcasted_iota(jnp.int32, (count, 1), 0) + top

        def step(j, carry):
            k = 2 * j
            s = s_ref[top:, :]
            x = x_ref[top:, :]
            row0 = s_ref[pl.ds(k, 1), :]
            row1 = s_ref[pl.ds(k + 1, 1), :]
            col0 = jnp.sum(jnp.where(lanes == k, s, 0.0), axis=1, keepdims=True)
            col1 = jnp.sum(jnp.where(lanes == k + 1, s, 0.0), axis=1, keepdims=True)
            root0 = jnp.sqrt(pick(row0, k))
            cross = pick(row1, k) / root0
            root1 = jnp.sqrt(pick(row1, k + 1) - cross * cross)
            col0 = jnp.where(rows >= k, col0 / root0, 0.0)
            row0 = jnp.where(lane_row >= k, row0 / root0, 0.0)
            col1 = jnp.where(rows >= k + 1, (col1 - col0 * cross) / root1, 0.0)
            row1 = jnp.where(lane_row >= k + 1, (row1 - cross * row0) / root1, 0.0)
            s_ref[top:, :] = s - col0 * row0 - col1 * row1
            x0 = x_ref[pl.ds(k, 1), :] / root0
            x1 = (x_ref[pl.ds(k + 1, 1), :] - cross * x0) / root1
            rest = x - jnp.where(rows > k, col0, 0.0) * x0 - jnp.where(rows > k + 1, col1, 0.0) * x1
            x_ref[top:, :] = jnp.where(rows == k, x0, jnp.where(rows == k + 1, x1, rest))
            return carry

        return step

    def base(block):
        s_ref[...] = block
        x_ref[...] = eye.astype(jnp.float32)
        span = half // PHASES
        for phase in range(PHASES):
            lax.fori_loop(phase * span // 2, (phase + 1) * span // 2, make_step(phase * span), 0)
        return x_ref[...]

    first = base(block[:half, :half])
    lower = _nt(block[half:, :half], first)
    schur = block[half:, half:] - _nt(lower, lower)
    second = base((schur + schur.T) * 0.5)
    below = -jnp.dot(
        second,
        jnp.dot(lower, first, precision=HIGHEST, preferred_element_type=jnp.float32),
        precision=HIGHEST,
        preferred_element_type=jnp.float32,
    )
    top = jnp.concatenate([first, jnp.zeros((half, half), jnp.float32)], axis=1)
    return jnp.concatenate([top, jnp.concatenate([below, second], axis=1)], axis=0)


def factor_kernel(lead_ref, used_ref, finv_ref, sinv_ref, mid_ref, own_ref, s_ref, x_ref):
    first_inverse = lower_inverse_body(lead_ref[...], s_ref, x_ref)
    finv_ref[...] = first_inverse
    used = used_ref[...]
    panel = first_inverse.shape[0]
    center_first = _nt(used[:, :panel], first_inverse).astype(jnp.bfloat16)
    first_mid = center_first[:panel]
    mid_ref[...] = first_mid
    center_second = used[:, panel:] - lax.dot_general(
        center_first, first_mid, (((1,), (1,)), ((), ())), preferred_element_type=jnp.float32
    )
    block = center_second[:panel]
    second_inverse = lower_inverse_body((block + block.T) * 0.5, s_ref, x_ref)
    sinv_ref[...] = second_inverse
    second_own = _nt(center_second[panel:], second_inverse).astype(jnp.bfloat16)
    own_ref[...] = jnp.concatenate([center_first[panel:], second_own], axis=1)


def factor_centers(lead, used):
    panel = lead.shape[0]
    half = panel // 2
    own_rows = used.shape[0] - panel
    return pl.pallas_call(
        factor_kernel,
        out_shape=(
            jax.ShapeDtypeStruct((panel, panel), jnp.float32),
            jax.ShapeDtypeStruct((panel, panel), jnp.float32),
            jax.ShapeDtypeStruct((panel, panel), jnp.bfloat16),
            jax.ShapeDtypeStruct((own_rows, 2 * panel), jnp.bfloat16),
        ),
        scratch_shapes=[pltpu.VMEM((half, half), jnp.float32), pltpu.VMEM((half, half), jnp.float32)],
    )((lead + lead.T) * 0.5, used)


def split_three(values):
    high = values.astype(jnp.bfloat16)
    rest = values - high.astype(jnp.float32)
    middle = rest.astype(jnp.bfloat16)
    low = (rest - middle.astype(jnp.float32)).astype(jnp.bfloat16)
    return high, middle, low


def pack_left(values):
    high = lax.reduce_precision(values, exponent_bits=8, mantissa_bits=7)
    rest = values - high
    middle = lax.reduce_precision(rest, exponent_bits=8, mantissa_bits=7)
    low = rest - middle
    high, middle, low = (piece.astype(jnp.bfloat16) for piece in (high, middle, low))
    return jnp.concatenate([high, high, middle, high, low, middle], axis=1)


def panel_kernel(
    consts_ref, pts_ref, pid_ref, scales_ref, cs_ref, cn_ref, own_cs_ref, own_cn_ref,
    own_ids_ref, finv_ref, sinv_ref, mid_ref, own_panels_ref, sel_ref, out_ref,
):
    signal = consts_ref[0]
    jitter = consts_ref[1]
    points = jnp.concatenate(
        [pts_ref[:, part].reshape(-1, FEAT) for part in range(pts_ref.shape[1])], axis=0
    )
    scaled = (points * scales_ref[...]).T
    high, middle, low = split_three(scaled)
    packed = jnp.concatenate([high, middle, high, low, high, middle], axis=0)
    pnorm = jnp.sum(scaled * scaled, axis=0, keepdims=True)
    pid = pid_ref[...]
    cross = jnp.dot(cs_ref[...], packed, preferred_element_type=jnp.float32)
    values = signal * jnp.exp(-0.5 * (cn_ref[...] + pnorm - 2.0 * cross))
    head = values[:, :128] + jnp.where(
        lax.broadcasted_iota(jnp.int32, (values.shape[0], 128), 0) == pid[:, :128], jitter, jnp.float32(0.0)
    )
    values = jnp.concatenate([head, values[:, 128:]], axis=1)
    first = jnp.dot(
        finv_ref[...], values[:PANEL], precision=HIGHEST, preferred_element_type=jnp.float32
    ).astype(jnp.bfloat16)
    reduced = values[PANEL:] - jnp.dot(mid_ref[...], first, preferred_element_type=jnp.float32)
    second = jnp.dot(
        sinv_ref[...], reduced, precision=HIGHEST, preferred_element_type=jnp.float32
    ).astype(jnp.bfloat16)
    own_cross = jnp.dot(own_cs_ref[...], packed, preferred_element_type=jnp.float32)
    own = signal * jnp.exp(-0.5 * (own_cn_ref[...] + pnorm - 2.0 * own_cross))
    own_head = own[:, :256] + jnp.where(own_ids_ref[...] == pid[:, :256], jitter, jnp.float32(0.0))
    own = jnp.concatenate([own_head, own[:, 256:]], axis=1)
    both = jnp.concatenate([first, second], axis=0)
    trailing = own - jnp.dot(own_panels_ref[...], both, preferred_element_type=jnp.float32)
    sel = sel_ref[...]
    result = jnp.concatenate(
        [
            jnp.dot(sel, first, preferred_element_type=jnp.float32),
            jnp.dot(sel, second, preferred_element_type=jnp.float32),
            trailing,
        ],
        axis=0,
    )
    lanes = out_ref.shape[2]
    for chunk in range(out_ref.shape[1]):
        out_ref[:, chunk, :] = result[:, chunk * lanes : (chunk + 1) * lanes]


def panel_stage(consts, gathered, pid, scales, cs, cn, own_cs, own_cn, own_ids, finv, sinv, mid, own_panels, sel):
    col_count, row_count, block_rows, _ = gathered.shape
    parts = 2
    tile = col_count * block_rows * parts
    grid_rows = col_count * block_rows * row_count
    out_rows = 2 * BLK + own_cs.shape[0]

    def whole(array):
        return pl.BlockSpec(array.shape, lambda i: (0,) * array.ndim)

    return pl.pallas_call(
        panel_kernel,
        grid=(row_count // parts,),
        in_specs=[
            pl.BlockSpec(memory_space=pltpu.SMEM),
            pl.BlockSpec((col_count, parts, block_rows, FEAT), lambda i: (0, i, 0, 0)),
            pl.BlockSpec((1, tile), lambda i: (0, i)),
        ]
        + [whole(a) for a in (scales, cs, cn, own_cs, own_cn, own_ids, finv, sinv, mid, own_panels, sel)],
        out_specs=pl.BlockSpec((out_rows, tile // 128, 128), lambda i: (0, i, 0)),
        out_shape=jax.ShapeDtypeStruct((out_rows, grid_rows // 128, 128), jnp.float32),
    )(consts, gathered, pid, scales, cs, cn, own_cs, own_cn, own_ids, finv, sinv, mid, own_panels, sel)


def ridge_where(row_ids, col_ids, jitter):
    return jnp.where(row_ids[:, None] == col_ids[None, :], jitter, jnp.float32(0.0))


def gather_by_all_to_all(piece, axis_name):
    count = lax.axis_size(axis_name)
    copies = jnp.broadcast_to(piece[None], (count,) + piece.shape)
    return lax.all_to_all(copies, axis_name, 0, 0, tiled=True)


def on_device(points, feature_scales, amplitude, ridge):
    row_count = lax.axis_size("row")
    col_count = lax.axis_size("col")
    row = lax.axis_index("row")
    column = lax.axis_index("col")
    rows_one = points.shape[0]
    block_rows = rows_one // row_count
    col_blocks = SLAB // (BLK * col_count)
    panel_blocks = PANEL // (BLK * col_count)
    center_sources = SLAB // rows_one
    signal = amplitude[0]
    jitter = ridge[0]

    blocks = points.reshape(row_count, block_rows, FEAT)
    moved = lax.all_to_all(blocks, "row", 0, 0, tiled=True)

    point_count = rows_one * col_count
    point_ids = (
        lax.broadcasted_iota(jnp.int32, (point_count // block_rows, block_rows), 0) * row_count
        + row
    ) * block_rows + lax.broadcasted_iota(jnp.int32, (point_count // block_rows, block_rows), 1)
    point_ids = point_ids.reshape(1, point_count)
    select = jnp.where(
        lax.broadcasted_iota(jnp.int32, (BLK, PANEL), 1)
        == column * BLK + lax.broadcasted_iota(jnp.int32, (BLK, PANEL), 0),
        1.0,
        0.0,
    ).astype(jnp.bfloat16)
    consts = jnp.stack([signal, jitter])
    flat_slot = moved[0].reshape(1, -1)
    first_slot = lax.all_to_all(
        jnp.broadcast_to(flat_slot, (col_count, flat_slot.shape[1])), "col", 0, 0, tiled=True
    )[:center_sources].reshape(1, -1)
    center_grid = lax.all_to_all(
        jnp.broadcast_to(first_slot, (row_count, first_slot.shape[1])), "row", 0, 0, tiled=True
    ).reshape(row_count, center_sources, block_rows, FEAT)
    point_ids, select, consts, center_grid = lax.optimization_barrier(
        (point_ids, select, consts, center_grid)
    )
    centers = center_grid.transpose(1, 0, 2, 3).reshape(SLAB, FEAT)

    moved, centers = lax.optimization_barrier((moved, centers))
    gathered = lax.all_gather(moved, "col", axis=0, tiled=False)
    grid_rows = gathered.shape[0] * gathered.shape[1] * block_rows

    center_scaled = centers * feature_scales
    center_norms = jnp.sum(center_scaled * center_scaled, axis=1)


    own_ids = (
        (
            lax.broadcasted_iota(jnp.int32, (col_blocks, BLK), 0) * col_count + column
        )
        * BLK
        + lax.broadcasted_iota(jnp.int32, (col_blocks, BLK), 1)
    )[2 * panel_blocks :].reshape(-1)
    own_scaled = jnp.take(center_scaled, own_ids, axis=0)
    own_norms = jnp.take(center_norms, own_ids, axis=0)

    lead_ids = jnp.arange(PANEL, dtype=jnp.int32)
    k11 = kernel_block(
        center_scaled[:PANEL], center_norms[:PANEL], center_scaled[:PANEL], center_norms[:PANEL], signal
    ) + ridge_where(lead_ids, lead_ids, jitter)
    used_ids = jnp.concatenate([jnp.arange(PANEL, 2 * PANEL, dtype=jnp.int32), own_ids])
    used_scaled = jnp.concatenate([center_scaled[PANEL : 2 * PANEL], own_scaled])
    used_norms = jnp.concatenate([center_norms[PANEL : 2 * PANEL], own_norms])
    used_kernel = kernel_block(
        used_scaled, used_norms, center_scaled[: 2 * PANEL], center_norms[: 2 * PANEL], signal
    ) + ridge_where(used_ids, jnp.arange(2 * PANEL, dtype=jnp.int32), jitter)
    first_inverse, second_inverse, first_mid, own_panels = factor_centers(k11, used_kernel)

    finished = panel_stage(
        consts,
        gathered,
        point_ids,
        feature_scales.reshape(1, FEAT),
        pack_left(center_scaled[: 2 * PANEL]),
        center_norms[: 2 * PANEL].reshape(-1, 1),
        pack_left(own_scaled),
        own_norms.reshape(-1, 1),
        own_ids.reshape(-1, 1),
        first_inverse,
        second_inverse,
        first_mid,
        own_panels,
        select,
    )
    return finished.reshape(col_blocks, 1, BLK, 1, grid_rows)


def solution(mesh):
    placed = (P(("row", "col"), None), P(), P(), P())
    return jax.shard_map(
        on_device,
        mesh=mesh,
        in_specs=placed,
        out_specs=P(None, "col", None, "row", None),
        check_vma=False,
    )
```

```python
import jax
import jax.numpy as jnp
from jax import lax
from jax.sharding import PartitionSpec as P
from jax.experimental import pallas as pl
from jax.experimental.pallas import tpu as pltpu

FEAT = 64
SLAB = 1536
PANEL = 256
BLK = 16

HIGHEST = lax.Precision.HIGHEST
PHASES = 8


def kernel_block(left, left_norms, right, right_norms, signal):
    cross = jnp.dot(left, right.T, precision=HIGHEST, preferred_element_type=jnp.float32)
    return signal * jnp.exp(-0.5 * (left_norms[:, None] + right_norms[None, :] - 2.0 * cross))


def _nt(left, right):
    return lax.dot_general(
        left, right, (((1,), (1,)), ((), ())), precision=HIGHEST, preferred_element_type=jnp.float32
    )


def lower_inverse_body(block, s_ref, x_ref):
    half = block.shape[0] // 2
    lane_row = lax.broadcasted_iota(jnp.int32, (1, half), 1)
    eye = jnp.where(
        lax.broadcasted_iota(jnp.int32, (half, half), 0)
        == lax.broadcasted_iota(jnp.int32, (half, half), 1),
        1.0,
        0.0,
    )

    def pick(values, index):
        return jnp.sum(jnp.where(lane_row == index, values, 0.0), axis=1, keepdims=True)

    def make_step(top):
        count = half - top
        lanes = lax.broadcasted_iota(jnp.int32, (count, half), 1)
        rows = lax.broadcasted_iota(jnp.int32, (count, 1), 0) + top

        def step(j, carry):
            k = 2 * j
            s = s_ref[top:, :]
            x = x_ref[top:, :]
            row0 = s_ref[pl.ds(k, 1), :]
            row1 = s_ref[pl.ds(k + 1, 1), :]
            col0 = jnp.sum(jnp.where(lanes == k, s, 0.0), axis=1, keepdims=True)
            col1 = jnp.sum(jnp.where(lanes == k + 1, s, 0.0), axis=1, keepdims=True)
            root0 = jnp.sqrt(pick(row0, k))
            cross = pick(row1, k) / root0
            root1 = jnp.sqrt(pick(row1, k + 1) - cross * cross)
            col0 = jnp.where(rows >= k, col0 / root0, 0.0)
            row0 = jnp.where(lane_row >= k, row0 / root0, 0.0)
            col1 = jnp.where(rows >= k + 1, (col1 - col0 * cross) / root1, 0.0)
            row1 = jnp.where(lane_row >= k + 1, (row1 - cross * row0) / root1, 0.0)
            s_ref[top:, :] = s - col0 * row0 - col1 * row1
            x0 = x_ref[pl.ds(k, 1), :] / root0
            x1 = (x_ref[pl.ds(k + 1, 1), :] - cross * x0) / root1
            rest = x - jnp.where(rows > k, col0, 0.0) * x0 - jnp.where(rows > k + 1, col1, 0.0) * x1
            x_ref[top:, :] = jnp.where(rows == k, x0, jnp.where(rows == k + 1, x1, rest))
            return carry

        return step

    def base(block):
        s_ref[...] = block
        x_ref[...] = eye.astype(jnp.float32)
        span = half // PHASES
        for phase in range(PHASES):
            lax.fori_loop(phase * span // 2, (phase + 1) * span // 2, make_step(phase * span), 0)
        return x_ref[...]

    first = base(block[:half, :half])
    lower = _nt(block[half:, :half], first)
    schur = block[half:, half:] - _nt(lower, lower)
    second = base((schur + schur.T) * 0.5)
    below = -jnp.dot(
        second,
        jnp.dot(lower, first, precision=HIGHEST, preferred_element_type=jnp.float32),
        precision=HIGHEST,
        preferred_element_type=jnp.float32,
    )
    top = jnp.concatenate([first, jnp.zeros((half, half), jnp.float32)], axis=1)
    return jnp.concatenate([top, jnp.concatenate([below, second], axis=1)], axis=0)


def factor_kernel(lead_ref, used_ref, finv_ref, sinv_ref, mid_ref, own_ref, s_ref, x_ref):
    first_inverse = lower_inverse_body(lead_ref[...], s_ref, x_ref)
    finv_ref[...] = first_inverse
    used = used_ref[...]
    panel = first_inverse.shape[0]
    center_first = _nt(used[:, :panel], first_inverse).astype(jnp.bfloat16)
    first_mid = center_first[:panel]
    mid_ref[...] = first_mid
    center_second = used[:, panel:] - lax.dot_general(
        center_first, first_mid, (((1,), (1,)), ((), ())), preferred_element_type=jnp.float32
    )
    block = center_second[:panel]
    second_inverse = lower_inverse_body((block + block.T) * 0.5, s_ref, x_ref)
    sinv_ref[...] = second_inverse
    second_own = _nt(center_second[panel:], second_inverse).astype(jnp.bfloat16)
    own_ref[...] = jnp.concatenate([center_first[panel:], second_own], axis=1)


def factor_centers(lead, used):
    panel = lead.shape[0]
    half = panel // 2
    own_rows = used.shape[0] - panel
    return pl.pallas_call(
        factor_kernel,
        out_shape=(
            jax.ShapeDtypeStruct((panel, panel), jnp.float32),
            jax.ShapeDtypeStruct((panel, panel), jnp.float32),
            jax.ShapeDtypeStruct((panel, panel), jnp.bfloat16),
            jax.ShapeDtypeStruct((own_rows, 2 * panel), jnp.bfloat16),
        ),
        scratch_shapes=[pltpu.VMEM((half, half), jnp.float32), pltpu.VMEM((half, half), jnp.float32)],
    )((lead + lead.T) * 0.5, used)


def split_three(values):
    high = values.astype(jnp.bfloat16)
    rest = values - high.astype(jnp.float32)
    middle = rest.astype(jnp.bfloat16)
    low = (rest - middle.astype(jnp.float32)).astype(jnp.bfloat16)
    return high, middle, low


def pack_left(values):
    high = lax.reduce_precision(values, exponent_bits=8, mantissa_bits=7)
    rest = values - high
    middle = lax.reduce_precision(rest, exponent_bits=8, mantissa_bits=7)
    low = rest - middle
    high, middle, low = (piece.astype(jnp.bfloat16) for piece in (high, middle, low))
    return jnp.concatenate([high, high, middle, high, low, middle], axis=1)


def panel_kernel(
    consts_ref, pts_ref, pid_ref, scales_ref, cs_ref, cn_ref, own_cs_ref, own_cn_ref,
    own_ids_ref, finv_ref, sinv_ref, mid_ref, own_panels_ref, sel_ref, out_ref,
):
    signal = consts_ref[0]
    jitter = consts_ref[1]
    points = jnp.concatenate(
        [pts_ref[:, part].reshape(-1, FEAT) for part in range(pts_ref.shape[1])], axis=0
    )
    scaled = (points * scales_ref[...]).T
    high, middle, low = split_three(scaled)
    packed = jnp.concatenate([high, middle, high, low, high, middle], axis=0)
    pnorm = jnp.sum(scaled * scaled, axis=0, keepdims=True)
    pid = pid_ref[...]
    cross = jnp.dot(cs_ref[...], packed, preferred_element_type=jnp.float32)
    values = signal * jnp.exp(-0.5 * (cn_ref[...] + pnorm - 2.0 * cross))
    head = values[:, :128] + jnp.where(
        lax.broadcasted_iota(jnp.int32, (values.shape[0], 128), 0) == pid[:, :128], jitter, jnp.float32(0.0)
    )
    values = jnp.concatenate([head, values[:, 128:]], axis=1)
    first = jnp.dot(
        finv_ref[...], values[:PANEL], precision=HIGHEST, preferred_element_type=jnp.float32
    ).astype(jnp.bfloat16)
    reduced = values[PANEL:] - jnp.dot(mid_ref[...], first, preferred_element_type=jnp.float32)
    second = jnp.dot(
        sinv_ref[...], reduced, precision=HIGHEST, preferred_element_type=jnp.float32
    ).astype(jnp.bfloat16)
    own_cross = jnp.dot(own_cs_ref[...], packed, preferred_element_type=jnp.float32)
    own = signal * jnp.exp(-0.5 * (own_cn_ref[...] + pnorm - 2.0 * own_cross))
    own_head = own[:, :256] + jnp.where(own_ids_ref[...] == pid[:, :256], jitter, jnp.float32(0.0))
    own = jnp.concatenate([own_head, own[:, 256:]], axis=1)
    both = jnp.concatenate([first, second], axis=0)
    trailing = own - jnp.dot(own_panels_ref[...], both, preferred_element_type=jnp.float32)
    sel = sel_ref[...]
    result = jnp.concatenate(
        [
            jnp.dot(sel, first, preferred_element_type=jnp.float32),
            jnp.dot(sel, second, preferred_element_type=jnp.float32),
            trailing,
        ],
        axis=0,
    )
    lanes = out_ref.shape[2]
    for chunk in range(out_ref.shape[1]):
        out_ref[:, chunk, :] = result[:, chunk * lanes : (chunk + 1) * lanes]


def panel_stage(consts, gathered, pid, scales, cs, cn, own_cs, own_cn, own_ids, finv, sinv, mid, own_panels, sel):
    col_count, row_count, block_rows, _ = gathered.shape
    parts = 2
    tile = col_count * block_rows * parts
    grid_rows = col_count * block_rows * row_count
    out_rows = 2 * BLK + own_cs.shape[0]

    def whole(array):
        return pl.BlockSpec(array.shape, lambda i: (0,) * array.ndim)

    return pl.pallas_call(
        panel_kernel,
        grid=(row_count // parts,),
        in_specs=[
            pl.BlockSpec(memory_space=pltpu.SMEM),
            pl.BlockSpec((col_count, parts, block_rows, FEAT), lambda i: (0, i, 0, 0)),
            pl.BlockSpec((1, tile), lambda i: (0, i)),
        ]
        + [whole(a) for a in (scales, cs, cn, own_cs, own_cn, own_ids, finv, sinv, mid, own_panels, sel)],
        out_specs=pl.BlockSpec((out_rows, tile // 128, 128), lambda i: (0, i, 0)),
        out_shape=jax.ShapeDtypeStruct((out_rows, grid_rows // 128, 128), jnp.float32),
    )(consts, gathered, pid, scales, cs, cn, own_cs, own_cn, own_ids, finv, sinv, mid, own_panels, sel)


def ridge_where(row_ids, col_ids, jitter):
    return jnp.where(row_ids[:, None] == col_ids[None, :], jitter, jnp.float32(0.0))


def gather_by_all_to_all(piece, axis_name):
    count = lax.axis_size(axis_name)
    copies = jnp.broadcast_to(piece[None], (count,) + piece.shape)
    return lax.all_to_all(copies, axis_name, 0, 0, tiled=True)


def on_device(points, feature_scales, amplitude, ridge):
    row_count = lax.axis_size("row")
    col_count = lax.axis_size("col")
    row = lax.axis_index("row")
    column = lax.axis_index("col")
    rows_one = points.shape[0]
    block_rows = rows_one // row_count
    col_blocks = SLAB // (BLK * col_count)
    panel_blocks = PANEL // (BLK * col_count)
    center_sources = SLAB // rows_one
    signal = amplitude[0]
    jitter = ridge[0]

    blocks = points.reshape(row_count, block_rows * FEAT)
    moved_flat = lax.all_to_all(blocks, "row", 0, 0, tiled=True)
    moved = moved_flat.reshape(row_count, block_rows, FEAT)

    flat_slot = moved_flat[:1]
    first_slot = lax.all_to_all(
        jnp.broadcast_to(flat_slot, (col_count, flat_slot.shape[1])), "col", 0, 0, tiled=True
    )[:center_sources].reshape(1, -1)
    center_grid = lax.all_to_all(
        jnp.broadcast_to(first_slot, (row_count, first_slot.shape[1])), "row", 0, 0, tiled=True
    ).reshape(row_count, center_sources, block_rows, FEAT)
    centers = center_grid.transpose(1, 0, 2, 3).reshape(SLAB, FEAT)

    moved, centers = lax.optimization_barrier((moved, centers))
    gathered = lax.all_gather(moved, "col", axis=0, tiled=False)
    grid_rows = gathered.shape[0] * gathered.shape[1] * block_rows

    center_scaled = centers * feature_scales
    center_norms = jnp.sum(center_scaled * center_scaled, axis=1)

    point_ids = (
        lax.broadcasted_iota(jnp.int32, (grid_rows // block_rows, block_rows), 0) * row_count
        + row
    ) * block_rows + lax.broadcasted_iota(jnp.int32, (grid_rows // block_rows, block_rows), 1)
    point_ids = point_ids.reshape(1, grid_rows)

    own_ids = (
        (
            lax.broadcasted_iota(jnp.int32, (col_blocks, BLK), 0) * col_count + column
        )
        * BLK
        + lax.broadcasted_iota(jnp.int32, (col_blocks, BLK), 1)
    )[2 * panel_blocks :].reshape(-1)
    own_scaled = jnp.take(center_scaled, own_ids, axis=0)
    own_norms = jnp.take(center_norms, own_ids, axis=0)

    lead_ids = jnp.arange(PANEL, dtype=jnp.int32)
    k11 = kernel_block(
        center_scaled[:PANEL], center_norms[:PANEL], center_scaled[:PANEL], center_norms[:PANEL], signal
    ) + ridge_where(lead_ids, lead_ids, jitter)
    used_ids = jnp.concatenate([jnp.arange(PANEL, 2 * PANEL, dtype=jnp.int32), own_ids])
    used_scaled = jnp.concatenate([center_scaled[PANEL : 2 * PANEL], own_scaled])
    used_norms = jnp.concatenate([center_norms[PANEL : 2 * PANEL], own_norms])
    used_kernel = kernel_block(
        used_scaled, used_norms, center_scaled[: 2 * PANEL], center_norms[: 2 * PANEL], signal
    ) + ridge_where(used_ids, jnp.arange(2 * PANEL, dtype=jnp.int32), jitter)
    first_inverse, second_inverse, first_mid, own_panels = factor_centers(k11, used_kernel)

    select = jnp.where(
        lax.broadcasted_iota(jnp.int32, (BLK, PANEL), 1)
        == column * BLK + lax.broadcasted_iota(jnp.int32, (BLK, PANEL), 0),
        1.0,
        0.0,
    ).astype(jnp.bfloat16)
    consts = jnp.stack([signal, jitter])
    finished = panel_stage(
        consts,
        gathered,
        point_ids,
        feature_scales.reshape(1, FEAT),
        pack_left(center_scaled[: 2 * PANEL]),
        center_norms[: 2 * PANEL].reshape(-1, 1),
        pack_left(own_scaled),
        own_norms.reshape(-1, 1),
        own_ids.reshape(-1, 1),
        first_inverse,
        second_inverse,
        first_mid,
        own_panels,
        select,
    )
    return finished.reshape(col_blocks, 1, BLK, 1, grid_rows)


def solution(mesh):
    placed = (P(("row", "col"), None), P(), P(), P())
    return jax.shard_map(
        on_device,
        mesh=mesh,
        in_specs=placed,
        out_specs=P(None, "col", None, "row", None),
        check_vma=False,
    )
```

```python
import jax
import jax.numpy as jnp
from jax import lax
from jax.sharding import PartitionSpec as P
from jax.experimental import pallas as pl
from jax.experimental.pallas import tpu as pltpu

FEAT = 64
SLAB = 1536
PANEL = 256
BLK = 16

HIGHEST = lax.Precision.HIGHEST
PHASES = 16


def kernel_block(left, left_norms, right, right_norms, signal):
    cross = jnp.dot(left, right.T, precision=HIGHEST, preferred_element_type=jnp.float32)
    return signal * jnp.exp(-0.5 * (left_norms[:, None] + right_norms[None, :] - 2.0 * cross))


def _nt(left, right):
    return lax.dot_general(
        left, right, (((1,), (1,)), ((), ())), precision=HIGHEST, preferred_element_type=jnp.float32
    )


def lower_inverse_body(block, s_ref, x_ref):
    half = block.shape[0] // 2
    lane_row = lax.broadcasted_iota(jnp.int32, (1, half), 1)
    eye = jnp.where(
        lax.broadcasted_iota(jnp.int32, (half, half), 0)
        == lax.broadcasted_iota(jnp.int32, (half, half), 1),
        1.0,
        0.0,
    )

    def pick(values, index):
        return jnp.sum(jnp.where(lane_row == index, values, 0.0), axis=1, keepdims=True)

    def make_step(top):
        count = half - top
        lanes = lax.broadcasted_iota(jnp.int32, (count, half), 1)
        rows = lax.broadcasted_iota(jnp.int32, (count, 1), 0) + top

        def step(j, carry):
            k = 2 * j
            s = s_ref[top:, :]
            x = x_ref[top:, :]
            row0 = s_ref[pl.ds(k, 1), :]
            row1 = s_ref[pl.ds(k + 1, 1), :]
            col0 = jnp.sum(jnp.where(lanes == k, s, 0.0), axis=1, keepdims=True)
            col1 = jnp.sum(jnp.where(lanes == k + 1, s, 0.0), axis=1, keepdims=True)
            root0 = jnp.sqrt(pick(row0, k))
            cross = pick(row1, k) / root0
            root1 = jnp.sqrt(pick(row1, k + 1) - cross * cross)
            col0 = jnp.where(rows >= k, col0 / root0, 0.0)
            row0 = jnp.where(lane_row >= k, row0 / root0, 0.0)
            col1 = jnp.where(rows >= k + 1, (col1 - col0 * cross) / root1, 0.0)
            row1 = jnp.where(lane_row >= k + 1, (row1 - cross * row0) / root1, 0.0)
            s_ref[top:, :] = s - col0 * row0 - col1 * row1
            x0 = x_ref[pl.ds(k, 1), :] / root0
            x1 = (x_ref[pl.ds(k + 1, 1), :] - cross * x0) / root1
            rest = x - jnp.where(rows > k, col0, 0.0) * x0 - jnp.where(rows > k + 1, col1, 0.0) * x1
            x_ref[top:, :] = jnp.where(rows == k, x0, jnp.where(rows == k + 1, x1, rest))
            return carry

        return step

    def base(block):
        s_ref[...] = block
        x_ref[...] = eye.astype(jnp.float32)
        span = half // PHASES
        for phase in range(PHASES):
            lax.fori_loop(phase * span // 2, (phase + 1) * span // 2, make_step(phase * span), 0)
        return x_ref[...]

    first = base(block[:half, :half])
    lower = _nt(block[half:, :half], first)
    schur = block[half:, half:] - _nt(lower, lower)
    second = base((schur + schur.T) * 0.5)
    below = -jnp.dot(
        second,
        jnp.dot(lower, first, precision=HIGHEST, preferred_element_type=jnp.float32),
        precision=HIGHEST,
        preferred_element_type=jnp.float32,
    )
    top = jnp.concatenate([first, jnp.zeros((half, half), jnp.float32)], axis=1)
    return jnp.concatenate([top, jnp.concatenate([below, second], axis=1)], axis=0)


def factor_kernel(lead_ref, used_ref, finv_ref, sinv_ref, mid_ref, own_ref, s_ref, x_ref):
    first_inverse = lower_inverse_body(lead_ref[...], s_ref, x_ref)
    finv_ref[...] = first_inverse
    used = used_ref[...]
    panel = first_inverse.shape[0]
    center_first = _nt(used[:, :panel], first_inverse).astype(jnp.bfloat16)
    first_mid = center_first[:panel]
    mid_ref[...] = first_mid
    center_second = used[:, panel:] - lax.dot_general(
        center_first, first_mid, (((1,), (1,)), ((), ())), preferred_element_type=jnp.float32
    )
    block = center_second[:panel]
    second_inverse = lower_inverse_body((block + block.T) * 0.5, s_ref, x_ref)
    sinv_ref[...] = second_inverse
    second_own = _nt(center_second[panel:], second_inverse).astype(jnp.bfloat16)
    own_ref[...] = jnp.concatenate([center_first[panel:], second_own], axis=1)


def factor_centers(lead, used):
    panel = lead.shape[0]
    half = panel // 2
    own_rows = used.shape[0] - panel
    return pl.pallas_call(
        factor_kernel,
        out_shape=(
            jax.ShapeDtypeStruct((panel, panel), jnp.float32),
            jax.ShapeDtypeStruct((panel, panel), jnp.float32),
            jax.ShapeDtypeStruct((panel, panel), jnp.bfloat16),
            jax.ShapeDtypeStruct((own_rows, 2 * panel), jnp.bfloat16),
        ),
        scratch_shapes=[pltpu.VMEM((half, half), jnp.float32), pltpu.VMEM((half, half), jnp.float32)],
    )((lead + lead.T) * 0.5, used)


def split_three(values):
    high = values.astype(jnp.bfloat16)
    rest = values - high.astype(jnp.float32)
    middle = rest.astype(jnp.bfloat16)
    low = (rest - middle.astype(jnp.float32)).astype(jnp.bfloat16)
    return high, middle, low


def pack_left(values):
    high = lax.reduce_precision(values, exponent_bits=8, mantissa_bits=7)
    rest = values - high
    middle = lax.reduce_precision(rest, exponent_bits=8, mantissa_bits=7)
    low = rest - middle
    high, middle, low = (piece.astype(jnp.bfloat16) for piece in (high, middle, low))
    return jnp.concatenate([high, high, middle, high, low, middle], axis=1)


def panel_kernel(
    consts_ref, pts_ref, pid_ref, scales_ref, cs_ref, cn_ref, own_cs_ref, own_cn_ref,
    own_ids_ref, finv_ref, sinv_ref, mid_ref, own_panels_ref, sel_ref, out_ref,
):
    signal = consts_ref[0]
    jitter = consts_ref[1]
    points = jnp.concatenate(
        [pts_ref[:, part].reshape(-1, FEAT) for part in range(pts_ref.shape[1])], axis=0
    )
    scaled = (points * scales_ref[...]).T
    high, middle, low = split_three(scaled)
    packed = jnp.concatenate([high, middle, high, low, high, middle], axis=0)
    pnorm = jnp.sum(scaled * scaled, axis=0, keepdims=True)
    pid = pid_ref[...]
    cross = jnp.dot(cs_ref[...], packed, preferred_element_type=jnp.float32)
    values = signal * jnp.exp(-0.5 * (cn_ref[...] + pnorm - 2.0 * cross))
    head = values[:, :128] + jnp.where(
        lax.broadcasted_iota(jnp.int32, (values.shape[0], 128), 0) == pid[:, :128], jitter, jnp.float32(0.0)
    )
    values = jnp.concatenate([head, values[:, 128:]], axis=1)
    first = jnp.dot(
        finv_ref[...], values[:PANEL], precision=HIGHEST, preferred_element_type=jnp.float32
    ).astype(jnp.bfloat16)
    reduced = values[PANEL:] - jnp.dot(mid_ref[...], first, preferred_element_type=jnp.float32)
    second = jnp.dot(
        sinv_ref[...], reduced, precision=HIGHEST, preferred_element_type=jnp.float32
    ).astype(jnp.bfloat16)
    own_cross = jnp.dot(own_cs_ref[...], packed, preferred_element_type=jnp.float32)
    own = signal * jnp.exp(-0.5 * (own_cn_ref[...] + pnorm - 2.0 * own_cross))
    own_head = own[:, :256] + jnp.where(own_ids_ref[...] == pid[:, :256], jitter, jnp.float32(0.0))
    own = jnp.concatenate([own_head, own[:, 256:]], axis=1)
    both = jnp.concatenate([first, second], axis=0)
    trailing = own - jnp.dot(own_panels_ref[...], both, preferred_element_type=jnp.float32)
    sel = sel_ref[...]
    result = jnp.concatenate(
        [
            jnp.dot(sel, first, preferred_element_type=jnp.float32),
            jnp.dot(sel, second, preferred_element_type=jnp.float32),
            trailing,
        ],
        axis=0,
    )
    lanes = out_ref.shape[2]
    for chunk in range(out_ref.shape[1]):
        out_ref[:, chunk, :] = result[:, chunk * lanes : (chunk + 1) * lanes]


def panel_stage(consts, gathered, pid, scales, cs, cn, own_cs, own_cn, own_ids, finv, sinv, mid, own_panels, sel):
    col_count, row_count, block_rows, _ = gathered.shape
    parts = 2
    tile = col_count * block_rows * parts
    grid_rows = col_count * block_rows * row_count
    out_rows = 2 * BLK + own_cs.shape[0]

    def whole(array):
        return pl.BlockSpec(array.shape, lambda i: (0,) * array.ndim)

    return pl.pallas_call(
        panel_kernel,
        grid=(row_count // parts,),
        in_specs=[
            pl.BlockSpec(memory_space=pltpu.SMEM),
            pl.BlockSpec((col_count, parts, block_rows, FEAT), lambda i: (0, i, 0, 0)),
            pl.BlockSpec((1, tile), lambda i: (0, i)),
        ]
        + [whole(a) for a in (scales, cs, cn, own_cs, own_cn, own_ids, finv, sinv, mid, own_panels, sel)],
        out_specs=pl.BlockSpec((out_rows, tile // 128, 128), lambda i: (0, i, 0)),
        out_shape=jax.ShapeDtypeStruct((out_rows, grid_rows // 128, 128), jnp.float32),
    )(consts, gathered, pid, scales, cs, cn, own_cs, own_cn, own_ids, finv, sinv, mid, own_panels, sel)


def ridge_where(row_ids, col_ids, jitter):
    return jnp.where(row_ids[:, None] == col_ids[None, :], jitter, jnp.float32(0.0))


def gather_by_all_to_all(piece, axis_name):
    count = lax.axis_size(axis_name)
    copies = jnp.broadcast_to(piece[None], (count,) + piece.shape)
    return lax.all_to_all(copies, axis_name, 0, 0, tiled=True)


def on_device(points, feature_scales, amplitude, ridge):
    row_count = lax.axis_size("row")
    col_count = lax.axis_size("col")
    row = lax.axis_index("row")
    column = lax.axis_index("col")
    rows_one = points.shape[0]
    block_rows = rows_one // row_count
    col_blocks = SLAB // (BLK * col_count)
    panel_blocks = PANEL // (BLK * col_count)
    center_sources = SLAB // rows_one
    signal = amplitude[0]
    jitter = ridge[0]

    blocks = points.reshape(row_count, block_rows * FEAT)
    moved_flat = lax.all_to_all(blocks, "row", 0, 0, tiled=True)
    moved = moved_flat.reshape(row_count, block_rows, FEAT)

    flat_slot = moved_flat[:1]
    first_slot = lax.all_to_all(
        jnp.broadcast_to(flat_slot, (col_count, flat_slot.shape[1])), "col", 0, 0, tiled=True
    )[:center_sources].reshape(1, -1)
    center_grid = lax.all_to_all(
        jnp.broadcast_to(first_slot, (row_count, first_slot.shape[1])), "row", 0, 0, tiled=True
    ).reshape(row_count, center_sources, block_rows, FEAT)
    centers = center_grid.transpose(1, 0, 2, 3).reshape(SLAB, FEAT)

    moved, centers = lax.optimization_barrier((moved, centers))
    gathered = lax.all_gather(moved, "col", axis=0, tiled=False)
    grid_rows = gathered.shape[0] * gathered.shape[1] * block_rows

    center_scaled = centers * feature_scales
    center_norms = jnp.sum(center_scaled * center_scaled, axis=1)

    point_ids = (
        lax.broadcasted_iota(jnp.int32, (grid_rows // block_rows, block_rows), 0) * row_count
        + row
    ) * block_rows + lax.broadcasted_iota(jnp.int32, (grid_rows // block_rows, block_rows), 1)
    point_ids = point_ids.reshape(1, grid_rows)

    own_ids = (
        (
            lax.broadcasted_iota(jnp.int32, (col_blocks, BLK), 0) * col_count + column
        )
        * BLK
        + lax.broadcasted_iota(jnp.int32, (col_blocks, BLK), 1)
    )[2 * panel_blocks :].reshape(-1)
    own_scaled = jnp.take(center_scaled, own_ids, axis=0)
    own_norms = jnp.take(center_norms, own_ids, axis=0)

    lead_ids = jnp.arange(PANEL, dtype=jnp.int32)
    k11 = kernel_block(
        center_scaled[:PANEL], center_norms[:PANEL], center_scaled[:PANEL], center_norms[:PANEL], signal
    ) + ridge_where(lead_ids, lead_ids, jitter)
    used_ids = jnp.concatenate([jnp.arange(PANEL, 2 * PANEL, dtype=jnp.int32), own_ids])
    used_scaled = jnp.concatenate([center_scaled[PANEL : 2 * PANEL], own_scaled])
    used_norms = jnp.concatenate([center_norms[PANEL : 2 * PANEL], own_norms])
    used_kernel = kernel_block(
        used_scaled, used_norms, center_scaled[: 2 * PANEL], center_norms[: 2 * PANEL], signal
    ) + ridge_where(used_ids, jnp.arange(2 * PANEL, dtype=jnp.int32), jitter)
    first_inverse, second_inverse, first_mid, own_panels = factor_centers(k11, used_kernel)

    select = jnp.where(
        lax.broadcasted_iota(jnp.int32, (BLK, PANEL), 1)
        == column * BLK + lax.broadcasted_iota(jnp.int32, (BLK, PANEL), 0),
        1.0,
        0.0,
    ).astype(jnp.bfloat16)
    consts = jnp.stack([signal, jitter])
    finished = panel_stage(
        consts,
        gathered,
        point_ids,
        feature_scales.reshape(1, FEAT),
        pack_left(center_scaled[: 2 * PANEL]),
        center_norms[: 2 * PANEL].reshape(-1, 1),
        pack_left(own_scaled),
        own_norms.reshape(-1, 1),
        own_ids.reshape(-1, 1),
        first_inverse,
        second_inverse,
        first_mid,
        own_panels,
        select,
    )
    return finished.reshape(col_blocks, 1, BLK, 1, grid_rows)


def solution(mesh):
    placed = (P(("row", "col"), None), P(), P(), P())
    return jax.shard_map(
        on_device,
        mesh=mesh,
        in_specs=placed,
        out_specs=P(None, "col", None, "row", None),
        check_vma=False,
    )
```

```python
import jax
import jax.numpy as jnp
from jax import lax
from jax.sharding import PartitionSpec as P
from jax.experimental import pallas as pl
from jax.experimental.pallas import tpu as pltpu

FEAT = 64
SLAB = 1536
PANEL = 256
BLK = 16

HIGHEST = lax.Precision.HIGHEST
PHASES = 8


def kernel_block(left, left_norms, right, right_norms, signal):
    cross = jnp.dot(left, right.T, precision=HIGHEST, preferred_element_type=jnp.float32)
    return signal * jnp.exp(-0.5 * (left_norms[:, None] + right_norms[None, :] - 2.0 * cross))


def _nt(left, right):
    return lax.dot_general(
        left, right, (((1,), (1,)), ((), ())), precision=HIGHEST, preferred_element_type=jnp.float32
    )


def lower_inverse_body(block, s_ref, x_ref):
    half = block.shape[0] // 2
    lane_row = lax.broadcasted_iota(jnp.int32, (1, half), 1)
    eye = jnp.where(
        lax.broadcasted_iota(jnp.int32, (half, half), 0)
        == lax.broadcasted_iota(jnp.int32, (half, half), 1),
        1.0,
        0.0,
    )

    def pick(values, index):
        return jnp.sum(jnp.where(lane_row == index, values, 0.0), axis=1, keepdims=True)

    def make_step(top):
        count = half - top
        lanes = lax.broadcasted_iota(jnp.int32, (count, half), 1)
        rows = lax.broadcasted_iota(jnp.int32, (count, 1), 0) + top

        def step(j, carry):
            k = 2 * j
            s = s_ref[top:, :]
            x = x_ref[top:, :]
            row0 = s_ref[pl.ds(k, 1), :]
            row1 = s_ref[pl.ds(k + 1, 1), :]
            col0 = jnp.sum(jnp.where(lanes == k, s, 0.0), axis=1, keepdims=True)
            col1 = jnp.sum(jnp.where(lanes == k + 1, s, 0.0), axis=1, keepdims=True)
            root0 = jnp.sqrt(pick(row0, k))
            cross = pick(row1, k) / root0
            root1 = jnp.sqrt(pick(row1, k + 1) - cross * cross)
            col0 = jnp.where(rows >= k, col0 / root0, 0.0)
            row0 = jnp.where(lane_row >= k, row0 / root0, 0.0)
            col1 = jnp.where(rows >= k + 1, (col1 - col0 * cross) / root1, 0.0)
            row1 = jnp.where(lane_row >= k + 1, (row1 - cross * row0) / root1, 0.0)
            s_ref[top:, :] = s - col0 * row0 - col1 * row1
            x0 = x_ref[pl.ds(k, 1), :] / root0
            x1 = (x_ref[pl.ds(k + 1, 1), :] - cross * x0) / root1
            rest = x - jnp.where(rows > k, col0, 0.0) * x0 - jnp.where(rows > k + 1, col1, 0.0) * x1
            x_ref[top:, :] = jnp.where(rows == k, x0, jnp.where(rows == k + 1, x1, rest))
            return carry

        return step

    def base(block):
        s_ref[...] = block
        x_ref[...] = eye.astype(jnp.float32)
        span = half // PHASES
        for phase in range(PHASES):
            lax.fori_loop(phase * span // 2, (phase + 1) * span // 2, make_step(phase * span), 0)
        return x_ref[...]

    first = base(block[:half, :half])
    lower = _nt(block[half:, :half], first)
    schur = block[half:, half:] - _nt(lower, lower)
    second = base((schur + schur.T) * 0.5)
    below = -jnp.dot(
        second,
        jnp.dot(lower, first, precision=HIGHEST, preferred_element_type=jnp.float32),
        precision=HIGHEST,
        preferred_element_type=jnp.float32,
    )
    top = jnp.concatenate([first, jnp.zeros((half, half), jnp.float32)], axis=1)
    return jnp.concatenate([top, jnp.concatenate([below, second], axis=1)], axis=0)


def factor_kernel(block_ref, finv_ref, sinv_ref, mid_ref, own_ref, s_ref, x_ref):
    panel = finv_ref.shape[0]
    lead = block_ref[:panel, :panel]
    first_inverse = lower_inverse_body((lead + lead.T) * 0.5, s_ref, x_ref)
    finv_ref[...] = first_inverse
    used = block_ref[panel:, :]
    center_first = _nt(used[:, :panel], first_inverse).astype(jnp.bfloat16)
    first_mid = center_first[:panel]
    mid_ref[...] = first_mid
    center_second = used[:, panel:] - lax.dot_general(
        center_first, first_mid, (((1,), (1,)), ((), ())), preferred_element_type=jnp.float32
    )
    block = center_second[:panel]
    second_inverse = lower_inverse_body((block + block.T) * 0.5, s_ref, x_ref)
    sinv_ref[...] = second_inverse
    second_own = _nt(center_second[panel:], second_inverse).astype(jnp.bfloat16)
    own_ref[...] = jnp.concatenate([center_first[panel:], second_own], axis=1)


def factor_centers(block):
    panel = block.shape[1] // 2
    half = panel // 2
    own_rows = block.shape[0] - 2 * panel
    return pl.pallas_call(
        factor_kernel,
        out_shape=(
            jax.ShapeDtypeStruct((panel, panel), jnp.float32),
            jax.ShapeDtypeStruct((panel, panel), jnp.float32),
            jax.ShapeDtypeStruct((panel, panel), jnp.bfloat16),
            jax.ShapeDtypeStruct((own_rows, 2 * panel), jnp.bfloat16),
        ),
        scratch_shapes=[pltpu.VMEM((half, half), jnp.float32), pltpu.VMEM((half, half), jnp.float32)],
    )(block)


def split_three(values):
    high = values.astype(jnp.bfloat16)
    rest = values - high.astype(jnp.float32)
    middle = rest.astype(jnp.bfloat16)
    low = (rest - middle.astype(jnp.float32)).astype(jnp.bfloat16)
    return high, middle, low


def pack_left(values):
    high = lax.reduce_precision(values, exponent_bits=8, mantissa_bits=7)
    rest = values - high
    middle = lax.reduce_precision(rest, exponent_bits=8, mantissa_bits=7)
    low = rest - middle
    high, middle, low = (piece.astype(jnp.bfloat16) for piece in (high, middle, low))
    return jnp.concatenate([high, high, middle, high, low, middle], axis=1)


def panel_kernel(
    consts_ref, pts_ref, pid_ref, scales_ref, cs_ref, cn_ref, own_cs_ref, own_cn_ref,
    own_ids_ref, finv_ref, sinv_ref, mid_ref, own_panels_ref, sel_ref, out_ref,
):
    signal = consts_ref[0]
    jitter = consts_ref[1]
    points = jnp.concatenate(
        [pts_ref[:, part].reshape(-1, FEAT) for part in range(pts_ref.shape[1])], axis=0
    )
    scaled = (points * scales_ref[...]).T
    high, middle, low = split_three(scaled)
    packed = jnp.concatenate([high, middle, high, low, high, middle], axis=0)
    pnorm = jnp.sum(scaled * scaled, axis=0, keepdims=True)
    pid = pid_ref[...]
    cross = jnp.dot(cs_ref[...], packed, preferred_element_type=jnp.float32)
    values = signal * jnp.exp(-0.5 * (cn_ref[...] + pnorm - 2.0 * cross))
    head = values[:, :128] + jnp.where(
        lax.broadcasted_iota(jnp.int32, (values.shape[0], 128), 0) == pid[:, :128], jitter, jnp.float32(0.0)
    )
    values = jnp.concatenate([head, values[:, 128:]], axis=1)
    first = jnp.dot(
        finv_ref[...], values[:PANEL], precision=HIGHEST, preferred_element_type=jnp.float32
    ).astype(jnp.bfloat16)
    reduced = values[PANEL:] - jnp.dot(mid_ref[...], first, preferred_element_type=jnp.float32)
    second = jnp.dot(
        sinv_ref[...], reduced, precision=HIGHEST, preferred_element_type=jnp.float32
    ).astype(jnp.bfloat16)
    own_cross = jnp.dot(own_cs_ref[...], packed, preferred_element_type=jnp.float32)
    own = signal * jnp.exp(-0.5 * (own_cn_ref[...] + pnorm - 2.0 * own_cross))
    own_head = own[:, :256] + jnp.where(own_ids_ref[...] == pid[:, :256], jitter, jnp.float32(0.0))
    own = jnp.concatenate([own_head, own[:, 256:]], axis=1)
    both = jnp.concatenate([first, second], axis=0)
    trailing = own - jnp.dot(own_panels_ref[...], both, preferred_element_type=jnp.float32)
    sel = sel_ref[...]
    result = jnp.concatenate(
        [
            jnp.dot(sel, first, preferred_element_type=jnp.float32),
            jnp.dot(sel, second, preferred_element_type=jnp.float32),
            trailing,
        ],
        axis=0,
    )
    lanes = out_ref.shape[2]
    for chunk in range(out_ref.shape[1]):
        out_ref[:, chunk, :] = result[:, chunk * lanes : (chunk + 1) * lanes]


def panel_stage(consts, gathered, pid, scales, cs, cn, own_cs, own_cn, own_ids, finv, sinv, mid, own_panels, sel):
    col_count, row_count, block_rows, _ = gathered.shape
    parts = 2
    tile = col_count * block_rows * parts
    grid_rows = col_count * block_rows * row_count
    out_rows = 2 * BLK + own_cs.shape[0]

    def whole(array):
        return pl.BlockSpec(array.shape, lambda i: (0,) * array.ndim)

    return pl.pallas_call(
        panel_kernel,
        grid=(row_count // parts,),
        in_specs=[
            pl.BlockSpec(memory_space=pltpu.SMEM),
            pl.BlockSpec((col_count, parts, block_rows, FEAT), lambda i: (0, i, 0, 0)),
            pl.BlockSpec((1, tile), lambda i: (0, i)),
        ]
        + [whole(a) for a in (scales, cs, cn, own_cs, own_cn, own_ids, finv, sinv, mid, own_panels, sel)],
        out_specs=pl.BlockSpec((out_rows, tile // 128, 128), lambda i: (0, i, 0)),
        out_shape=jax.ShapeDtypeStruct((out_rows, grid_rows // 128, 128), jnp.float32),
    )(consts, gathered, pid, scales, cs, cn, own_cs, own_cn, own_ids, finv, sinv, mid, own_panels, sel)


def ridge_where(row_ids, col_ids, jitter):
    return jnp.where(row_ids[:, None] == col_ids[None, :], jitter, jnp.float32(0.0))


def gather_by_all_to_all(piece, axis_name):
    count = lax.axis_size(axis_name)
    copies = jnp.broadcast_to(piece[None], (count,) + piece.shape)
    return lax.all_to_all(copies, axis_name, 0, 0, tiled=True)


def on_device(points, feature_scales, amplitude, ridge):
    row_count = lax.axis_size("row")
    col_count = lax.axis_size("col")
    row = lax.axis_index("row")
    column = lax.axis_index("col")
    rows_one = points.shape[0]
    block_rows = rows_one // row_count
    col_blocks = SLAB // (BLK * col_count)
    panel_blocks = PANEL // (BLK * col_count)
    center_sources = SLAB // rows_one
    signal = amplitude[0]
    jitter = ridge[0]

    blocks = points.reshape(row_count, block_rows * FEAT)
    moved_flat = lax.all_to_all(blocks, "row", 0, 0, tiled=True)
    moved = moved_flat.reshape(row_count, block_rows, FEAT)

    flat_slot = moved_flat[:1]
    first_slot = lax.all_to_all(
        jnp.broadcast_to(flat_slot, (col_count, flat_slot.shape[1])), "col", 0, 0, tiled=True
    )[:center_sources].reshape(1, -1)
    center_grid = lax.all_to_all(
        jnp.broadcast_to(first_slot, (row_count, first_slot.shape[1])), "row", 0, 0, tiled=True
    ).reshape(row_count, center_sources, block_rows, FEAT)
    centers = center_grid.transpose(1, 0, 2, 3).reshape(SLAB, FEAT)

    moved, centers = lax.optimization_barrier((moved, centers))
    gathered = lax.all_gather(moved, "col", axis=0, tiled=False)
    grid_rows = gathered.shape[0] * gathered.shape[1] * block_rows

    center_scaled = centers * feature_scales
    center_norms = jnp.sum(center_scaled * center_scaled, axis=1)

    point_ids = (
        lax.broadcasted_iota(jnp.int32, (grid_rows // block_rows, block_rows), 0) * row_count
        + row
    ) * block_rows + lax.broadcasted_iota(jnp.int32, (grid_rows // block_rows, block_rows), 1)
    point_ids = point_ids.reshape(1, grid_rows)

    own_ids = (
        (
            lax.broadcasted_iota(jnp.int32, (col_blocks, BLK), 0) * col_count + column
        )
        * BLK
        + lax.broadcasted_iota(jnp.int32, (col_blocks, BLK), 1)
    )[2 * panel_blocks :].reshape(-1)
    own_scaled = jnp.take(center_scaled, own_ids, axis=0)
    own_norms = jnp.take(center_norms, own_ids, axis=0)

    used_ids = jnp.concatenate([jnp.arange(2 * PANEL, dtype=jnp.int32), own_ids])
    used_scaled = jnp.concatenate([center_scaled[: 2 * PANEL], own_scaled])
    used_norms = jnp.concatenate([center_norms[: 2 * PANEL], own_norms])
    used_kernel = kernel_block(
        used_scaled, used_norms, center_scaled[: 2 * PANEL], center_norms[: 2 * PANEL], signal
    ) + ridge_where(used_ids, jnp.arange(2 * PANEL, dtype=jnp.int32), jitter)
    first_inverse, second_inverse, first_mid, own_panels = factor_centers(used_kernel)

    select = jnp.where(
        lax.broadcasted_iota(jnp.int32, (BLK, PANEL), 1)
        == column * BLK + lax.broadcasted_iota(jnp.int32, (BLK, PANEL), 0),
        1.0,
        0.0,
    ).astype(jnp.bfloat16)
    consts = jnp.stack([signal, jitter])
    finished = panel_stage(
        consts,
        gathered,
        point_ids,
        feature_scales.reshape(1, FEAT),
        pack_left(center_scaled[: 2 * PANEL]),
        center_norms[: 2 * PANEL].reshape(-1, 1),
        pack_left(own_scaled),
        own_norms.reshape(-1, 1),
        own_ids.reshape(-1, 1),
        first_inverse,
        second_inverse,
        first_mid,
        own_panels,
        select,
    )
    return finished.reshape(col_blocks, 1, BLK, 1, grid_rows)


def solution(mesh):
    placed = (P(("row", "col"), None), P(), P(), P())
    return jax.shard_map(
        on_device,
        mesh=mesh,
        in_specs=placed,
        out_specs=P(None, "col", None, "row", None),
        check_vma=False,
    )
```
